32 devices in a mesh: comp: 4 (over x, core), blk: 8 (over z, y).
Axes of the slice: x: 2, y: 2, z: 4, core: 2. Of those that a mesh axis runs over, the one named last changes fastest.
Arguments:
- start_modes: float32 [4, 32768, 256], P('comp', 'blk')
- stiff_diag: float32 [4, 256, 128, 128], P('comp', 'blk')
- stiff_off: float32 [4, 256, 128, 128], P('comp', 'blk'), may hold values from -0.625 to 0.625
- mass_blocks: float32 [4, 256, 128, 128], P('comp', 'blk')
- coupling: float32 [4, 256, 128, 128], P('comp', 'blk'), may hold values from -6 to 6
- interface_block: int32 [4, 256], P('comp', 'blk'), may hold values from 0 to 8
- global_iface: int32 [4, 8], P('comp'), may hold values from 0 to 15
Outputs:
- modes: float32 [4, 32768, 256], P('comp', 'blk')
- reduced_stiffness: float32 [4, 256, 256], P('comp')
- assembled: float32 [16, 128, 128], P('comp')
The draws below stay inside these ranges and needn't reach their ends.
All inputs are finite; a program needn't handle non-finite values.
Results may differ from the reference program's by a relative error of at most 0.0003.
Values sent between devices are 32-bit elements; how exact they have to be, the bound alone decides.
No kernel may reach another device: no remote copies, remote signals or barrier semaphores. Data moves between devices by JAX's collectives and lax.ppermute only.
A program may use at most 128 MiB of HBM per device.

```python
import math
import jax
import jax.numpy as jnp
import numpy as np
from jax import lax

BS = 128
MODES = 256
ITERS = 2
COMPS = 4
NBLK = 256
NIF = 8
GIF = 16


def region_soft(key):
    return jax.random.randint(jax.random.fold_in(key, 5), (COMPS, NBLK), 0, 2)


def draw_start_modes(key, part):
    soft_rows = region_soft(key).reshape(COMPS, NBLK, 1, 1)
    character = jax.random.randint(jax.random.fold_in(key, 31), (COMPS, 1, 1, MODES + 1), 0, 2)
    weight = jnp.where(soft_rows == character, 1.0, 0.25).astype(jnp.float32)
    noise = jax.random.normal(jax.random.fold_in(key, 32), (COMPS, NBLK, BS, MODES + 1), jnp.float32)
    columns = noise * weight
    mixing = jax.random.uniform(jax.random.fold_in(key, 33), (COMPS, 1, 1, MODES), jnp.float32, -0.8, 0.8)
    mixed = columns[:, :, :, :MODES] + mixing * columns[:, :, :, 1:]
    return jnp.clip(mixed, -6.0, 6.0).reshape(COMPS, NBLK * BS, MODES)


def draw_stiff_diag(key, part):
    random_part = jax.random.normal(jax.random.fold_in(key, 11), (COMPS, NBLK, BS, BS), jnp.float32)
    symmetric = (random_part + jnp.swapaxes(random_part, 2, 3)) * (0.6 / (2.0 * BS) ** 0.5)
    soft_rows = region_soft(key).reshape(COMPS, NBLK, 1, 1)
    soft_level = jnp.full((COMPS, NBLK, 1, 1), 2.8, jnp.float32)
    stiff_level = jnp.full((COMPS, NBLK, 1, 1), 11.0, jnp.float32)
    diag_level = jnp.where(soft_rows == 1, soft_level, stiff_level)
    return symmetric + diag_level * jnp.eye(BS, dtype=jnp.float32)


def draw_mass_blocks(key, part):
    random_part = jax.random.normal(jax.random.fold_in(key, 21), (COMPS, NBLK, BS, BS), jnp.float32)
    symmetric = (random_part + jnp.swapaxes(random_part, 2, 3)) * (0.3 / (2.0 * BS) ** 0.5)
    diag_level = jnp.ones((COMPS, NBLK, 1, 1), jnp.float32)
    return symmetric + diag_level * jnp.eye(BS, dtype=jnp.float32)


def place_ends(values, rng, smallest, largest):
    longest = values.shape.index(max(values.shape))
    spots = []
    for shift in (0, 1):
        where = [jax.random.randint(jax.random.fold_in(rng, axis), (), 0, length) for axis, length in enumerate(values.shape)]
        where[longest] = (where[longest] + shift) % values.shape[longest]
        spots.append(tuple(where))
    return values.at[spots[0]].set(smallest).at[spots[1]].set(largest)


def levels(stream_key, extent, shards, smallest, top_value):
    def one(axis_at, blocks):
        heights = jax.random.uniform(jax.random.fold_in(jax.random.fold_in(stream_key, 6), axis_at), (blocks,), jnp.float32, smallest / len(shards), top_value / len(shards))
        return jnp.repeat(jnp.exp(heights), extent[axis_at] // blocks).reshape((-1,) + (1,) * (len(extent) - axis_at - 1))

    level = one(*shards[0])
    for cut in shards[1:]:
        level = level * one(*cut)
    return level


def rank_table(amount, lean):
    loads = [(1 << 20) // math.isqrt(standing ** lean) + 1 for standing in range(1, amount + 1)]
    width = 1 + sum(loads) // (1 << 30)
    return np.cumsum(np.array([max(1, weight // width) for weight in loads]))


def ranked_ids(key, extent, number_of, slope):
    listing = rank_table(number_of, slope)
    pick = jax.random.randint(jax.random.fold_in(key, 1), extent, 0, int(listing[number_of - 1]))
    standing = jnp.searchsorted(jnp.asarray(listing, jnp.int32), pick, side="right")
    return jax.random.permutation(jax.random.fold_in(key, 2), number_of)[standing].astype(jnp.int32)


def scatter_about(rng, extent, spread, most, cuts=(), kind=jnp.bfloat16):
    factor_of = levels(rng, extent, cuts, -0.22, 0.18) if cuts else 1.0
    drawn = jax.random.normal(rng, extent, jnp.float32) * spread * factor_of
    return jnp.minimum(jnp.maximum(drawn, -most), most).astype(kind)


def setup_inputs(seed: int = 0) -> dict:
    key_list = jax.random.split(jax.random.key(seed), 8)
    start_modes = draw_start_modes(jax.random.fold_in(key_list[7], 71), 0)
    stiff_diag = draw_stiff_diag(jax.random.fold_in(key_list[7], 71), 0)
    stiff_off = scatter_about(key_list[2], (COMPS, NBLK, BS, BS), (0.45 / BS ** 0.5), 0.625, ((0, 4), (1, 8)), jnp.float32)
    mass_blocks = draw_mass_blocks(jax.random.fold_in(key_list[7], 71), 0)
    coupling = scatter_about(key_list[4], (COMPS, NBLK, BS, BS), 1.0, 6.0, ((0, 4), (1, 8)), jnp.float32)
    interface_block = place_ends(jax.random.randint(key_list[5], (COMPS, NBLK), 0, NIF + 1), jax.random.fold_in(key_list[5], 1), 0, NIF).astype(jnp.int32)
    global_iface = place_ends(ranked_ids(key_list[6], (COMPS, NIF), GIF, 2), jax.random.fold_in(key_list[6], 3), 0, GIF - 1).astype(jnp.int32)
    return dict(start_modes=start_modes, stiff_diag=stiff_diag, stiff_off=stiff_off, mass_blocks=mass_blocks, coupling=coupling, interface_block=interface_block, global_iface=global_iface)


highest = lax.Precision.HIGHEST
step_size = 0.15

def block_product(blocks, vectors):
    return jnp.einsum('bij,bjm->bim', blocks, vectors, precision=highest)

def stiff_apply(stiff_self, stiff_link, vectors):
    zero_block = jnp.zeros_like(vectors[:1])
    preceding = jnp.concatenate([zero_block, vectors[:-1]], 0)
    following = jnp.concatenate([vectors[1:], zero_block], 0)
    link_after = jnp.concatenate([stiff_link[1:], jnp.zeros_like(stiff_link[:1])], 0)
    result = block_product(stiff_self, vectors) + block_product(stiff_link, preceding)
    return result + jnp.einsum('bji,bjm->bim', link_after, following, precision=highest)

def lower_inverse(matrix):
    factor = jnp.linalg.cholesky(matrix)
    unit_matrix = jnp.eye(matrix.shape[0], dtype=matrix.dtype)
    return lax.linalg.triangular_solve(factor, unit_matrix, left_side=True, lower=True)

def component(start_flat, stiff_self, stiff_link, mass_self, coupling_blocks, interface_ids):
    dof_count, mode_count = start_flat.shape
    blocks_count = stiff_self.shape[0]
    block_size = stiff_self.shape[1]
    basis = start_flat
    stiff_basis = stiff_apply(stiff_self, stiff_link, basis.reshape(blocks_count, block_size, mode_count)).reshape(dof_count, mode_count)
    reduced = jnp.zeros((mode_count, mode_count), start_flat.dtype)
    for sweep in range(ITERS):
        filtered = basis - step_size * stiff_basis
        mass_part = block_product(mass_self, filtered.reshape(blocks_count, block_size, mode_count)).reshape(dof_count, mode_count)
        mass_gram = jnp.dot(filtered.T, mass_part, precision=highest) / dof_count
        factor_inv = lower_inverse(mass_gram)
        basis = jnp.dot(filtered, factor_inv.T, precision=highest)
        stiff_basis = stiff_apply(stiff_self, stiff_link, basis.reshape(blocks_count, block_size, mode_count)).reshape(dof_count, mode_count)
        reduced = jnp.dot(basis.T, stiff_basis, precision=highest) / dof_count
    block_terms = jnp.einsum('bkm,bkl->bml', basis.reshape(blocks_count, block_size, mode_count), coupling_blocks, precision=highest)
    onehot = (interface_ids[:, None] == jnp.arange(NIF, dtype=jnp.int32)[None, :]).astype(start_flat.dtype)
    coupling_proj = jnp.einsum('bj,bml->mjl', onehot, block_terms, precision=highest) / dof_count ** 0.5
    reduced_inv = lower_inverse(reduced)
    scaled = jnp.einsum('nm,mjl->njl', reduced_inv, coupling_proj, precision=highest)
    condensed = jnp.einsum('njk,njl->jkl', scaled, scaled, precision=highest)
    return (basis, reduced, condensed)

def reference(start_modes, stiff_diag, stiff_off, mass_blocks, coupling, interface_block, global_iface):
    modes, reduced, condensed = lax.map(lambda packed: component(*packed), (start_modes, stiff_diag, stiff_off, mass_blocks, coupling, interface_block))
    placed = (global_iface[:, :, None] == jnp.arange(GIF, dtype=jnp.int32)[None, None, :]).astype(start_modes.dtype)
    assembled = jnp.einsum('cjg,cjkl->gkl', placed, condensed, precision=highest)
    return (modes, reduced, assembled)
```

```python
import jax
import jax.numpy as jnp
from jax import lax
from jax.sharding import PartitionSpec as P

ITERS = 2
GIFC = 4


highest = lax.Precision.HIGHEST
step_size = 0.15


def passed_along(value, axis, steps):
    count = lax.axis_size(axis)
    initial, last = (max(0, -steps), min(count, count - steps))
    return lax.ppermute(value, axis, [(source, source + steps) for source in range(initial, last)])


def extended_2(block, sides, width):
    for axis, dim in sides:
        count = lax.axis_size(axis)
        forward = [(i, i + 1) for i in range(count - 1)]
        backward = [(target, source) for source, target in forward]
        low = lax.ppermute(
            lax.slice_in_dim(block, block.shape[dim] - width, None, axis=dim), axis, forward
        )
        high = lax.ppermute(lax.slice_in_dim(block, 0, width, axis=dim), axis, backward)
        block = jnp.concatenate([low, block, high], axis=dim)
    return block


def block_product(blocks, vectors):
    return jnp.einsum("bij,bjm->bim", blocks, vectors, precision=highest)


def local(start_modes, stiff_diag, stiff_off, mass_blocks, coupling, interface_block, global_iface):
    start_flat = start_modes[0]
    stiff_self = stiff_diag[0]
    stiff_link = stiff_off[0]
    mass_self = mass_blocks[0]
    coupling_blocks = coupling[0]
    interface_ids = interface_block[0]
    global_ids = global_iface[0]
    row_count, mode_count = start_flat.shape
    blocks_dev = stiff_self.shape[0]
    block_size = stiff_self.shape[1]
    dof_count = row_count * lax.axis_size("blk")
    link_next = passed_along(stiff_link[:1], "blk", -1)
    link_after = jnp.concatenate([stiff_link[1:], link_next], 0)

    def stiff_apply(vectors):
        padded = extended_2(vectors, (("blk", 0),), block_size)
        extended = padded.reshape(blocks_dev + 2, block_size, mode_count)
        result = block_product(stiff_self, extended[1 : blocks_dev + 1]) + block_product(
            stiff_link, extended[:blocks_dev]
        )
        result = result + jnp.einsum("bji,bjm->bim", link_after, extended[2:], precision=highest)
        return result.reshape(row_count, mode_count)

    def mass_apply(vectors):
        return block_product(
            mass_self, vectors.reshape(blocks_dev, block_size, mode_count)
        ).reshape(row_count, mode_count)

    def gram_matrix(left, right):
        return jnp.dot(left.T, right, precision=highest)

    first = start_flat - step_size * stiff_apply(start_flat)
    second = first - step_size * stiff_apply(first)
    stiff_second = stiff_apply(second)
    iface_count = global_ids.shape[0]
    block_terms = jnp.einsum(
        "bkm,bkl->bml",
        second.reshape(blocks_dev, block_size, mode_count),
        coupling_blocks,
        precision=highest,
    )
    onehot = (interface_ids[:, None] == jnp.arange(iface_count, dtype=jnp.int32)[None, :]).astype(
        jnp.float32
    )
    coupling_term = jnp.einsum("bj,bml->mjl", onehot, block_terms, precision=highest)
    first_gram, mass_gram, stiff_gram, coupling_sum = lax.psum(
        (
            gram_matrix(first, mass_apply(first)),
            gram_matrix(second, mass_apply(second)),
            gram_matrix(second, stiff_second),
            coupling_term,
        ),
        "blk",
    )
    factors = jnp.linalg.cholesky(jnp.stack([first_gram, mass_gram, stiff_gram]) / dof_count)
    guard = 0.0 * jnp.sum(factors[0])
    unit_matrix = jnp.broadcast_to(jnp.eye(mode_count, dtype=jnp.float32), (2, mode_count, mode_count))
    inverses = lax.linalg.triangular_solve(factors[1:], unit_matrix, left_side=True, lower=True)
    factor_inv = inverses[0] + guard
    chain_inv = inverses[1] + guard
    basis = jnp.dot(second, factor_inv.T, precision=highest)
    reduced = (
        jnp.dot(
            jnp.dot(factor_inv, stiff_gram, precision=highest), factor_inv.T, precision=highest
        )
        / dof_count
    )
    scaled = jnp.einsum("nm,mjl->njl", chain_inv, coupling_sum, precision=highest) / dof_count**0.5
    condensed = jnp.einsum("njk,njl->jkl", scaled, scaled, precision=highest)
    global_count = GIFC * lax.axis_size("comp")
    placed = (global_ids[:, None] == jnp.arange(global_count, dtype=jnp.int32)[None, :]).astype(
        jnp.float32
    )
    dense_sum = jnp.einsum("jg,jkl->gkl", placed, condensed, precision=highest)
    owned = lax.psum_scatter(dense_sum, "comp", scatter_dimension=0, tiled=True)
    return (basis[None], reduced[None], owned)


def solution(mesh):
    in_specs = (
        P("comp", "blk", None),
        P("comp", "blk", None, None),
        P("comp", "blk", None, None),
        P("comp", "blk", None, None),
        P("comp", "blk", None, None),
        P("comp", "blk"),
        P("comp", None),
    )
    out_specs = (P("comp", "blk", None), P("comp", None, None), P("comp", None, None))
    return jax.shard_map(local, mesh=mesh, in_specs=in_specs, out_specs=out_specs, check_vma=False)
```

```python
import jax
import jax.numpy as jnp
from jax import lax
from jax.experimental import pallas as pl
from jax.experimental.pallas import tpu as pltpu
from jax.sharding import PartitionSpec as P

ITERS = 2
GIFC = 4


highest = lax.Precision.HIGHEST
step_size = 0.15


def passed_along(value, axis, steps):
    count = lax.axis_size(axis)
    initial, last = (max(0, -steps), min(count, count - steps))
    return lax.ppermute(value, axis, [(source, source + steps) for source in range(initial, last)])


def extended_2(block, sides, width):
    for axis, dim in sides:
        count = lax.axis_size(axis)
        forward = [(i, i + 1) for i in range(count - 1)]
        backward = [(target, source) for source, target in forward]
        low = lax.ppermute(
            lax.slice_in_dim(block, block.shape[dim] - width, None, axis=dim), axis, forward
        )
        high = lax.ppermute(lax.slice_in_dim(block, 0, width, axis=dim), axis, backward)
        block = jnp.concatenate([low, block, high], axis=dim)
    return block


def block_product(blocks, vectors):
    return jnp.einsum("bij,bjm->bim", blocks, vectors, precision=highest)


def _inverse_factor_kernel(a_in, w_out, a_ref, x_ref):
    batch, size, _ = a_in.shape
    a_ref[...] = a_in[...]
    rows = lax.broadcasted_iota(jnp.int32, (size, size), 0)
    cols = lax.broadcasted_iota(jnp.int32, (size, size), 1)
    eye = jnp.where(rows == cols, 1.0, 0.0).astype(jnp.float32)
    x_ref[...] = jnp.broadcast_to(eye, (batch, size, size))
    phase = 64
    lanes = 128
    sublanes = 8

    def row_of(ref, k, col0, col1):
        tile0 = pl.multiple_of((k // sublanes) * sublanes, sublanes)
        tile = ref[:, pl.ds(tile0, sublanes), col0:col1]
        sub = lax.broadcasted_iota(jnp.int32, tile.shape, 1) + tile0
        return jnp.sum(jnp.where(sub == k, tile, 0.0), axis=1, keepdims=True)

    for start in range(0, size, phase):
        a_col0 = (start // lanes) * lanes
        x_col1 = min(size, -(-(start + phase) // lanes) * lanes)

        def step(k, carry, start=start, a_col0=a_col0, x_col1=x_col1):
            row_a = row_of(a_ref, k, a_col0, size)
            row_x = row_of(x_ref, k, 0, x_col1)
            block0 = pl.multiple_of((k // lanes) * lanes, lanes)
            col_block = a_ref[:, start:, pl.ds(block0, lanes)]
            lane = lax.broadcasted_iota(jnp.int32, col_block.shape, 2) + block0
            col = jnp.sum(jnp.where(lane == k, col_block, 0.0), axis=2, keepdims=True)
            lane_a = lax.broadcasted_iota(jnp.int32, row_a.shape, 2) + a_col0
            pivot = jnp.sum(jnp.where(lane_a == k, row_a, 0.0), axis=2, keepdims=True)
            row_ids = lax.broadcasted_iota(jnp.int32, col.shape, 1) + start
            mult = jnp.where(row_ids > k, col / pivot, 0.0)
            a_ref[:, start:, a_col0:] = a_ref[:, start:, a_col0:] - mult * row_a
            x_ref[:, start:, :x_col1] = x_ref[:, start:, :x_col1] - mult * row_x
            return carry

        lax.fori_loop(start, start + phase, step, 0)
    pivots = jnp.sum(jnp.where(rows == cols, a_ref[...], 0.0), axis=2, keepdims=True)
    w_out[...] = x_ref[...] * lax.rsqrt(pivots)


def inverse_factors(matrices):
    batch, size, _ = matrices.shape
    return pl.pallas_call(
        _inverse_factor_kernel,
        out_shape=jax.ShapeDtypeStruct(matrices.shape, jnp.float32),
        in_specs=[pl.BlockSpec(memory_space=pltpu.VMEM)],
        out_specs=pl.BlockSpec(memory_space=pltpu.VMEM),
        scratch_shapes=[
            pltpu.VMEM(matrices.shape, jnp.float32),
            pltpu.VMEM(matrices.shape, jnp.float32),
        ],
    )(matrices)


def local(start_modes, stiff_diag, stiff_off, mass_blocks, coupling, interface_block, global_iface):
    start_flat = start_modes[0]
    stiff_self = stiff_diag[0]
    stiff_link = stiff_off[0]
    mass_self = mass_blocks[0]
    coupling_blocks = coupling[0]
    interface_ids = interface_block[0]
    global_ids = global_iface[0]
    row_count, mode_count = start_flat.shape
    blocks_dev = stiff_self.shape[0]
    block_size = stiff_self.shape[1]
    dof_count = row_count * lax.axis_size("blk")
    link_next = passed_along(stiff_link[:1], "blk", -1)
    link_after = jnp.concatenate([stiff_link[1:], link_next], 0)

    def stiff_apply(vectors):
        padded = extended_2(vectors, (("blk", 0),), block_size)
        extended = padded.reshape(blocks_dev + 2, block_size, mode_count)
        result = block_product(stiff_self, extended[1 : blocks_dev + 1]) + block_product(
            stiff_link, extended[:blocks_dev]
        )
        result = result + jnp.einsum("bji,bjm->bim", link_after, extended[2:], precision=highest)
        return result.reshape(row_count, mode_count)

    def mass_apply(vectors):
        return block_product(
            mass_self, vectors.reshape(blocks_dev, block_size, mode_count)
        ).reshape(row_count, mode_count)

    def gram_matrix(left, right):
        return jnp.dot(left.T, right, precision=highest)

    first = start_flat - step_size * stiff_apply(start_flat)
    second = first - step_size * stiff_apply(first)
    stiff_second = stiff_apply(second)
    iface_count = global_ids.shape[0]
    block_terms = jnp.einsum(
        "bkm,bkl->bml",
        second.reshape(blocks_dev, block_size, mode_count),
        coupling_blocks,
        precision=highest,
    )
    onehot = (interface_ids[:, None] == jnp.arange(iface_count, dtype=jnp.int32)[None, :]).astype(
        jnp.float32
    )
    coupling_term = jnp.einsum("bj,bml->mjl", onehot, block_terms, precision=highest)
    first_gram, mass_gram, stiff_gram, coupling_sum = lax.psum(
        (
            gram_matrix(first, mass_apply(first)),
            gram_matrix(second, mass_apply(second)),
            gram_matrix(second, stiff_second),
            coupling_term,
        ),
        "blk",
    )
    grams = jnp.stack([first_gram, mass_gram, stiff_gram]) / dof_count
    inverses = inverse_factors(0.5 * (grams + jnp.swapaxes(grams, 1, 2)))
    guard = 0.0 * jnp.sum(inverses[0])
    factor_inv = inverses[1] + guard
    chain_inv = inverses[2] + guard
    basis = jnp.dot(second, factor_inv.T, precision=highest)
    reduced = (
        jnp.dot(
            jnp.dot(factor_inv, stiff_gram, precision=highest), factor_inv.T, precision=highest
        )
        / dof_count
    )
    scaled = jnp.einsum("nm,mjl->njl", chain_inv, coupling_sum, precision=highest) / dof_count**0.5
    condensed = jnp.einsum("njk,njl->jkl", scaled, scaled, precision=highest)
    global_count = GIFC * lax.axis_size("comp")
    placed = (global_ids[:, None] == jnp.arange(global_count, dtype=jnp.int32)[None, :]).astype(
        jnp.float32
    )
    dense_sum = jnp.einsum("jg,jkl->gkl", placed, condensed, precision=highest)
    owned = lax.psum_scatter(dense_sum, "comp", scatter_dimension=0, tiled=True)
    return (basis[None], reduced[None], owned)


def solution(mesh):
    in_specs = (
        P("comp", "blk", None),
        P("comp", "blk", None, None),
        P("comp", "blk", None, None),
        P("comp", "blk", None, None),
        P("comp", "blk", None, None),
        P("comp", "blk"),
        P("comp", None),
    )
    out_specs = (P("comp", "blk", None), P("comp", None, None), P("comp", None, None))
    return jax.shard_map(local, mesh=mesh, in_specs=in_specs, out_specs=out_specs, check_vma=False)
```

```python
import jax
import jax.numpy as jnp
from jax import lax
from jax.experimental import pallas as pl
from jax.experimental.pallas import tpu as pltpu
from jax.sharding import PartitionSpec as P

ITERS = 2
GIFC = 4


highest = lax.Precision.HIGHEST
fast = lax.Precision.HIGH
step_size = 0.15


def passed_along(value, axis, steps):
    count = lax.axis_size(axis)
    initial, last = (max(0, -steps), min(count, count - steps))
    return lax.ppermute(value, axis, [(source, source + steps) for source in range(initial, last)])


def extended_2(block, sides, width):
    for axis, dim in sides:
        count = lax.axis_size(axis)
        forward = [(i, i + 1) for i in range(count - 1)]
        backward = [(target, source) for source, target in forward]
        low = lax.ppermute(
            lax.slice_in_dim(block, block.shape[dim] - width, None, axis=dim), axis, forward
        )
        high = lax.ppermute(lax.slice_in_dim(block, 0, width, axis=dim), axis, backward)
        block = jnp.concatenate([low, block, high], axis=dim)
    return block


def block_product(blocks, vectors):
    return jnp.einsum("bij,bjm->bim", blocks, vectors, precision=fast)


def _inverse_factor_kernel(a_in, w_out, a_ref, x_ref):
    batch, size, _ = a_in.shape
    a_ref[...] = a_in[...]
    rows = lax.broadcasted_iota(jnp.int32, (size, size), 0)
    cols = lax.broadcasted_iota(jnp.int32, (size, size), 1)
    eye = jnp.where(rows == cols, 1.0, 0.0).astype(jnp.float32)
    x_ref[...] = jnp.broadcast_to(eye, (batch, size, size))
    phase = 64
    lanes = 128
    sublanes = 8

    def row_of(ref, k, col0, col1):
        tile0 = pl.multiple_of((k // sublanes) * sublanes, sublanes)
        tile = ref[:, pl.ds(tile0, sublanes), col0:col1]
        sub = lax.broadcasted_iota(jnp.int32, tile.shape, 1) + tile0
        return jnp.sum(jnp.where(sub == k, tile, 0.0), axis=1, keepdims=True)

    for start in range(0, size, phase):
        a_col0 = (start // lanes) * lanes
        x_col1 = min(size, -(-(start + phase) // lanes) * lanes)

        def step(k, carry, start=start, a_col0=a_col0, x_col1=x_col1):
            row_a = row_of(a_ref, k, a_col0, size)
            row_x = row_of(x_ref, k, 0, x_col1)
            block0 = pl.multiple_of((k // lanes) * lanes, lanes)
            col_block = a_ref[:, start:, pl.ds(block0, lanes)]
            lane = lax.broadcasted_iota(jnp.int32, col_block.shape, 2) + block0
            col = jnp.sum(jnp.where(lane == k, col_block, 0.0), axis=2, keepdims=True)
            lane_a = lax.broadcasted_iota(jnp.int32, row_a.shape, 2) + a_col0
            pivot = jnp.sum(jnp.where(lane_a == k, row_a, 0.0), axis=2, keepdims=True)
            row_ids = lax.broadcasted_iota(jnp.int32, col.shape, 1) + start
            mult = jnp.where(row_ids > k, col / pivot, 0.0)
            a_ref[:, start:, a_col0:] = a_ref[:, start:, a_col0:] - mult * row_a
            x_ref[:, start:, :x_col1] = x_ref[:, start:, :x_col1] - mult * row_x
            return carry

        lax.fori_loop(start, start + phase, step, 0)
    pivots = jnp.sum(jnp.where(rows == cols, a_ref[...], 0.0), axis=2, keepdims=True)
    w_out[...] = x_ref[...] * lax.rsqrt(pivots)


def inverse_factors(matrices):
    batch, size, _ = matrices.shape
    return pl.pallas_call(
        _inverse_factor_kernel,
        out_shape=jax.ShapeDtypeStruct(matrices.shape, jnp.float32),
        in_specs=[pl.BlockSpec(memory_space=pltpu.VMEM)],
        out_specs=pl.BlockSpec(memory_space=pltpu.VMEM),
        scratch_shapes=[
            pltpu.VMEM(matrices.shape, jnp.float32),
            pltpu.VMEM(matrices.shape, jnp.float32),
        ],
    )(matrices)


def local(start_modes, stiff_diag, stiff_off, mass_blocks, coupling, interface_block, global_iface):
    start_flat = start_modes[0]
    stiff_self = stiff_diag[0]
    stiff_link = stiff_off[0]
    mass_self = mass_blocks[0]
    coupling_blocks = coupling[0]
    interface_ids = interface_block[0]
    global_ids = global_iface[0]
    row_count, mode_count = start_flat.shape
    blocks_dev = stiff_self.shape[0]
    block_size = stiff_self.shape[1]
    dof_count = row_count * lax.axis_size("blk")
    link_next = passed_along(stiff_link[:1], "blk", -1)
    link_after = jnp.concatenate([stiff_link[1:], link_next], 0)

    def stiff_apply(vectors):
        padded = extended_2(vectors, (("blk", 0),), block_size)
        extended = padded.reshape(blocks_dev + 2, block_size, mode_count)
        result = block_product(stiff_self, extended[1 : blocks_dev + 1]) + block_product(
            stiff_link, extended[:blocks_dev]
        )
        result = result + jnp.einsum("bji,bjm->bim", link_after, extended[2:], precision=fast)
        return result.reshape(row_count, mode_count)

    def mass_apply(vectors):
        return block_product(
            mass_self, vectors.reshape(blocks_dev, block_size, mode_count)
        ).reshape(row_count, mode_count)

    def gram_matrix(left, right):
        return jnp.dot(left.T, right, precision=fast)

    first = start_flat - step_size * stiff_apply(start_flat)
    second = first - step_size * stiff_apply(first)
    stiff_second = stiff_apply(second)
    iface_count = global_ids.shape[0]
    block_terms = jnp.einsum(
        "bkm,bkl->bml",
        second.reshape(blocks_dev, block_size, mode_count),
        coupling_blocks,
        precision=fast,
    )
    onehot = (interface_ids[:, None] == jnp.arange(iface_count, dtype=jnp.int32)[None, :]).astype(
        jnp.float32
    )
    coupling_term = jnp.einsum("bj,bml->mjl", onehot, block_terms, precision=highest)
    first_gram, mass_gram, stiff_gram, coupling_sum = lax.psum(
        (
            gram_matrix(first, mass_apply(first)),
            gram_matrix(second, mass_apply(second)),
            gram_matrix(second, stiff_second),
            coupling_term,
        ),
        "blk",
    )
    grams = jnp.stack([first_gram, mass_gram, stiff_gram]) / dof_count
    inverses = inverse_factors(0.5 * (grams + jnp.swapaxes(grams, 1, 2)))
    guard = 0.0 * jnp.sum(inverses[0])
    factor_inv = inverses[1] + guard
    chain_inv = inverses[2] + guard
    basis = jnp.dot(second, factor_inv.T, precision=fast)
    reduced = (
        jnp.dot(
            jnp.dot(factor_inv, stiff_gram, precision=highest), factor_inv.T, precision=highest
        )
        / dof_count
    )
    scaled = jnp.einsum("nm,mjl->njl", chain_inv, coupling_sum, precision=highest) / dof_count**0.5
    condensed = jnp.einsum("njk,njl->jkl", scaled, scaled, precision=highest)
    global_count = GIFC * lax.axis_size("comp")
    placed = (global_ids[:, None] == jnp.arange(global_count, dtype=jnp.int32)[None, :]).astype(
        jnp.float32
    )
    dense_sum = jnp.einsum("jg,jkl->gkl", placed, condensed, precision=highest)
    owned = lax.psum_scatter(dense_sum, "comp", scatter_dimension=0, tiled=True)
    return (basis[None], reduced[None], owned)


def solution(mesh):
    in_specs = (
        P("comp", "blk", None),
        P("comp", "blk", None, None),
        P("comp", "blk", None, None),
        P("comp", "blk", None, None),
        P("comp", "blk", None, None),
        P("comp", "blk"),
        P("comp", None),
    )
    out_specs = (P("comp", "blk", None), P("comp", None, None), P("comp", None, None))
    return jax.shard_map(local, mesh=mesh, in_specs=in_specs, out_specs=out_specs, check_vma=False)
```

```python
import jax
import jax.numpy as jnp
from jax import lax
from jax.experimental import pallas as pl
from jax.experimental.pallas import tpu as pltpu
from jax.sharding import PartitionSpec as P

ITERS = 2
GIFC = 4


highest = lax.Precision.HIGHEST
fast = lax.Precision.HIGH
step_size = 0.15


def passed_along(value, axis, steps):
    count = lax.axis_size(axis)
    initial, last = (max(0, -steps), min(count, count - steps))
    return lax.ppermute(value, axis, [(source, source + steps) for source in range(initial, last)])


def extended_2(block, sides, width):
    for axis, dim in sides:
        count = lax.axis_size(axis)
        forward = [(i, i + 1) for i in range(count - 1)]
        backward = [(target, source) for source, target in forward]
        low = lax.ppermute(
            lax.slice_in_dim(block, block.shape[dim] - width, None, axis=dim), axis, forward
        )
        high = lax.ppermute(lax.slice_in_dim(block, 0, width, axis=dim), axis, backward)
        block = jnp.concatenate([low, block, high], axis=dim)
    return block


def permute_sum(value, axis):
    count = lax.axis_size(axis)
    rounds = count.bit_length() - 1
    assert count == 1 << rounds
    me = lax.axis_index(axis)
    shape = value.shape
    flat = value.reshape(-1)
    piece = flat.shape[0] >> rounds
    assert piece << rounds == flat.shape[0]
    for level in range(rounds):
        half = flat.shape[0] // 2
        upper = (me >> level) & 1
        pairs = [(i, i ^ (1 << level)) for i in range(count)]
        sent = lax.dynamic_slice_in_dim(flat, (1 - upper) * half, half)
        kept = lax.dynamic_slice_in_dim(flat, upper * half, half)
        flat = kept + lax.ppermute(sent, axis, pairs)
    for level in reversed(range(rounds)):
        upper = (me >> level) & 1
        pairs = [(i, i ^ (1 << level)) for i in range(count)]
        other = lax.ppermute(flat, axis, pairs)
        flat = jnp.where(
            upper == 1, jnp.concatenate([other, flat]), jnp.concatenate([flat, other])
        )
    return flat.reshape(shape)


def block_product(blocks, vectors):
    return jnp.einsum("bij,bjm->bim", blocks, vectors, precision=fast)


def _inverse_factor_kernel(a_in, w_out, a_ref, x_ref):
    batch, size, _ = a_in.shape
    a_ref[...] = a_in[...]
    rows = lax.broadcasted_iota(jnp.int32, (size, size), 0)
    cols = lax.broadcasted_iota(jnp.int32, (size, size), 1)
    eye = jnp.where(rows == cols, 1.0, 0.0).astype(jnp.float32)
    x_ref[...] = jnp.broadcast_to(eye, (batch, size, size))
    phase = 64
    lanes = 128
    sublanes = 8

    def row_of(ref, k, col0, col1):
        tile0 = pl.multiple_of((k // sublanes) * sublanes, sublanes)
        tile = ref[:, pl.ds(tile0, sublanes), col0:col1]
        sub = lax.broadcasted_iota(jnp.int32, tile.shape, 1) + tile0
        return jnp.sum(jnp.where(sub == k, tile, 0.0), axis=1, keepdims=True)

    for start in range(0, size, phase):
        a_col0 = (start // lanes) * lanes
        x_col1 = min(size, -(-(start + phase) // lanes) * lanes)

        def step(k, carry, start=start, a_col0=a_col0, x_col1=x_col1):
            row_a = row_of(a_ref, k, a_col0, size)
            row_x = row_of(x_ref, k, 0, x_col1)
            block0 = pl.multiple_of((k // lanes) * lanes, lanes)
            col_block = a_ref[:, start:, pl.ds(block0, lanes)]
            lane = lax.broadcasted_iota(jnp.int32, col_block.shape, 2) + block0
            col = jnp.sum(jnp.where(lane == k, col_block, 0.0), axis=2, keepdims=True)
            lane_a = lax.broadcasted_iota(jnp.int32, row_a.shape, 2) + a_col0
            pivot = jnp.sum(jnp.where(lane_a == k, row_a, 0.0), axis=2, keepdims=True)
            row_ids = lax.broadcasted_iota(jnp.int32, col.shape, 1) + start
            mult = jnp.where(row_ids > k, col / pivot, 0.0)
            a_ref[:, start:, a_col0:] = a_ref[:, start:, a_col0:] - mult * row_a
            x_ref[:, start:, :x_col1] = x_ref[:, start:, :x_col1] - mult * row_x
            return carry

        lax.fori_loop(start, start + phase, step, 0)
    pivots = jnp.sum(jnp.where(rows == cols, a_ref[...], 0.0), axis=2, keepdims=True)
    w_out[...] = x_ref[...] * lax.rsqrt(pivots)


def inverse_factors(matrices):
    batch, size, _ = matrices.shape
    return pl.pallas_call(
        _inverse_factor_kernel,
        out_shape=jax.ShapeDtypeStruct(matrices.shape, jnp.float32),
        in_specs=[pl.BlockSpec(memory_space=pltpu.VMEM)],
        out_specs=pl.BlockSpec(memory_space=pltpu.VMEM),
        scratch_shapes=[
            pltpu.VMEM(matrices.shape, jnp.float32),
            pltpu.VMEM(matrices.shape, jnp.float32),
        ],
    )(matrices)


def local(start_modes, stiff_diag, stiff_off, mass_blocks, coupling, interface_block, global_iface):
    start_flat = start_modes[0]
    stiff_self = stiff_diag[0]
    stiff_link = stiff_off[0]
    mass_self = mass_blocks[0]
    coupling_blocks = coupling[0]
    interface_ids = interface_block[0]
    global_ids = global_iface[0]
    row_count, mode_count = start_flat.shape
    blocks_dev = stiff_self.shape[0]
    block_size = stiff_self.shape[1]
    dof_count = row_count * lax.axis_size("blk")
    link_next = passed_along(stiff_link[:1], "blk", -1)
    link_after = jnp.concatenate([stiff_link[1:], link_next], 0)

    def stiff_apply(vectors):
        padded = extended_2(vectors, (("blk", 0),), block_size)
        extended = padded.reshape(blocks_dev + 2, block_size, mode_count)
        result = block_product(stiff_self, extended[1 : blocks_dev + 1]) + block_product(
            stiff_link, extended[:blocks_dev]
        )
        result = result + jnp.einsum("bji,bjm->bim", link_after, extended[2:], precision=fast)
        return result.reshape(row_count, mode_count)

    def mass_apply(vectors):
        return block_product(
            mass_self, vectors.reshape(blocks_dev, block_size, mode_count)
        ).reshape(row_count, mode_count)

    def gram_matrix(left, right):
        return jnp.dot(left.T, right, precision=fast)

    first = start_flat - step_size * stiff_apply(start_flat)
    second = first - step_size * stiff_apply(first)
    iface_count = global_ids.shape[0]
    block_terms = jnp.einsum(
        "bkm,bkl->bml",
        second.reshape(blocks_dev, block_size, mode_count),
        coupling_blocks,
        precision=fast,
    )
    onehot = (interface_ids[:, None] == jnp.arange(iface_count, dtype=jnp.int32)[None, :]).astype(
        jnp.float32
    )
    coupling_term = jnp.einsum("bj,bml->mjl", onehot, block_terms, precision=highest)
    second, coupling_term = lax.optimization_barrier((second, coupling_term))
    coupling_sum = permute_sum(coupling_term, "blk")
    stiff_second = stiff_apply(second)
    first_gram, mass_gram, stiff_gram = permute_sum(
        jnp.stack(
            [
                gram_matrix(first, mass_apply(first)),
                gram_matrix(second, mass_apply(second)),
                gram_matrix(second, stiff_second),
            ]
        ),
        "blk",
    )
    grams = jnp.stack([first_gram, mass_gram, stiff_gram]) / dof_count
    inverses = inverse_factors(0.5 * (grams + jnp.swapaxes(grams, 1, 2)))
    guard = 0.0 * jnp.sum(inverses[0])
    factor_inv = inverses[1] + guard
    chain_inv = inverses[2] + guard
    basis = jnp.dot(second, factor_inv.T, precision=fast)
    reduced = (
        jnp.dot(
            jnp.dot(factor_inv, stiff_gram, precision=highest), factor_inv.T, precision=highest
        )
        / dof_count
    )
    scaled = jnp.einsum("nm,mjl->njl", chain_inv, coupling_sum, precision=highest) / dof_count**0.5
    condensed = jnp.einsum("njk,njl->jkl", scaled, scaled, precision=highest)
    global_count = GIFC * lax.axis_size("comp")
    placed = (global_ids[:, None] == jnp.arange(global_count, dtype=jnp.int32)[None, :]).astype(
        jnp.float32
    )
    dense_sum = jnp.einsum("jg,jkl->gkl", placed, condensed, precision=highest)
    owned = lax.psum_scatter(dense_sum, "comp", scatter_dimension=0, tiled=True)
    return (basis[None], reduced[None], owned)


def solution(mesh):
    in_specs = (
        P("comp", "blk", None),
        P("comp", "blk", None, None),
        P("comp", "blk", None, None),
        P("comp", "blk", None, None),
        P("comp", "blk", None, None),
        P("comp", "blk"),
        P("comp", None),
    )
    out_specs = (P("comp", "blk", None), P("comp", None, None), P("comp", None, None))
    return jax.shard_map(local, mesh=mesh, in_specs=in_specs, out_specs=out_specs, check_vma=False)
```

```python
import jax
import jax.numpy as jnp
from jax import lax
from jax.experimental import pallas as pl
from jax.experimental.pallas import tpu as pltpu
from jax.sharding import PartitionSpec as P

ITERS = 2
GIFC = 4


highest = lax.Precision.HIGHEST
fast = lax.Precision.HIGH
step_size = 0.15


def passed_along(value, axis, steps):
    count = lax.axis_size(axis)
    initial, last = (max(0, -steps), min(count, count - steps))
    return lax.ppermute(value, axis, [(source, source + steps) for source in range(initial, last)])


def extended_2(block, sides, width):
    for axis, dim in sides:
        count = lax.axis_size(axis)
        forward = [(i, i + 1) for i in range(count - 1)]
        backward = [(target, source) for source, target in forward]
        low = lax.ppermute(
            lax.slice_in_dim(block, block.shape[dim] - width, None, axis=dim), axis, forward
        )
        high = lax.ppermute(lax.slice_in_dim(block, 0, width, axis=dim), axis, backward)
        block = jnp.concatenate([low, block, high], axis=dim)
    return block


def permute_sum(value, axis, order):
    count = lax.axis_size(axis)
    rounds = count.bit_length() - 1
    assert count == 1 << rounds and sorted(order) == list(range(rounds))
    me = lax.axis_index(axis)
    shape = value.shape
    flat = value.reshape(-1)
    piece = flat.shape[0] >> rounds
    assert piece << rounds == flat.shape[0]
    for level in order:
        half = flat.shape[0] // 2
        upper = (me >> level) & 1
        pairs = [(i, i ^ (1 << level)) for i in range(count)]
        sent = lax.dynamic_slice_in_dim(flat, (1 - upper) * half, half)
        kept = lax.dynamic_slice_in_dim(flat, upper * half, half)
        flat = kept + lax.ppermute(sent, axis, pairs)
    for level in reversed(order):
        upper = (me >> level) & 1
        pairs = [(i, i ^ (1 << level)) for i in range(count)]
        other = lax.ppermute(flat, axis, pairs)
        flat = jnp.where(
            upper == 1, jnp.concatenate([other, flat]), jnp.concatenate([flat, other])
        )
    return flat.reshape(shape)


def block_product(blocks, vectors):
    return jnp.einsum("bij,bjm->bim", blocks, vectors, precision=fast)


def _inverse_factor_kernel(a_in, w_out, a_ref, x_ref):
    batch, size, _ = a_in.shape
    a_ref[...] = a_in[...]
    rows = lax.broadcasted_iota(jnp.int32, (size, size), 0)
    cols = lax.broadcasted_iota(jnp.int32, (size, size), 1)
    eye = jnp.where(rows == cols, 1.0, 0.0).astype(jnp.float32)
    x_ref[...] = jnp.broadcast_to(eye, (batch, size, size))
    phase = 64
    lanes = 128
    sublanes = 8

    def row_of(ref, k, col0, col1):
        tile0 = pl.multiple_of((k // sublanes) * sublanes, sublanes)
        tile = ref[:, pl.ds(tile0, sublanes), col0:col1]
        sub = lax.broadcasted_iota(jnp.int32, tile.shape, 1) + tile0
        return jnp.sum(jnp.where(sub == k, tile, 0.0), axis=1, keepdims=True)

    for start in range(0, size, phase):
        a_col0 = (start // lanes) * lanes
        x_col1 = min(size, -(-(start + phase) // lanes) * lanes)

        def step(k, carry, start=start, a_col0=a_col0, x_col1=x_col1):
            row_a = row_of(a_ref, k, a_col0, size)
            row_x = row_of(x_ref, k, 0, x_col1)
            block0 = pl.multiple_of((k // lanes) * lanes, lanes)
            col_block = a_ref[:, start:, pl.ds(block0, lanes)]
            lane = lax.broadcasted_iota(jnp.int32, col_block.shape, 2) + block0
            col = jnp.sum(jnp.where(lane == k, col_block, 0.0), axis=2, keepdims=True)
            lane_a = lax.broadcasted_iota(jnp.int32, row_a.shape, 2) + a_col0
            pivot = jnp.sum(jnp.where(lane_a == k, row_a, 0.0), axis=2, keepdims=True)
            row_ids = lax.broadcasted_iota(jnp.int32, col.shape, 1) + start
            mult = jnp.where(row_ids > k, col / pivot, 0.0)
            a_ref[:, start:, a_col0:] = a_ref[:, start:, a_col0:] - mult * row_a
            x_ref[:, start:, :x_col1] = x_ref[:, start:, :x_col1] - mult * row_x
            return carry

        lax.fori_loop(start, start + phase, step, 0)
    pivots = jnp.sum(jnp.where(rows == cols, a_ref[...], 0.0), axis=2, keepdims=True)
    w_out[...] = x_ref[...] * lax.rsqrt(pivots)


def inverse_factors(matrices):
    batch, size, _ = matrices.shape
    return pl.pallas_call(
        _inverse_factor_kernel,
        out_shape=jax.ShapeDtypeStruct(matrices.shape, jnp.float32),
        in_specs=[pl.BlockSpec(memory_space=pltpu.VMEM)],
        out_specs=pl.BlockSpec(memory_space=pltpu.VMEM),
        scratch_shapes=[
            pltpu.VMEM(matrices.shape, jnp.float32),
            pltpu.VMEM(matrices.shape, jnp.float32),
        ],
    )(matrices)


def local(start_modes, stiff_diag, stiff_off, mass_blocks, coupling, interface_block, global_iface):
    start_flat = start_modes[0]
    stiff_self = stiff_diag[0]
    stiff_link = stiff_off[0]
    mass_self = mass_blocks[0]
    coupling_blocks = coupling[0]
    interface_ids = interface_block[0]
    global_ids = global_iface[0]
    row_count, mode_count = start_flat.shape
    blocks_dev = stiff_self.shape[0]
    block_size = stiff_self.shape[1]
    dof_count = row_count * lax.axis_size("blk")
    link_next = passed_along(stiff_link[:1], "blk", -1)
    link_after = jnp.concatenate([stiff_link[1:], link_next], 0)

    def stiff_apply(vectors):
        padded = extended_2(vectors, (("blk", 0),), block_size)
        extended = padded.reshape(blocks_dev + 2, block_size, mode_count)
        result = block_product(stiff_self, extended[1 : blocks_dev + 1]) + block_product(
            stiff_link, extended[:blocks_dev]
        )
        result = result + jnp.einsum("bji,bjm->bim", link_after, extended[2:], precision=fast)
        return result.reshape(row_count, mode_count)

    def mass_apply(vectors):
        return block_product(
            mass_self, vectors.reshape(blocks_dev, block_size, mode_count)
        ).reshape(row_count, mode_count)

    def gram_matrix(left, right):
        return jnp.dot(left.T, right, precision=fast)

    first = start_flat - step_size * stiff_apply(start_flat)
    second = first - step_size * stiff_apply(first)
    iface_count = global_ids.shape[0]
    block_terms = jnp.einsum(
        "bkm,bkl->bml",
        second.reshape(blocks_dev, block_size, mode_count),
        coupling_blocks,
        precision=fast,
    )
    onehot = (interface_ids[:, None] == jnp.arange(iface_count, dtype=jnp.int32)[None, :]).astype(
        jnp.float32
    )
    coupling_term = jnp.einsum("bj,bml->mjl", onehot, block_terms, precision=highest)
    second, coupling_term = lax.optimization_barrier((second, coupling_term))
    rounds = lax.axis_size("blk").bit_length() - 1
    levels = list(range(rounds))
    swapped = levels[1:2] + levels[:1] + levels[2:]
    coupling_sum = permute_sum(coupling_term, "blk", swapped)
    stiff_second = stiff_apply(second)
    first_gram, mass_gram, stiff_gram = permute_sum(
        jnp.stack(
            [
                gram_matrix(first, mass_apply(first)),
                gram_matrix(second, mass_apply(second)),
                gram_matrix(second, stiff_second),
            ]
        ),
        "blk",
        levels,
    )
    grams = jnp.stack([first_gram, mass_gram, stiff_gram]) / dof_count
    inverses = inverse_factors(0.5 * (grams + jnp.swapaxes(grams, 1, 2)))
    guard = 0.0 * jnp.sum(inverses[0])
    factor_inv = inverses[1] + guard
    chain_inv = inverses[2] + guard
    basis = jnp.dot(second, factor_inv.T, precision=fast)
    reduced = (
        jnp.dot(
            jnp.dot(factor_inv, stiff_gram, precision=highest), factor_inv.T, precision=highest
        )
        / dof_count
    )
    scaled = jnp.einsum("nm,mjl->njl", chain_inv, coupling_sum, precision=highest) / dof_count**0.5
    condensed = jnp.einsum("njk,njl->jkl", scaled, scaled, precision=highest)
    global_count = GIFC * lax.axis_size("comp")
    placed = (global_ids[:, None] == jnp.arange(global_count, dtype=jnp.int32)[None, :]).astype(
        jnp.float32
    )
    dense_sum = jnp.einsum("jg,jkl->gkl", placed, condensed, precision=highest)
    owned = lax.psum_scatter(dense_sum, "comp", scatter_dimension=0, tiled=True)
    return (basis[None], reduced[None], owned)


def solution(mesh):
    in_specs = (
        P("comp", "blk", None),
        P("comp", "blk", None, None),
        P("comp", "blk", None, None),
        P("comp", "blk", None, None),
        P("comp", "blk", None, None),
        P("comp", "blk"),
        P("comp", None),
    )
    out_specs = (P("comp", "blk", None), P("comp", None, None), P("comp", None, None))
    return jax.shard_map(local, mesh=mesh, in_specs=in_specs, out_specs=out_specs, check_vma=False)
```

```python
import jax
import jax.numpy as jnp
from jax import lax
from jax.experimental import pallas as pl
from jax.experimental.pallas import tpu as pltpu
from jax.sharding import PartitionSpec as P

ITERS = 2
GIFC = 4


highest = lax.Precision.HIGHEST
fast = lax.Precision.HIGH
step_size = 0.15


def passed_along(value, axis, steps):
    count = lax.axis_size(axis)
    initial, last = (max(0, -steps), min(count, count - steps))
    return lax.ppermute(value, axis, [(source, source + steps) for source in range(initial, last)])


def extended_2(block, sides, width):
    for axis, dim in sides:
        count = lax.axis_size(axis)
        forward = [(i, i + 1) for i in range(count - 1)]
        backward = [(target, source) for source, target in forward]
        low = lax.ppermute(
            lax.slice_in_dim(block, block.shape[dim] - width, None, axis=dim), axis, forward
        )
        high = lax.ppermute(lax.slice_in_dim(block, 0, width, axis=dim), axis, backward)
        block = jnp.concatenate([low, block, high], axis=dim)
    return block


def permute_sum(value, axis, order):
    count = lax.axis_size(axis)
    rounds = count.bit_length() - 1
    assert count == 1 << rounds and sorted(order) == list(range(rounds))
    me = lax.axis_index(axis)
    shape = value.shape
    flat = value.reshape(-1)
    piece = flat.shape[0] >> rounds
    assert piece << rounds == flat.shape[0]
    for level in order:
        half = flat.shape[0] // 2
        upper = (me >> level) & 1
        pairs = [(i, i ^ (1 << level)) for i in range(count)]
        sent = lax.dynamic_slice_in_dim(flat, (1 - upper) * half, half)
        kept = lax.dynamic_slice_in_dim(flat, upper * half, half)
        flat = kept + lax.ppermute(sent, axis, pairs)
    for level in reversed(order):
        upper = (me >> level) & 1
        pairs = [(i, i ^ (1 << level)) for i in range(count)]
        other = lax.ppermute(flat, axis, pairs)
        flat = jnp.where(
            upper == 1, jnp.concatenate([other, flat]), jnp.concatenate([flat, other])
        )
    return flat.reshape(shape)


def block_product(blocks, vectors):
    return jnp.einsum("bij,bjm->bim", blocks, vectors, precision=fast)


def _inverse_factor_kernel(a_in, w_out, root_out, a_ref, x_ref):
    batch, size, _ = a_in.shape
    solved = x_ref.shape[0]
    a_ref[...] = a_in[...]
    rows = lax.broadcasted_iota(jnp.int32, (size, size), 0)
    cols = lax.broadcasted_iota(jnp.int32, (size, size), 1)
    eye = jnp.where(rows == cols, 1.0, 0.0).astype(jnp.float32)
    x_ref[...] = jnp.broadcast_to(eye, x_ref.shape)
    phase = 32
    lanes = 128
    sublanes = 8

    def pick_rows(tile, tile0, k):
        sub = lax.broadcasted_iota(jnp.int32, tile.shape, 1) + tile0
        first = jnp.sum(jnp.where(sub == k, tile, 0.0), axis=1, keepdims=True)
        second = jnp.sum(jnp.where(sub == k + 1, tile, 0.0), axis=1, keepdims=True)
        return first, second

    def lane_value(row, col0, k):
        lane = lax.broadcasted_iota(jnp.int32, row.shape, 2) + col0
        return jnp.sum(jnp.where(lane == k, row, 0.0), axis=2, keepdims=True)

    for start in range(0, size, phase):
        a_col0 = (start // lanes) * lanes
        x_col1 = min(size, -(-(start + phase) // lanes) * lanes)

        def step(pair, carry, start=start, a_col0=a_col0, x_col1=x_col1):
            k = start + 2 * pair
            tile0 = pl.multiple_of((k // sublanes) * sublanes, sublanes)
            row_a0, row_a1 = pick_rows(a_ref[:, pl.ds(tile0, sublanes), a_col0:], tile0, k)
            row_x0, row_x1 = pick_rows(x_ref[:, pl.ds(tile0, sublanes), :x_col1], tile0, k)
            block0 = pl.multiple_of((k // lanes) * lanes, lanes)
            col_block = a_ref[:, start:, pl.ds(block0, lanes)]
            lane = lax.broadcasted_iota(jnp.int32, col_block.shape, 2) + block0
            col0 = jnp.sum(jnp.where(lane == k, col_block, 0.0), axis=2, keepdims=True)
            col1 = jnp.sum(jnp.where(lane == k + 1, col_block, 0.0), axis=2, keepdims=True)
            pivot0 = lane_value(row_a0, a_col0, k)
            upper01 = lane_value(row_a0, a_col0, k + 1)
            lower10 = lane_value(row_a1, a_col0, k)
            diag11 = lane_value(row_a1, a_col0, k + 1)
            ratio = lower10 / pivot0
            pivot1 = diag11 - ratio * upper01
            row_ids = lax.broadcasted_iota(jnp.int32, col0.shape, 1) + start
            mult0 = jnp.where(row_ids > k, col0 / pivot0, 0.0)
            mult1 = jnp.where(row_ids > k + 1, (col1 - mult0 * upper01) / pivot1, 0.0)
            row_a1 = row_a1 - ratio * row_a0
            row_x1 = row_x1 - ratio[batch - solved :] * row_x0
            a_ref[:, start:, a_col0:] = a_ref[:, start:, a_col0:] - mult0 * row_a0 - mult1 * row_a1
            x_ref[:, start:, :x_col1] = (
                x_ref[:, start:, :x_col1]
                - mult0[batch - solved :] * row_x0
                - mult1[batch - solved :] * row_x1
            )
            return carry

        lax.fori_loop(0, phase // 2, step, 0)
    pivots = jnp.sum(jnp.where(rows == cols, a_ref[...], 0.0), axis=2, keepdims=True)
    roots = lax.rsqrt(pivots)
    w_out[...] = x_ref[...] * roots[batch - solved :]
    root_out[...] = jnp.broadcast_to(roots, root_out.shape)


def inverse_factors(matrices, solved):
    batch, size, _ = matrices.shape
    return pl.pallas_call(
        _inverse_factor_kernel,
        out_shape=(
            jax.ShapeDtypeStruct((solved, size, size), jnp.float32),
            jax.ShapeDtypeStruct((batch, size, 128), jnp.float32),
        ),
        in_specs=[pl.BlockSpec(memory_space=pltpu.VMEM)],
        out_specs=(pl.BlockSpec(memory_space=pltpu.VMEM), pl.BlockSpec(memory_space=pltpu.VMEM)),
        scratch_shapes=[
            pltpu.VMEM(matrices.shape, jnp.float32),
            pltpu.VMEM((solved, size, size), jnp.float32),
        ],
    )(matrices)


def local(start_modes, stiff_diag, stiff_off, mass_blocks, coupling, interface_block, global_iface):
    start_flat = start_modes[0]
    stiff_self = stiff_diag[0]
    stiff_link = stiff_off[0]
    mass_self = mass_blocks[0]
    coupling_blocks = coupling[0]
    interface_ids = interface_block[0]
    global_ids = global_iface[0]
    row_count, mode_count = start_flat.shape
    blocks_dev = stiff_self.shape[0]
    block_size = stiff_self.shape[1]
    dof_count = row_count * lax.axis_size("blk")
    link_next = passed_along(stiff_link[:1], "blk", -1)
    link_after = jnp.concatenate([stiff_link[1:], link_next], 0)

    def stiff_apply(vectors):
        padded = extended_2(vectors, (("blk", 0),), block_size)
        extended = padded.reshape(blocks_dev + 2, block_size, mode_count)
        result = block_product(stiff_self, extended[1 : blocks_dev + 1]) + block_product(
            stiff_link, extended[:blocks_dev]
        )
        result = result + jnp.einsum("bji,bjm->bim", link_after, extended[2:], precision=fast)
        return result.reshape(row_count, mode_count)

    def mass_apply(vectors):
        return block_product(
            mass_self, vectors.reshape(blocks_dev, block_size, mode_count)
        ).reshape(row_count, mode_count)

    def gram_matrix(left, right):
        return jnp.dot(left.T, right, precision=fast)

    first = start_flat - step_size * stiff_apply(start_flat)
    second = first - step_size * stiff_apply(first)
    iface_count = global_ids.shape[0]
    block_terms = jnp.einsum(
        "bkm,bkl->bml",
        second.reshape(blocks_dev, block_size, mode_count),
        coupling_blocks,
        precision=fast,
    )
    onehot = (interface_ids[:, None] == jnp.arange(iface_count, dtype=jnp.int32)[None, :]).astype(
        jnp.float32
    )
    coupling_term = jnp.einsum("bj,bml->mjl", onehot, block_terms, precision=highest)
    second, coupling_term = lax.optimization_barrier((second, coupling_term))
    rounds = lax.axis_size("blk").bit_length() - 1
    levels = list(range(rounds))
    swapped = levels[1:2] + levels[:1] + levels[2:]
    coupling_sum = permute_sum(coupling_term, "blk", swapped)
    stiff_second = stiff_apply(second)
    first_gram, mass_gram, stiff_gram = permute_sum(
        jnp.stack(
            [
                gram_matrix(first, mass_apply(first)),
                gram_matrix(second, mass_apply(second)),
                gram_matrix(second, stiff_second),
            ]
        ),
        "blk",
        levels,
    )
    grams = jnp.stack([first_gram, mass_gram, stiff_gram]) / dof_count
    inverses, roots = inverse_factors(0.5 * (grams + jnp.swapaxes(grams, 1, 2)), 2)
    guard = 0.0 * jnp.sum(roots[0])
    factor_inv = inverses[0] + guard
    chain_inv = inverses[1] + guard
    basis = jnp.dot(second, factor_inv.T, precision=fast)
    reduced = (
        jnp.dot(
            jnp.dot(factor_inv, stiff_gram, precision=highest), factor_inv.T, precision=highest
        )
        / dof_count
    )
    scaled = jnp.einsum("nm,mjl->njl", chain_inv, coupling_sum, precision=highest) / dof_count**0.5
    condensed = jnp.einsum("njk,njl->jkl", scaled, scaled, precision=highest)
    global_count = GIFC * lax.axis_size("comp")
    placed = (global_ids[:, None] == jnp.arange(global_count, dtype=jnp.int32)[None, :]).astype(
        jnp.float32
    )
    dense_sum = jnp.einsum("jg,jkl->gkl", placed, condensed, precision=highest)
    owned = lax.psum_scatter(dense_sum, "comp", scatter_dimension=0, tiled=True)
    return (basis[None], reduced[None], owned)


def solution(mesh):
    in_specs = (
        P("comp", "blk", None),
        P("comp", "blk", None, None),
        P("comp", "blk", None, None),
        P("comp", "blk", None, None),
        P("comp", "blk", None, None),
        P("comp", "blk"),
        P("comp", None),
    )
    out_specs = (P("comp", "blk", None), P("comp", None, None), P("comp", None, None))
    return jax.shard_map(local, mesh=mesh, in_specs=in_specs, out_specs=out_specs, check_vma=False)
```

```python
import jax
import jax.numpy as jnp
from jax import lax
from jax.experimental import pallas as pl
from jax.experimental.pallas import tpu as pltpu
from jax.sharding import PartitionSpec as P

ITERS = 2
GIFC = 4


highest = lax.Precision.HIGHEST
fast = lax.Precision.HIGH
step_size = 0.15


def passed_along(value, axis, steps):
    count = lax.axis_size(axis)
    initial, last = (max(0, -steps), min(count, count - steps))
    return lax.ppermute(value, axis, [(source, source + steps) for source in range(initial, last)])


def extended_2(block, sides, width):
    for axis, dim in sides:
        count = lax.axis_size(axis)
        forward = [(i, i + 1) for i in range(count - 1)]
        backward = [(target, source) for source, target in forward]
        low = lax.ppermute(
            lax.slice_in_dim(block, block.shape[dim] - width, None, axis=dim), axis, forward
        )
        high = lax.ppermute(lax.slice_in_dim(block, 0, width, axis=dim), axis, backward)
        block = jnp.concatenate([low, block, high], axis=dim)
    return block


def permute_sum(value, axis, order):
    count = lax.axis_size(axis)
    rounds = count.bit_length() - 1
    assert count == 1 << rounds and sorted(order) == list(range(rounds))
    me = lax.axis_index(axis)
    shape = value.shape
    flat = value.reshape(-1)
    piece = flat.shape[0] >> rounds
    assert piece << rounds == flat.shape[0]
    for level in order:
        half = flat.shape[0] // 2
        upper = (me >> level) & 1
        pairs = [(i, i ^ (1 << level)) for i in range(count)]
        sent = lax.dynamic_slice_in_dim(flat, (1 - upper) * half, half)
        kept = lax.dynamic_slice_in_dim(flat, upper * half, half)
        flat = kept + lax.ppermute(sent, axis, pairs)
    for level in reversed(order):
        upper = (me >> level) & 1
        pairs = [(i, i ^ (1 << level)) for i in range(count)]
        other = lax.ppermute(flat, axis, pairs)
        flat = jnp.where(
            upper == 1, jnp.concatenate([other, flat]), jnp.concatenate([flat, other])
        )
    return flat.reshape(shape)


def block_product(blocks, vectors):
    return jnp.einsum("bij,bjm->bim", blocks, vectors, precision=fast)


def _inverse_factor_kernel(a_in, w_out, root_out, a_ref, x_ref):
    batch, size, _ = a_in.shape
    solved = x_ref.shape[0]
    a_ref[...] = a_in[...]
    rows = lax.broadcasted_iota(jnp.int32, (size, size), 0)
    cols = lax.broadcasted_iota(jnp.int32, (size, size), 1)
    eye = jnp.where(rows == cols, 1.0, 0.0).astype(jnp.float32)
    x_ref[...] = jnp.broadcast_to(eye, x_ref.shape)
    phase = 32
    lanes = 128
    sublanes = 8

    def pick_rows(tile, tile0, k):
        sub = lax.broadcasted_iota(jnp.int32, tile.shape, 1) + tile0
        first = jnp.sum(jnp.where(sub == k, tile, 0.0), axis=1, keepdims=True)
        second = jnp.sum(jnp.where(sub == k + 1, tile, 0.0), axis=1, keepdims=True)
        return first, second

    def lane_value(row, col0, k):
        lane = lax.broadcasted_iota(jnp.int32, row.shape, 2) + col0
        return jnp.sum(jnp.where(lane == k, row, 0.0), axis=2, keepdims=True)

    for start in range(0, size, phase):
        a_col0 = (start // lanes) * lanes
        x_col1 = min(size, -(-(start + phase) // lanes) * lanes)

        def step(pair, carry, start=start, a_col0=a_col0, x_col1=x_col1):
            k = start + 2 * pair
            tile0 = pl.multiple_of((k // sublanes) * sublanes, sublanes)
            row_a0, row_a1 = pick_rows(a_ref[:, pl.ds(tile0, sublanes), a_col0:], tile0, k)
            row_x0, row_x1 = pick_rows(x_ref[:, pl.ds(tile0, sublanes), :x_col1], tile0, k)
            block0 = pl.multiple_of((k // lanes) * lanes, lanes)
            col_block = a_ref[:, start:, pl.ds(block0, lanes)]
            lane = lax.broadcasted_iota(jnp.int32, col_block.shape, 2) + block0
            col0 = jnp.sum(jnp.where(lane == k, col_block, 0.0), axis=2, keepdims=True)
            col1 = jnp.sum(jnp.where(lane == k + 1, col_block, 0.0), axis=2, keepdims=True)
            pivot0 = lane_value(row_a0, a_col0, k)
            upper01 = lane_value(row_a0, a_col0, k + 1)
            lower10 = lane_value(row_a1, a_col0, k)
            diag11 = lane_value(row_a1, a_col0, k + 1)
            ratio = lower10 / pivot0
            pivot1 = diag11 - ratio * upper01
            row_ids = lax.broadcasted_iota(jnp.int32, col0.shape, 1) + start
            mult0 = jnp.where(row_ids > k, col0 / pivot0, 0.0)
            mult1 = jnp.where(row_ids > k + 1, (col1 - mult0 * upper01) / pivot1, 0.0)
            row_a1 = row_a1 - ratio * row_a0
            row_x1 = row_x1 - ratio[batch - solved :] * row_x0
            a_ref[:, start:, a_col0:] = a_ref[:, start:, a_col0:] - mult0 * row_a0 - mult1 * row_a1
            x_ref[:, start:, :x_col1] = (
                x_ref[:, start:, :x_col1]
                - mult0[batch - solved :] * row_x0
                - mult1[batch - solved :] * row_x1
            )
            return carry

        lax.fori_loop(0, phase // 2, step, 0)
    pivots = jnp.sum(jnp.where(rows == cols, a_ref[...], 0.0), axis=2, keepdims=True)
    roots = lax.rsqrt(pivots)
    w_out[...] = x_ref[...] * roots[batch - solved :]
    root_out[...] = jnp.broadcast_to(roots, root_out.shape)


def inverse_factors(matrices, solved):
    batch, size, _ = matrices.shape
    return pl.pallas_call(
        _inverse_factor_kernel,
        out_shape=(
            jax.ShapeDtypeStruct((solved, size, size), jnp.float32),
            jax.ShapeDtypeStruct((batch, size, 128), jnp.float32),
        ),
        in_specs=[pl.BlockSpec(memory_space=pltpu.VMEM)],
        out_specs=(pl.BlockSpec(memory_space=pltpu.VMEM), pl.BlockSpec(memory_space=pltpu.VMEM)),
        scratch_shapes=[
            pltpu.VMEM(matrices.shape, jnp.float32),
            pltpu.VMEM((solved, size, size), jnp.float32),
        ],
    )(matrices)


def local(start_modes, stiff_diag, stiff_off, mass_blocks, coupling, interface_block, global_iface):
    start_flat = start_modes[0]
    stiff_self = stiff_diag[0]
    stiff_link = stiff_off[0]
    mass_self = mass_blocks[0]
    coupling_blocks = coupling[0]
    interface_ids = interface_block[0]
    global_ids = global_iface[0]
    row_count, mode_count = start_flat.shape
    blocks_dev = stiff_self.shape[0]
    block_size = stiff_self.shape[1]
    dof_count = row_count * lax.axis_size("blk")
    link_next = passed_along(stiff_link[:1], "blk", -1)
    link_after = jnp.concatenate([stiff_link[1:], link_next], 0)

    def stiff_apply(vectors):
        padded = extended_2(vectors, (("blk", 0),), block_size)
        extended = padded.reshape(blocks_dev + 2, block_size, mode_count)
        result = block_product(stiff_self, extended[1 : blocks_dev + 1]) + block_product(
            stiff_link, extended[:blocks_dev]
        )
        result = result + jnp.einsum("bji,bjm->bim", link_after, extended[2:], precision=fast)
        return result.reshape(row_count, mode_count)

    def mass_apply(vectors):
        return block_product(
            mass_self, vectors.reshape(blocks_dev, block_size, mode_count)
        ).reshape(row_count, mode_count)

    def gram_matrix(left, right):
        return jnp.dot(left.T, right, precision=fast)

    first = start_flat - step_size * stiff_apply(start_flat)
    second = first - step_size * stiff_apply(first)
    iface_count = global_ids.shape[0]
    block_terms = jnp.einsum(
        "bkm,bkl->bml",
        second.reshape(blocks_dev, block_size, mode_count),
        coupling_blocks,
        precision=fast,
    )
    onehot = (interface_ids[:, None] == jnp.arange(iface_count, dtype=jnp.int32)[None, :]).astype(
        jnp.float32
    )
    coupling_term = jnp.einsum("bj,bml->mjl", onehot, block_terms, precision=highest)
    second, coupling_term = lax.optimization_barrier((second, coupling_term))
    rounds = lax.axis_size("blk").bit_length() - 1
    levels = list(range(rounds))
    swapped = levels[1:2] + levels[:1] + levels[2:]
    coupling_sum = permute_sum(coupling_term, "blk", swapped)
    stiff_second = stiff_apply(second)
    first_gram, mass_gram, stiff_gram = permute_sum(
        jnp.stack(
            [
                gram_matrix(first, mass_apply(first)),
                gram_matrix(second, mass_apply(second)),
                gram_matrix(second, stiff_second),
            ]
        ),
        "blk",
        levels,
    )
    grams = jnp.stack([first_gram, mass_gram, stiff_gram]) / dof_count
    inverses, roots = inverse_factors(0.5 * (grams + jnp.swapaxes(grams, 1, 2)), 2)
    guard = 0.0 * jnp.sum(roots[0])
    factor_inv = inverses[0] + guard
    chain_inv = inverses[1] + guard
    basis = jnp.dot(second, factor_inv.T, precision=fast)
    reduced = (
        jnp.dot(
            jnp.dot(factor_inv, stiff_gram, precision=highest), factor_inv.T, precision=highest
        )
        / dof_count
    )
    scaled = jnp.einsum("nm,mjl->njl", chain_inv, coupling_sum, precision=highest) / dof_count**0.5
    condensed = jnp.einsum("njk,njl->jkl", scaled, scaled, precision=highest)
    global_count = GIFC * lax.axis_size("comp")
    placed = (global_ids[:, None] == jnp.arange(global_count, dtype=jnp.int32)[None, :]).astype(
        jnp.float32
    )
    dense_sum = jnp.einsum("jg,jkl->gkl", placed, condensed, precision=highest)
    comp_count = lax.axis_size("comp")
    comp_me = lax.axis_index("comp")
    owned = lax.dynamic_slice_in_dim(dense_sum, comp_me * GIFC, GIFC)
    for shift in range(1, comp_count):
        target = lax.rem(comp_me + shift, comp_count)
        outgoing = lax.dynamic_slice_in_dim(dense_sum, target * GIFC, GIFC)
        pairs = [(i, (i + shift) % comp_count) for i in range(comp_count)]
        owned = owned + lax.ppermute(outgoing, "comp", pairs)
    return (basis[None], reduced[None], owned)


def solution(mesh):
    in_specs = (
        P("comp", "blk", None),
        P("comp", "blk", None, None),
        P("comp", "blk", None, None),
        P("comp", "blk", None, None),
        P("comp", "blk", None, None),
        P("comp", "blk"),
        P("comp", None),
    )
    out_specs = (P("comp", "blk", None), P("comp", None, None), P("comp", None, None))
    return jax.shard_map(local, mesh=mesh, in_specs=in_specs, out_specs=out_specs, check_vma=False)
```

```python
import functools
import jax
import jax.numpy as jnp
from jax import lax
from jax.experimental import pallas as pl
from jax.experimental.pallas import tpu as pltpu
from jax.sharding import PartitionSpec as P

ITERS = 2
GIFC = 4


highest = lax.Precision.HIGHEST
fast = lax.Precision.HIGH
step_size = 0.15


def passed_along(value, axis, steps):
    count = lax.axis_size(axis)
    initial, last = (max(0, -steps), min(count, count - steps))
    return lax.ppermute(value, axis, [(source, source + steps) for source in range(initial, last)])


def extended_2(block, sides, width):
    for axis, dim in sides:
        count = lax.axis_size(axis)
        forward = [(i, i + 1) for i in range(count - 1)]
        backward = [(target, source) for source, target in forward]
        low = lax.ppermute(
            lax.slice_in_dim(block, block.shape[dim] - width, None, axis=dim), axis, forward
        )
        high = lax.ppermute(lax.slice_in_dim(block, 0, width, axis=dim), axis, backward)
        block = jnp.concatenate([low, block, high], axis=dim)
    return block


def permute_sum(value, axis, order):
    count = lax.axis_size(axis)
    rounds = count.bit_length() - 1
    assert count == 1 << rounds and sorted(order) == list(range(rounds))
    me = lax.axis_index(axis)
    shape = value.shape
    flat = value.reshape(-1)
    piece = flat.shape[0] >> rounds
    assert piece << rounds == flat.shape[0]
    for level in order:
        half = flat.shape[0] // 2
        upper = (me >> level) & 1
        pairs = [(i, i ^ (1 << level)) for i in range(count)]
        sent = lax.dynamic_slice_in_dim(flat, (1 - upper) * half, half)
        kept = lax.dynamic_slice_in_dim(flat, upper * half, half)
        flat = kept + lax.ppermute(sent, axis, pairs)
    for level in reversed(order):
        upper = (me >> level) & 1
        pairs = [(i, i ^ (1 << level)) for i in range(count)]
        other = lax.ppermute(flat, axis, pairs)
        flat = jnp.where(
            upper == 1, jnp.concatenate([other, flat]), jnp.concatenate([flat, other])
        )
    return flat.reshape(shape)


def block_product(blocks, vectors):
    return jnp.einsum("bij,bjm->bim", blocks, vectors, precision=fast)


def _split_dot(left, right):
    left_hi = left.astype(jnp.bfloat16)
    left_lo = (left - left_hi.astype(jnp.float32)).astype(jnp.bfloat16)
    right_hi = right.astype(jnp.bfloat16)
    right_lo = (right - right_hi.astype(jnp.float32)).astype(jnp.bfloat16)
    total = jnp.dot(left_hi, right_hi, preferred_element_type=jnp.float32)
    total = total + jnp.dot(left_lo, right_hi, preferred_element_type=jnp.float32)
    return total + jnp.dot(left_hi, right_lo, preferred_element_type=jnp.float32)


def _stiff_kernel(keep, scale, group, x_ref, prev_ref, next_ref, low_ref, high_ref,
                  diag_ref, link_ref, after_ref, out_ref):
    step = pl.program_id(0)
    last = pl.num_programs(0) - 1
    before = jnp.where(step == 0, low_ref[0], prev_ref[0])
    beyond = jnp.where(step == last, high_ref[0], next_ref[0])
    for j in range(group):
        here = x_ref[j]
        left = before if j == 0 else x_ref[j - 1]
        right = beyond if j == group - 1 else x_ref[j + 1]
        acc = _split_dot(diag_ref[j], here)
        acc = acc + _split_dot(link_ref[j], left)
        acc = acc + _split_dot(after_ref[j], right)
        out_ref[j] = scale * acc if keep == 0.0 else keep * here + scale * acc


def stiff_filter(vectors, low, high, diag, link, after_t, keep, scale, group=4):
    blocks, size, modes = vectors.shape
    steps = blocks // group
    assert steps * group == blocks
    block_spec = pl.BlockSpec((group, size, modes), lambda g: (g, 0, 0))
    single = (1, size, modes)
    mat_spec = pl.BlockSpec((group, size, size), lambda g: (g, 0, 0))
    return pl.pallas_call(
        functools.partial(_stiff_kernel, keep, scale, group),
        grid=(steps,),
        out_shape=jax.ShapeDtypeStruct(vectors.shape, jnp.float32),
        in_specs=[
            block_spec,
            pl.BlockSpec(single, lambda g: (jnp.maximum(g * group - 1, 0), 0, 0)),
            pl.BlockSpec(single, lambda g: (jnp.minimum(g * group + group, blocks - 1), 0, 0)),
            pl.BlockSpec(single, lambda g: (0, 0, 0)),
            pl.BlockSpec(single, lambda g: (0, 0, 0)),
            mat_spec,
            mat_spec,
            mat_spec,
        ],
        out_specs=block_spec,
    )(vectors, vectors, vectors, low, high, diag, link, after_t)


def _inverse_factor_kernel(a_in, w_out, root_out, a_ref, x_ref):
    batch, size, _ = a_in.shape
    solved = x_ref.shape[0]
    a_ref[...] = a_in[...]
    rows = lax.broadcasted_iota(jnp.int32, (size, size), 0)
    cols = lax.broadcasted_iota(jnp.int32, (size, size), 1)
    eye = jnp.where(rows == cols, 1.0, 0.0).astype(jnp.float32)
    x_ref[...] = jnp.broadcast_to(eye, x_ref.shape)
    phase = 32
    lanes = 128
    sublanes = 8

    def pick_rows(tile, tile0, k):
        sub = lax.broadcasted_iota(jnp.int32, tile.shape, 1) + tile0
        first = jnp.sum(jnp.where(sub == k, tile, 0.0), axis=1, keepdims=True)
        second = jnp.sum(jnp.where(sub == k + 1, tile, 0.0), axis=1, keepdims=True)
        return first, second

    def lane_value(row, col0, k):
        lane = lax.broadcasted_iota(jnp.int32, row.shape, 2) + col0
        return jnp.sum(jnp.where(lane == k, row, 0.0), axis=2, keepdims=True)

    for start in range(0, size, phase):
        a_col0 = (start // lanes) * lanes
        x_col1 = min(size, -(-(start + phase) // lanes) * lanes)

        def step(pair, carry, start=start, a_col0=a_col0, x_col1=x_col1):
            k = start + 2 * pair
            tile0 = pl.multiple_of((k // sublanes) * sublanes, sublanes)
            row_a0, row_a1 = pick_rows(a_ref[:, pl.ds(tile0, sublanes), a_col0:], tile0, k)
            row_x0, row_x1 = pick_rows(x_ref[:, pl.ds(tile0, sublanes), :x_col1], tile0, k)
            block0 = pl.multiple_of((k // lanes) * lanes, lanes)
            col_block = a_ref[:, start:, pl.ds(block0, lanes)]
            lane = lax.broadcasted_iota(jnp.int32, col_block.shape, 2) + block0
            col0 = jnp.sum(jnp.where(lane == k, col_block, 0.0), axis=2, keepdims=True)
            col1 = jnp.sum(jnp.where(lane == k + 1, col_block, 0.0), axis=2, keepdims=True)
            pivot0 = lane_value(row_a0, a_col0, k)
            upper01 = lane_value(row_a0, a_col0, k + 1)
            lower10 = lane_value(row_a1, a_col0, k)
            diag11 = lane_value(row_a1, a_col0, k + 1)
            ratio = lower10 / pivot0
            pivot1 = diag11 - ratio * upper01
            row_ids = lax.broadcasted_iota(jnp.int32, col0.shape, 1) + start
            mult0 = jnp.where(row_ids > k, col0 / pivot0, 0.0)
            mult1 = jnp.where(row_ids > k + 1, (col1 - mult0 * upper01) / pivot1, 0.0)
            row_a1 = row_a1 - ratio * row_a0
            row_x1 = row_x1 - ratio[batch - solved :] * row_x0
            a_ref[:, start:, a_col0:] = a_ref[:, start:, a_col0:] - mult0 * row_a0 - mult1 * row_a1
            x_ref[:, start:, :x_col1] = (
                x_ref[:, start:, :x_col1]
                - mult0[batch - solved :] * row_x0
                - mult1[batch - solved :] * row_x1
            )
            return carry

        lax.fori_loop(0, phase // 2, step, 0)
    pivots = jnp.sum(jnp.where(rows == cols, a_ref[...], 0.0), axis=2, keepdims=True)
    roots = lax.rsqrt(pivots)
    w_out[...] = x_ref[...] * roots[batch - solved :]
    root_out[...] = jnp.broadcast_to(roots, root_out.shape)


def inverse_factors(matrices, solved):
    batch, size, _ = matrices.shape
    return pl.pallas_call(
        _inverse_factor_kernel,
        out_shape=(
            jax.ShapeDtypeStruct((solved, size, size), jnp.float32),
            jax.ShapeDtypeStruct((batch, size, 128), jnp.float32),
        ),
        in_specs=[pl.BlockSpec(memory_space=pltpu.VMEM)],
        out_specs=(pl.BlockSpec(memory_space=pltpu.VMEM), pl.BlockSpec(memory_space=pltpu.VMEM)),
        scratch_shapes=[
            pltpu.VMEM(matrices.shape, jnp.float32),
            pltpu.VMEM((solved, size, size), jnp.float32),
        ],
    )(matrices)


def local(start_modes, stiff_diag, stiff_off, mass_blocks, coupling, interface_block, global_iface):
    start_flat = start_modes[0]
    stiff_self = stiff_diag[0]
    stiff_link = stiff_off[0]
    mass_self = mass_blocks[0]
    coupling_blocks = coupling[0]
    interface_ids = interface_block[0]
    global_ids = global_iface[0]
    row_count, mode_count = start_flat.shape
    blocks_dev = stiff_self.shape[0]
    block_size = stiff_self.shape[1]
    dof_count = row_count * lax.axis_size("blk")
    link_next = passed_along(stiff_link[:1], "blk", -1)
    link_after = jnp.concatenate([stiff_link[1:], link_next], 0)

    after_t = jnp.swapaxes(link_after, 1, 2)
    blk_count = lax.axis_size("blk")
    forward = [(i, i + 1) for i in range(blk_count - 1)]
    backward = [(target, source) for source, target in forward]

    def stiff_apply(vectors, keep, scale):
        low = lax.ppermute(vectors[row_count - block_size :], "blk", forward)
        high = lax.ppermute(vectors[:block_size], "blk", backward)
        result = stiff_filter(
            vectors.reshape(blocks_dev, block_size, mode_count),
            low[None],
            high[None],
            stiff_self,
            stiff_link,
            after_t,
            keep,
            scale,
        )
        return result.reshape(row_count, mode_count)

    def mass_apply(vectors):
        return block_product(
            mass_self, vectors.reshape(blocks_dev, block_size, mode_count)
        ).reshape(row_count, mode_count)

    def gram_matrix(left, right):
        return jnp.dot(left.T, right, precision=fast)

    first = stiff_apply(start_flat, 1.0, -step_size)
    second = stiff_apply(first, 1.0, -step_size)
    iface_count = global_ids.shape[0]
    block_terms = jnp.einsum(
        "bkm,bkl->bml",
        second.reshape(blocks_dev, block_size, mode_count),
        coupling_blocks,
        precision=fast,
    )
    onehot = (interface_ids[:, None] == jnp.arange(iface_count, dtype=jnp.int32)[None, :]).astype(
        jnp.float32
    )
    coupling_term = jnp.einsum("bj,bml->mjl", onehot, block_terms, precision=highest)
    second, coupling_term = lax.optimization_barrier((second, coupling_term))
    rounds = lax.axis_size("blk").bit_length() - 1
    levels = list(range(rounds))
    swapped = levels[1:2] + levels[:1] + levels[2:]
    coupling_sum = permute_sum(coupling_term, "blk", swapped)
    stiff_second = stiff_apply(second, 0.0, 1.0)
    first_gram, mass_gram, stiff_gram = permute_sum(
        jnp.stack(
            [
                gram_matrix(first, mass_apply(first)),
                gram_matrix(second, mass_apply(second)),
                gram_matrix(second, stiff_second),
            ]
        ),
        "blk",
        levels,
    )
    grams = jnp.stack([first_gram, mass_gram, stiff_gram]) / dof_count
    inverses, roots = inverse_factors(0.5 * (grams + jnp.swapaxes(grams, 1, 2)), 2)
    guard = 0.0 * jnp.sum(roots[0])
    factor_inv = inverses[0] + guard
    chain_inv = inverses[1] + guard
    basis = jnp.dot(second, factor_inv.T, precision=fast)
    reduced = (
        jnp.dot(
            jnp.dot(factor_inv, stiff_gram, precision=highest), factor_inv.T, precision=highest
        )
        / dof_count
    )
    scaled = jnp.einsum("nm,mjl->njl", chain_inv, coupling_sum, precision=highest) / dof_count**0.5
    condensed = jnp.einsum("njk,njl->jkl", scaled, scaled, precision=highest)
    global_count = GIFC * lax.axis_size("comp")
    placed = (global_ids[:, None] == jnp.arange(global_count, dtype=jnp.int32)[None, :]).astype(
        jnp.float32
    )
    dense_sum = jnp.einsum("jg,jkl->gkl", placed, condensed, precision=highest)
    comp_count = lax.axis_size("comp")
    comp_me = lax.axis_index("comp")
    owned = lax.dynamic_slice_in_dim(dense_sum, comp_me * GIFC, GIFC)
    for shift in range(1, comp_count):
        target = lax.rem(comp_me + shift, comp_count)
        outgoing = lax.dynamic_slice_in_dim(dense_sum, target * GIFC, GIFC)
        pairs = [(i, (i + shift) % comp_count) for i in range(comp_count)]
        owned = owned + lax.ppermute(outgoing, "comp", pairs)
    return (basis[None], reduced[None], owned)


def solution(mesh):
    in_specs = (
        P("comp", "blk", None),
        P("comp", "blk", None, None),
        P("comp", "blk", None, None),
        P("comp", "blk", None, None),
        P("comp", "blk", None, None),
        P("comp", "blk"),
        P("comp", None),
    )
    out_specs = (P("comp", "blk", None), P("comp", None, None), P("comp", None, None))
    return jax.shard_map(local, mesh=mesh, in_specs=in_specs, out_specs=out_specs, check_vma=False)
```

```python
import functools
import jax
import jax.numpy as jnp
from jax import lax
from jax.experimental import pallas as pl
from jax.experimental.pallas import tpu as pltpu
from jax.sharding import PartitionSpec as P

ITERS = 2
GIFC = 4


highest = lax.Precision.HIGHEST
fast = lax.Precision.HIGH
step_size = 0.15


def passed_along(value, axis, steps):
    count = lax.axis_size(axis)
    initial, last = (max(0, -steps), min(count, count - steps))
    return lax.ppermute(value, axis, [(source, source + steps) for source in range(initial, last)])


def extended_2(block, sides, width):
    for axis, dim in sides:
        count = lax.axis_size(axis)
        forward = [(i, i + 1) for i in range(count - 1)]
        backward = [(target, source) for source, target in forward]
        low = lax.ppermute(
            lax.slice_in_dim(block, block.shape[dim] - width, None, axis=dim), axis, forward
        )
        high = lax.ppermute(lax.slice_in_dim(block, 0, width, axis=dim), axis, backward)
        block = jnp.concatenate([low, block, high], axis=dim)
    return block


def permute_sum(value, axis, order):
    count = lax.axis_size(axis)
    rounds = count.bit_length() - 1
    assert count == 1 << rounds and sorted(order) == list(range(rounds))
    me = lax.axis_index(axis)
    shape = value.shape
    flat = value.reshape(-1)
    piece = flat.shape[0] >> rounds
    assert piece << rounds == flat.shape[0]
    for level in order:
        half = flat.shape[0] // 2
        upper = (me >> level) & 1
        pairs = [(i, i ^ (1 << level)) for i in range(count)]
        sent = lax.dynamic_slice_in_dim(flat, (1 - upper) * half, half)
        kept = lax.dynamic_slice_in_dim(flat, upper * half, half)
        flat = kept + lax.ppermute(sent, axis, pairs)
    for level in reversed(order):
        upper = (me >> level) & 1
        pairs = [(i, i ^ (1 << level)) for i in range(count)]
        other = lax.ppermute(flat, axis, pairs)
        flat = jnp.where(
            upper == 1, jnp.concatenate([other, flat]), jnp.concatenate([flat, other])
        )
    return flat.reshape(shape)


def block_product(blocks, vectors):
    return jnp.einsum("bij,bjm->bim", blocks, vectors, precision=fast)


def _split(value):
    high = value.astype(jnp.bfloat16)
    return high, (value - high.astype(jnp.float32)).astype(jnp.bfloat16)


def _split_dot(left, right):
    left_hi, left_lo = left
    right_hi, right_lo = right
    total = jnp.dot(left_hi, right_hi, preferred_element_type=jnp.float32)
    total = total + jnp.dot(left_lo, right_hi, preferred_element_type=jnp.float32)
    return total + jnp.dot(left_hi, right_lo, preferred_element_type=jnp.float32)


def _stiff_kernel(keep, scale, group, x_ref, prev_ref, next_ref, low_ref, high_ref,
                  diag_ref, link_ref, link_on_ref, tail_ref, out_ref):
    step = pl.program_id(0)
    last = pl.num_programs(0) - 1
    before = jnp.where(step == 0, low_ref[0], prev_ref[0])
    beyond = jnp.where(step == last, high_ref[0], next_ref[0])
    link_beyond = jnp.where(step == last, tail_ref[0], link_on_ref[0])
    parts = [_split(before)] + [_split(x_ref[j]) for j in range(group)] + [_split(beyond)]
    for j in range(group):
        after = link_ref[j + 1] if j + 1 < group else link_beyond
        acc = _split_dot(_split(diag_ref[j]), parts[j + 1])
        acc = acc + _split_dot(_split(link_ref[j]), parts[j])
        acc = acc + _split_dot(_split(after.T), parts[j + 2])
        out_ref[j] = scale * acc if keep == 0.0 else keep * x_ref[j] + scale * acc


def stiff_filter(vectors, low, high, diag, link, tail, keep, scale, group=4):
    blocks, size, modes = vectors.shape
    steps = blocks // group
    assert steps * group == blocks
    block_spec = pl.BlockSpec((group, size, modes), lambda g: (g, 0, 0))
    single = (1, size, modes)
    mat_spec = pl.BlockSpec((group, size, size), lambda g: (g, 0, 0))
    return pl.pallas_call(
        functools.partial(_stiff_kernel, keep, scale, group),
        grid=(steps,),
        out_shape=jax.ShapeDtypeStruct(vectors.shape, jnp.float32),
        in_specs=[
            block_spec,
            pl.BlockSpec(single, lambda g: (jnp.maximum(g * group - 1, 0), 0, 0)),
            pl.BlockSpec(single, lambda g: (jnp.minimum(g * group + group, blocks - 1), 0, 0)),
            pl.BlockSpec(single, lambda g: (0, 0, 0)),
            pl.BlockSpec(single, lambda g: (0, 0, 0)),
            mat_spec,
            mat_spec,
            pl.BlockSpec((1, size, size), lambda g: (jnp.minimum(g * group + group, blocks - 1), 0, 0)),
            pl.BlockSpec((1, size, size), lambda g: (0, 0, 0)),
        ],
        out_specs=block_spec,
    )(vectors, vectors, vectors, low, high, diag, link, link, tail)


def _inverse_factor_kernel(a_in, w_out, root_out, a_ref, x_ref):
    batch, size, _ = a_in.shape
    solved = x_ref.shape[0]
    a_ref[...] = a_in[...]
    rows = lax.broadcasted_iota(jnp.int32, (size, size), 0)
    cols = lax.broadcasted_iota(jnp.int32, (size, size), 1)
    eye = jnp.where(rows == cols, 1.0, 0.0).astype(jnp.float32)
    x_ref[...] = jnp.broadcast_to(eye, x_ref.shape)
    phase = 32
    lanes = 128
    sublanes = 8

    def pick_rows(tile, tile0, k):
        sub = lax.broadcasted_iota(jnp.int32, tile.shape, 1) + tile0
        first = jnp.sum(jnp.where(sub == k, tile, 0.0), axis=1, keepdims=True)
        second = jnp.sum(jnp.where(sub == k + 1, tile, 0.0), axis=1, keepdims=True)
        return first, second

    def lane_value(row, col0, k):
        lane = lax.broadcasted_iota(jnp.int32, row.shape, 2) + col0
        return jnp.sum(jnp.where(lane == k, row, 0.0), axis=2, keepdims=True)

    for start in range(0, size, phase):
        a_col0 = (start // lanes) * lanes
        x_col1 = min(size, -(-(start + phase) // lanes) * lanes)

        def step(pair, carry, start=start, a_col0=a_col0, x_col1=x_col1):
            k = start + 2 * pair
            tile0 = pl.multiple_of((k // sublanes) * sublanes, sublanes)
            row_a0, row_a1 = pick_rows(a_ref[:, pl.ds(tile0, sublanes), a_col0:], tile0, k)
            row_x0, row_x1 = pick_rows(x_ref[:, pl.ds(tile0, sublanes), :x_col1], tile0, k)
            block0 = pl.multiple_of((k // lanes) * lanes, lanes)
            col_block = a_ref[:, start:, pl.ds(block0, lanes)]
            lane = lax.broadcasted_iota(jnp.int32, col_block.shape, 2) + block0
            col0 = jnp.sum(jnp.where(lane == k, col_block, 0.0), axis=2, keepdims=True)
            col1 = jnp.sum(jnp.where(lane == k + 1, col_block, 0.0), axis=2, keepdims=True)
            pivot0 = lane_value(row_a0, a_col0, k)
            upper01 = lane_value(row_a0, a_col0, k + 1)
            lower10 = lane_value(row_a1, a_col0, k)
            diag11 = lane_value(row_a1, a_col0, k + 1)
            ratio = lower10 / pivot0
            pivot1 = diag11 - ratio * upper01
            row_ids = lax.broadcasted_iota(jnp.int32, col0.shape, 1) + start
            mult0 = jnp.where(row_ids > k, col0 / pivot0, 0.0)
            mult1 = jnp.where(row_ids > k + 1, (col1 - mult0 * upper01) / pivot1, 0.0)
            row_a1 = row_a1 - ratio * row_a0
            row_x1 = row_x1 - ratio[batch - solved :] * row_x0
            a_ref[:, start:, a_col0:] = a_ref[:, start:, a_col0:] - mult0 * row_a0 - mult1 * row_a1
            x_ref[:, start:, :x_col1] = (
                x_ref[:, start:, :x_col1]
                - mult0[batch - solved :] * row_x0
                - mult1[batch - solved :] * row_x1
            )
            return carry

        lax.fori_loop(0, phase // 2, step, 0)
    pivots = jnp.sum(jnp.where(rows == cols, a_ref[...], 0.0), axis=2, keepdims=True)
    roots = lax.rsqrt(pivots)
    w_out[...] = x_ref[...] * roots[batch - solved :]
    root_out[...] = jnp.broadcast_to(roots, root_out.shape)


def inverse_factors(matrices, solved):
    batch, size, _ = matrices.shape
    return pl.pallas_call(
        _inverse_factor_kernel,
        out_shape=(
            jax.ShapeDtypeStruct((solved, size, size), jnp.float32),
            jax.ShapeDtypeStruct((batch, size, 128), jnp.float32),
        ),
        in_specs=[pl.BlockSpec(memory_space=pltpu.VMEM)],
        out_specs=(pl.BlockSpec(memory_space=pltpu.VMEM), pl.BlockSpec(memory_space=pltpu.VMEM)),
        scratch_shapes=[
            pltpu.VMEM(matrices.shape, jnp.float32),
            pltpu.VMEM((solved, size, size), jnp.float32),
        ],
    )(matrices)


def local(start_modes, stiff_diag, stiff_off, mass_blocks, coupling, interface_block, global_iface):
    start_flat = start_modes[0]
    stiff_self = stiff_diag[0]
    stiff_link = stiff_off[0]
    mass_self = mass_blocks[0]
    coupling_blocks = coupling[0]
    interface_ids = interface_block[0]
    global_ids = global_iface[0]
    row_count, mode_count = start_flat.shape
    blocks_dev = stiff_self.shape[0]
    block_size = stiff_self.shape[1]
    dof_count = row_count * lax.axis_size("blk")
    link_next = passed_along(stiff_link[:1], "blk", -1)

    blk_count = lax.axis_size("blk")
    forward = [(i, i + 1) for i in range(blk_count - 1)]
    backward = [(target, source) for source, target in forward]

    def stiff_apply(vectors, keep, scale):
        low = lax.ppermute(vectors[row_count - block_size :], "blk", forward)
        high = lax.ppermute(vectors[:block_size], "blk", backward)
        result = stiff_filter(
            vectors.reshape(blocks_dev, block_size, mode_count),
            low[None],
            high[None],
            stiff_self,
            stiff_link,
            link_next,
            keep,
            scale,
        )
        return result.reshape(row_count, mode_count)

    def mass_apply(vectors):
        return block_product(
            mass_self, vectors.reshape(blocks_dev, block_size, mode_count)
        ).reshape(row_count, mode_count)

    def gram_matrix(left, right):
        return jnp.dot(left.T, right, precision=fast)

    first = stiff_apply(start_flat, 1.0, -step_size)
    second = stiff_apply(first, 1.0, -step_size)
    iface_count = global_ids.shape[0]
    block_terms = jnp.einsum(
        "bkm,bkl->bml",
        second.reshape(blocks_dev, block_size, mode_count),
        coupling_blocks,
        precision=fast,
    )
    onehot = (interface_ids[:, None] == jnp.arange(iface_count, dtype=jnp.int32)[None, :]).astype(
        jnp.float32
    )
    coupling_term = jnp.einsum("bj,bml->mjl", onehot, block_terms, precision=highest)
    second, coupling_term = lax.optimization_barrier((second, coupling_term))
    rounds = lax.axis_size("blk").bit_length() - 1
    levels = list(range(rounds))
    swapped = levels[1:2] + levels[:1] + levels[2:]
    coupling_sum = permute_sum(coupling_term, "blk", swapped)
    stiff_second = stiff_apply(second, 0.0, 1.0)
    first_gram, mass_gram, stiff_gram = permute_sum(
        jnp.stack(
            [
                gram_matrix(first, mass_apply(first)),
                gram_matrix(second, mass_apply(second)),
                gram_matrix(second, stiff_second),
            ]
        ),
        "blk",
        levels,
    )
    grams = jnp.stack([first_gram, mass_gram, stiff_gram]) / dof_count
    inverses, roots = inverse_factors(0.5 * (grams + jnp.swapaxes(grams, 1, 2)), 2)
    guard = 0.0 * jnp.sum(roots[0])
    factor_inv = inverses[0] + guard
    chain_inv = inverses[1] + guard
    basis = jnp.dot(second, factor_inv.T, precision=fast)
    reduced = (
        jnp.dot(
            jnp.dot(factor_inv, stiff_gram, precision=highest), factor_inv.T, precision=highest
        )
        / dof_count
    )
    scaled = jnp.einsum("nm,mjl->njl", chain_inv, coupling_sum, precision=highest) / dof_count**0.5
    condensed = jnp.einsum("njk,njl->jkl", scaled, scaled, precision=highest)
    global_count = GIFC * lax.axis_size("comp")
    placed = (global_ids[:, None] == jnp.arange(global_count, dtype=jnp.int32)[None, :]).astype(
        jnp.float32
    )
    dense_sum = jnp.einsum("jg,jkl->gkl", placed, condensed, precision=highest)
    comp_count = lax.axis_size("comp")
    comp_me = lax.axis_index("comp")
    owned = lax.dynamic_slice_in_dim(dense_sum, comp_me * GIFC, GIFC)
    for shift in range(1, comp_count):
        target = lax.rem(comp_me + shift, comp_count)
        outgoing = lax.dynamic_slice_in_dim(dense_sum, target * GIFC, GIFC)
        pairs = [(i, (i + shift) % comp_count) for i in range(comp_count)]
        owned = owned + lax.ppermute(outgoing, "comp", pairs)
    return (basis[None], reduced[None], owned)


def solution(mesh):
    in_specs = (
        P("comp", "blk", None),
        P("comp", "blk", None, None),
        P("comp", "blk", None, None),
        P("comp", "blk", None, None),
        P("comp", "blk", None, None),
        P("comp", "blk"),
        P("comp", None),
    )
    out_specs = (P("comp", "blk", None), P("comp", None, None), P("comp", None, None))
    return jax.shard_map(local, mesh=mesh, in_specs=in_specs, out_specs=out_specs, check_vma=False)
```

```python
import functools
import jax
import jax.numpy as jnp
from jax import lax
from jax.experimental import pallas as pl
from jax.experimental.pallas import tpu as pltpu
from jax.sharding import PartitionSpec as P

ITERS = 2
GIFC = 4


highest = lax.Precision.HIGHEST
fast = lax.Precision.HIGH
step_size = 0.15


def passed_along(value, axis, steps):
    count = lax.axis_size(axis)
    initial, last = (max(0, -steps), min(count, count - steps))
    return lax.ppermute(value, axis, [(source, source + steps) for source in range(initial, last)])


def extended_2(block, sides, width):
    for axis, dim in sides:
        count = lax.axis_size(axis)
        forward = [(i, i + 1) for i in range(count - 1)]
        backward = [(target, source) for source, target in forward]
        low = lax.ppermute(
            lax.slice_in_dim(block, block.shape[dim] - width, None, axis=dim), axis, forward
        )
        high = lax.ppermute(lax.slice_in_dim(block, 0, width, axis=dim), axis, backward)
        block = jnp.concatenate([low, block, high], axis=dim)
    return block


def permute_sum(value, axis, order):
    count = lax.axis_size(axis)
    rounds = count.bit_length() - 1
    assert count == 1 << rounds and sorted(order) == list(range(rounds))
    me = lax.axis_index(axis)
    shape = value.shape
    flat = value.reshape(-1)
    piece = flat.shape[0] >> rounds
    assert piece << rounds == flat.shape[0]
    for level in order:
        half = flat.shape[0] // 2
        upper = (me >> level) & 1
        pairs = [(i, i ^ (1 << level)) for i in range(count)]
        sent = lax.dynamic_slice_in_dim(flat, (1 - upper) * half, half)
        kept = lax.dynamic_slice_in_dim(flat, upper * half, half)
        flat = kept + lax.ppermute(sent, axis, pairs)
    for level in reversed(order):
        upper = (me >> level) & 1
        pairs = [(i, i ^ (1 << level)) for i in range(count)]
        other = lax.ppermute(flat, axis, pairs)
        flat = jnp.where(
            upper == 1, jnp.concatenate([other, flat]), jnp.concatenate([flat, other])
        )
    return flat.reshape(shape)


def block_product(blocks, vectors):
    return jnp.einsum("bij,bjm->bim", blocks, vectors, precision=fast)


def _split(value):
    high = value.astype(jnp.bfloat16)
    return high, (value - high.astype(jnp.float32)).astype(jnp.bfloat16)


def _split_dot(left, right):
    left_hi, left_lo = left
    right_hi, right_lo = right
    total = jnp.dot(left_hi, right_hi, preferred_element_type=jnp.float32)
    total = total + jnp.dot(left_lo, right_hi, preferred_element_type=jnp.float32)
    return total + jnp.dot(left_hi, right_lo, preferred_element_type=jnp.float32)


def _stiff_kernel(keep, scale, group, x_ref, prev_ref, next_ref, low_ref, high_ref,
                  diag_ref, link_ref, link_on_ref, tail_ref, out_ref):
    step = pl.program_id(0)
    last = pl.num_programs(0) - 1
    before = jnp.where(step == 0, low_ref[0], prev_ref[0])
    beyond = jnp.where(step == last, high_ref[0], next_ref[0])
    link_beyond = jnp.where(step == last, tail_ref[0], link_on_ref[0])
    parts = [_split(before)] + [_split(x_ref[j]) for j in range(group)] + [_split(beyond)]
    for j in range(group):
        after = link_ref[j + 1] if j + 1 < group else link_beyond
        diag_hi, diag_lo = _split(diag_ref[j])
        link_hi, link_lo = _split(link_ref[j])
        stacked_left = (
            jnp.concatenate([diag_hi, link_hi], axis=1),
            jnp.concatenate([diag_lo, link_lo], axis=1),
        )
        stacked_right = (
            jnp.concatenate([parts[j + 1][0], parts[j][0]], axis=0),
            jnp.concatenate([parts[j + 1][1], parts[j][1]], axis=0),
        )
        acc = _split_dot(stacked_left, stacked_right)
        acc = acc + _split_dot(_split(after.T), parts[j + 2])
        out_ref[j] = scale * acc if keep == 0.0 else keep * x_ref[j] + scale * acc


def stiff_filter(vectors, low, high, diag, link, tail, keep, scale, group=4):
    blocks, size, modes = vectors.shape
    steps = blocks // group
    assert steps * group == blocks
    block_spec = pl.BlockSpec((group, size, modes), lambda g: (g, 0, 0))
    single = (1, size, modes)
    mat_spec = pl.BlockSpec((group, size, size), lambda g: (g, 0, 0))
    return pl.pallas_call(
        functools.partial(_stiff_kernel, keep, scale, group),
        grid=(steps,),
        out_shape=jax.ShapeDtypeStruct(vectors.shape, jnp.float32),
        in_specs=[
            block_spec,
            pl.BlockSpec(single, lambda g: (jnp.maximum(g * group - 1, 0), 0, 0)),
            pl.BlockSpec(single, lambda g: (jnp.minimum(g * group + group, blocks - 1), 0, 0)),
            pl.BlockSpec(single, lambda g: (0, 0, 0)),
            pl.BlockSpec(single, lambda g: (0, 0, 0)),
            mat_spec,
            mat_spec,
            pl.BlockSpec((1, size, size), lambda g: (jnp.minimum(g * group + group, blocks - 1), 0, 0)),
            pl.BlockSpec((1, size, size), lambda g: (0, 0, 0)),
        ],
        out_specs=block_spec,
    )(vectors, vectors, vectors, low, high, diag, link, link, tail)


def _inverse_factor_kernel(a_in, w_out, root_out, a_ref, x_ref):
    batch, size, _ = a_in.shape
    solved = x_ref.shape[0]
    a_ref[...] = a_in[...]
    rows = lax.broadcasted_iota(jnp.int32, (size, size), 0)
    cols = lax.broadcasted_iota(jnp.int32, (size, size), 1)
    eye = jnp.where(rows == cols, 1.0, 0.0).astype(jnp.float32)
    x_ref[...] = jnp.broadcast_to(eye, x_ref.shape)
    phase = 32
    lanes = 128
    sublanes = 8

    def pick_rows(tile, tile0, k):
        sub = lax.broadcasted_iota(jnp.int32, tile.shape, 1) + tile0
        first = jnp.sum(jnp.where(sub == k, tile, 0.0), axis=1, keepdims=True)
        second = jnp.sum(jnp.where(sub == k + 1, tile, 0.0), axis=1, keepdims=True)
        return first, second

    def lane_value(row, col0, k):
        lane = lax.broadcasted_iota(jnp.int32, row.shape, 2) + col0
        return jnp.sum(jnp.where(lane == k, row, 0.0), axis=2, keepdims=True)

    for start in range(0, size, phase):
        a_col0 = (start // lanes) * lanes
        x_col1 = min(size, -(-(start + phase) // lanes) * lanes)

        def step(pair, carry, start=start, a_col0=a_col0, x_col1=x_col1):
            k = start + 2 * pair
            tile0 = pl.multiple_of((k // sublanes) * sublanes, sublanes)
            row_a0, row_a1 = pick_rows(a_ref[:, pl.ds(tile0, sublanes), a_col0:], tile0, k)
            row_x0, row_x1 = pick_rows(x_ref[:, pl.ds(tile0, sublanes), :x_col1], tile0, k)
            block0 = pl.multiple_of((k // lanes) * lanes, lanes)
            col_block = a_ref[:, start:, pl.ds(block0, lanes)]
            lane = lax.broadcasted_iota(jnp.int32, col_block.shape, 2) + block0
            col0 = jnp.sum(jnp.where(lane == k, col_block, 0.0), axis=2, keepdims=True)
            col1 = jnp.sum(jnp.where(lane == k + 1, col_block, 0.0), axis=2, keepdims=True)
            pivot0 = lane_value(row_a0, a_col0, k)
            upper01 = lane_value(row_a0, a_col0, k + 1)
            lower10 = lane_value(row_a1, a_col0, k)
            diag11 = lane_value(row_a1, a_col0, k + 1)
            ratio = lower10 / pivot0
            pivot1 = diag11 - ratio * upper01
            row_ids = lax.broadcasted_iota(jnp.int32, col0.shape, 1) + start
            mult0 = jnp.where(row_ids > k, col0 / pivot0, 0.0)
            mult1 = jnp.where(row_ids > k + 1, (col1 - mult0 * upper01) / pivot1, 0.0)
            row_a1 = row_a1 - ratio * row_a0
            row_x1 = row_x1 - ratio[batch - solved :] * row_x0
            a_ref[:, start:, a_col0:] = a_ref[:, start:, a_col0:] - mult0 * row_a0 - mult1 * row_a1
            x_ref[:, start:, :x_col1] = (
                x_ref[:, start:, :x_col1]
                - mult0[batch - solved :] * row_x0
                - mult1[batch - solved :] * row_x1
            )
            return carry

        lax.fori_loop(0, phase // 2, step, 0)
    pivots = jnp.sum(jnp.where(rows == cols, a_ref[...], 0.0), axis=2, keepdims=True)
    roots = lax.rsqrt(pivots)
    w_out[...] = x_ref[...] * roots[batch - solved :]
    root_out[...] = jnp.broadcast_to(roots, root_out.shape)


def inverse_factors(matrices, solved):
    batch, size, _ = matrices.shape
    return pl.pallas_call(
        _inverse_factor_kernel,
        out_shape=(
            jax.ShapeDtypeStruct((solved, size, size), jnp.float32),
            jax.ShapeDtypeStruct((batch, size, 128), jnp.float32),
        ),
        in_specs=[pl.BlockSpec(memory_space=pltpu.VMEM)],
        out_specs=(pl.BlockSpec(memory_space=pltpu.VMEM), pl.BlockSpec(memory_space=pltpu.VMEM)),
        scratch_shapes=[
            pltpu.VMEM(matrices.shape, jnp.float32),
            pltpu.VMEM((solved, size, size), jnp.float32),
        ],
    )(matrices)


def local(start_modes, stiff_diag, stiff_off, mass_blocks, coupling, interface_block, global_iface):
    start_flat = start_modes[0]
    stiff_self = stiff_diag[0]
    stiff_link = stiff_off[0]
    mass_self = mass_blocks[0]
    coupling_blocks = coupling[0]
    interface_ids = interface_block[0]
    global_ids = global_iface[0]
    row_count, mode_count = start_flat.shape
    blocks_dev = stiff_self.shape[0]
    block_size = stiff_self.shape[1]
    dof_count = row_count * lax.axis_size("blk")
    link_next = passed_along(stiff_link[:1], "blk", -1)

    blk_count = lax.axis_size("blk")
    forward = [(i, i + 1) for i in range(blk_count - 1)]
    backward = [(target, source) for source, target in forward]

    def stiff_apply(vectors, keep, scale):
        low = lax.ppermute(vectors[row_count - block_size :], "blk", forward)
        high = lax.ppermute(vectors[:block_size], "blk", backward)
        result = stiff_filter(
            vectors.reshape(blocks_dev, block_size, mode_count),
            low[None],
            high[None],
            stiff_self,
            stiff_link,
            link_next,
            keep,
            scale,
        )
        return result.reshape(row_count, mode_count)

    def mass_apply(vectors):
        return block_product(
            mass_self, vectors.reshape(blocks_dev, block_size, mode_count)
        ).reshape(row_count, mode_count)

    def gram_matrix(left, right):
        return jnp.dot(left.T, right, precision=fast)

    first = stiff_apply(start_flat, 1.0, -step_size)
    second = stiff_apply(first, 1.0, -step_size)
    iface_count = global_ids.shape[0]
    block_terms = jnp.einsum(
        "bkm,bkl->bml",
        second.reshape(blocks_dev, block_size, mode_count),
        coupling_blocks,
        precision=fast,
    )
    onehot = (interface_ids[:, None] == jnp.arange(iface_count, dtype=jnp.int32)[None, :]).astype(
        jnp.float32
    )
    coupling_term = jnp.einsum("bj,bml->mjl", onehot, block_terms, precision=highest)
    second, coupling_term = lax.optimization_barrier((second, coupling_term))
    rounds = lax.axis_size("blk").bit_length() - 1
    levels = list(range(rounds))
    swapped = levels[1:2] + levels[:1] + levels[2:]
    coupling_sum = permute_sum(coupling_term, "blk", swapped)
    stiff_second = stiff_apply(second, 0.0, 1.0)
    first_gram, mass_gram, stiff_gram = permute_sum(
        jnp.stack(
            [
                gram_matrix(first, mass_apply(first)),
                gram_matrix(second, mass_apply(second)),
                gram_matrix(second, stiff_second),
            ]
        ),
        "blk",
        levels,
    )
    grams = jnp.stack([first_gram, mass_gram, stiff_gram]) / dof_count
    inverses, roots = inverse_factors(0.5 * (grams + jnp.swapaxes(grams, 1, 2)), 2)
    guard = 0.0 * jnp.sum(roots[0])
    factor_inv = inverses[0] + guard
    chain_inv = inverses[1] + guard
    basis = jnp.dot(second, factor_inv.T, precision=fast)
    reduced = (
        jnp.dot(
            jnp.dot(factor_inv, stiff_gram, precision=highest), factor_inv.T, precision=highest
        )
        / dof_count
    )
    scaled = jnp.einsum("nm,mjl->njl", chain_inv, coupling_sum, precision=highest) / dof_count**0.5
    condensed = jnp.einsum("njk,njl->jkl", scaled, scaled, precision=highest)
    global_count = GIFC * lax.axis_size("comp")
    placed = (global_ids[:, None] == jnp.arange(global_count, dtype=jnp.int32)[None, :]).astype(
        jnp.float32
    )
    dense_sum = jnp.einsum("jg,jkl->gkl", placed, condensed, precision=highest)
    comp_count = lax.axis_size("comp")
    comp_me = lax.axis_index("comp")
    owned = lax.dynamic_slice_in_dim(dense_sum, comp_me * GIFC, GIFC)
    for shift in range(1, comp_count):
        target = lax.rem(comp_me + shift, comp_count)
        outgoing = lax.dynamic_slice_in_dim(dense_sum, target * GIFC, GIFC)
        pairs = [(i, (i + shift) % comp_count) for i in range(comp_count)]
        owned = owned + lax.ppermute(outgoing, "comp", pairs)
    return (basis[None], reduced[None], owned)


def solution(mesh):
    in_specs = (
        P("comp", "blk", None),
        P("comp", "blk", None, None),
        P("comp", "blk", None, None),
        P("comp", "blk", None, None),
        P("comp", "blk", None, None),
        P("comp", "blk"),
        P("comp", None),
    )
    out_specs = (P("comp", "blk", None), P("comp", None, None), P("comp", None, None))
    return jax.shard_map(local, mesh=mesh, in_specs=in_specs, out_specs=out_specs, check_vma=False)
```

```python
import functools
import jax
import jax.numpy as jnp
from jax import lax
from jax.experimental import pallas as pl
from jax.experimental.pallas import tpu as pltpu
from jax.sharding import PartitionSpec as P

ITERS = 2
GIFC = 4


highest = lax.Precision.HIGHEST
fast = lax.Precision.HIGH
step_size = 0.15


def passed_along(value, axis, steps):
    count = lax.axis_size(axis)
    initial, last = (max(0, -steps), min(count, count - steps))
    return lax.ppermute(value, axis, [(source, source + steps) for source in range(initial, last)])


def extended_2(block, sides, width):
    for axis, dim in sides:
        count = lax.axis_size(axis)
        forward = [(i, i + 1) for i in range(count - 1)]
        backward = [(target, source) for source, target in forward]
        low = lax.ppermute(
            lax.slice_in_dim(block, block.shape[dim] - width, None, axis=dim), axis, forward
        )
        high = lax.ppermute(lax.slice_in_dim(block, 0, width, axis=dim), axis, backward)
        block = jnp.concatenate([low, block, high], axis=dim)
    return block


def halving_step(flat, axis, level):
    count = lax.axis_size(axis)
    half = flat.shape[0] // 2
    upper = (lax.axis_index(axis) >> level) & 1
    pairs = [(i, i ^ (1 << level)) for i in range(count)]
    sent = lax.dynamic_slice_in_dim(flat, (1 - upper) * half, half)
    kept = lax.dynamic_slice_in_dim(flat, upper * half, half)
    return kept + lax.ppermute(sent, axis, pairs)


def doubling_step(flat, axis, level):
    count = lax.axis_size(axis)
    upper = (lax.axis_index(axis) >> level) & 1
    pairs = [(i, i ^ (1 << level)) for i in range(count)]
    other = lax.ppermute(flat, axis, pairs)
    return jnp.where(upper == 1, jnp.concatenate([other, flat]), jnp.concatenate([flat, other]))


def permute_sum(value, axis, order, done=0):
    count = lax.axis_size(axis)
    rounds = count.bit_length() - 1
    assert count == 1 << rounds and sorted(order) == list(range(rounds))
    flat = value.reshape(-1)
    assert (flat.shape[0] >> (rounds - done)) << (rounds - done) == flat.shape[0]
    for level in order[done:]:
        flat = halving_step(flat, axis, level)
    for level in reversed(order):
        flat = doubling_step(flat, axis, level)
    return flat


def block_product(blocks, vectors):
    return jnp.einsum("bij,bjm->bim", blocks, vectors, precision=fast)


def _split(value):
    high = value.astype(jnp.bfloat16)
    return high, (value - high.astype(jnp.float32)).astype(jnp.bfloat16)


def _split_dot(left, right):
    left_hi, left_lo = left
    right_hi, right_lo = right
    total = jnp.dot(left_hi, right_hi, preferred_element_type=jnp.float32)
    total = total + jnp.dot(left_lo, right_hi, preferred_element_type=jnp.float32)
    return total + jnp.dot(left_hi, right_lo, preferred_element_type=jnp.float32)


def _stiff_kernel(keep, scale, group, x_ref, prev_ref, next_ref, low_ref, high_ref,
                  diag_ref, link_ref, link_on_ref, tail_ref, out_ref):
    step = pl.program_id(0)
    last = pl.num_programs(0) - 1
    before = jnp.where(step == 0, low_ref[0], prev_ref[0])
    beyond = jnp.where(step == last, high_ref[0], next_ref[0])
    link_beyond = jnp.where(step == last, tail_ref[0], link_on_ref[0])
    parts = [_split(before)] + [_split(x_ref[j]) for j in range(group)] + [_split(beyond)]
    for j in range(group):
        after = link_ref[j + 1] if j + 1 < group else link_beyond
        diag_hi, diag_lo = _split(diag_ref[j])
        link_hi, link_lo = _split(link_ref[j])
        stacked_left = (
            jnp.concatenate([diag_hi, link_hi], axis=1),
            jnp.concatenate([diag_lo, link_lo], axis=1),
        )
        stacked_right = (
            jnp.concatenate([parts[j + 1][0], parts[j][0]], axis=0),
            jnp.concatenate([parts[j + 1][1], parts[j][1]], axis=0),
        )
        acc = _split_dot(stacked_left, stacked_right)
        acc = acc + _split_dot(_split(after.T), parts[j + 2])
        out_ref[j] = scale * acc if keep == 0.0 else keep * x_ref[j] + scale * acc


def stiff_filter(vectors, low, high, diag, link, tail, keep, scale, group=4):
    blocks, size, modes = vectors.shape
    steps = blocks // group
    assert steps * group == blocks
    block_spec = pl.BlockSpec((group, size, modes), lambda g: (g, 0, 0))
    single = (1, size, modes)
    mat_spec = pl.BlockSpec((group, size, size), lambda g: (g, 0, 0))
    return pl.pallas_call(
        functools.partial(_stiff_kernel, keep, scale, group),
        grid=(steps,),
        out_shape=jax.ShapeDtypeStruct(vectors.shape, jnp.float32),
        in_specs=[
            block_spec,
            pl.BlockSpec(single, lambda g: (jnp.maximum(g * group - 1, 0), 0, 0)),
            pl.BlockSpec(single, lambda g: (jnp.minimum(g * group + group, blocks - 1), 0, 0)),
            pl.BlockSpec(single, lambda g: (0, 0, 0)),
            pl.BlockSpec(single, lambda g: (0, 0, 0)),
            mat_spec,
            mat_spec,
            pl.BlockSpec((1, size, size), lambda g: (jnp.minimum(g * group + group, blocks - 1), 0, 0)),
            pl.BlockSpec((1, size, size), lambda g: (0, 0, 0)),
        ],
        out_specs=block_spec,
    )(vectors, vectors, vectors, low, high, diag, link, link, tail)


def _inverse_factor_kernel(a_in, w_out, root_out, a_ref, x_ref):
    batch, size, _ = a_in.shape
    solved = x_ref.shape[0]
    a_ref[...] = a_in[...]
    rows = lax.broadcasted_iota(jnp.int32, (size, size), 0)
    cols = lax.broadcasted_iota(jnp.int32, (size, size), 1)
    eye = jnp.where(rows == cols, 1.0, 0.0).astype(jnp.float32)
    x_ref[...] = jnp.broadcast_to(eye, x_ref.shape)
    phase = 32
    lanes = 128
    sublanes = 8

    def pick_rows(tile, tile0, k):
        sub = lax.broadcasted_iota(jnp.int32, tile.shape, 1) + tile0
        first = jnp.sum(jnp.where(sub == k, tile, 0.0), axis=1, keepdims=True)
        second = jnp.sum(jnp.where(sub == k + 1, tile, 0.0), axis=1, keepdims=True)
        return first, second

    def lane_value(row, col0, k):
        lane = lax.broadcasted_iota(jnp.int32, row.shape, 2) + col0
        return jnp.sum(jnp.where(lane == k, row, 0.0), axis=2, keepdims=True)

    for start in range(0, size, phase):
        a_col0 = (start // lanes) * lanes
        x_col1 = min(size, -(-(start + phase) // lanes) * lanes)

        def step(pair, carry, start=start, a_col0=a_col0, x_col1=x_col1):
            k = start + 2 * pair
            tile0 = pl.multiple_of((k // sublanes) * sublanes, sublanes)
            row_a0, row_a1 = pick_rows(a_ref[:, pl.ds(tile0, sublanes), a_col0:], tile0, k)
            row_x0, row_x1 = pick_rows(x_ref[:, pl.ds(tile0, sublanes), :x_col1], tile0, k)
            block0 = pl.multiple_of((k // lanes) * lanes, lanes)
            col_block = a_ref[:, start:, pl.ds(block0, lanes)]
            lane = lax.broadcasted_iota(jnp.int32, col_block.shape, 2) + block0
            col0 = jnp.sum(jnp.where(lane == k, col_block, 0.0), axis=2, keepdims=True)
            col1 = jnp.sum(jnp.where(lane == k + 1, col_block, 0.0), axis=2, keepdims=True)
            pivot0 = lane_value(row_a0, a_col0, k)
            upper01 = lane_value(row_a0, a_col0, k + 1)
            lower10 = lane_value(row_a1, a_col0, k)
            diag11 = lane_value(row_a1, a_col0, k + 1)
            ratio = lower10 / pivot0
            pivot1 = diag11 - ratio * upper01
            row_ids = lax.broadcasted_iota(jnp.int32, col0.shape, 1) + start
            mult0 = jnp.where(row_ids > k, col0 / pivot0, 0.0)
            mult1 = jnp.where(row_ids > k + 1, (col1 - mult0 * upper01) / pivot1, 0.0)
            row_a1 = row_a1 - ratio * row_a0
            row_x1 = row_x1 - ratio[batch - solved :] * row_x0
            a_ref[:, start:, a_col0:] = a_ref[:, start:, a_col0:] - mult0 * row_a0 - mult1 * row_a1
            x_ref[:, start:, :x_col1] = (
                x_ref[:, start:, :x_col1]
                - mult0[batch - solved :] * row_x0
                - mult1[batch - solved :] * row_x1
            )
            return carry

        lax.fori_loop(0, phase // 2, step, 0)
    pivots = jnp.sum(jnp.where(rows == cols, a_ref[...], 0.0), axis=2, keepdims=True)
    roots = lax.rsqrt(pivots)
    w_out[...] = x_ref[...] * roots[batch - solved :]
    root_out[...] = jnp.broadcast_to(roots, root_out.shape)


def inverse_factors(matrices, solved):
    batch, size, _ = matrices.shape
    return pl.pallas_call(
        _inverse_factor_kernel,
        out_shape=(
            jax.ShapeDtypeStruct((solved, size, size), jnp.float32),
            jax.ShapeDtypeStruct((batch, size, 128), jnp.float32),
        ),
        in_specs=[pl.BlockSpec(memory_space=pltpu.VMEM)],
        out_specs=(pl.BlockSpec(memory_space=pltpu.VMEM), pl.BlockSpec(memory_space=pltpu.VMEM)),
        scratch_shapes=[
            pltpu.VMEM(matrices.shape, jnp.float32),
            pltpu.VMEM((solved, size, size), jnp.float32),
        ],
    )(matrices)


def local(start_modes, stiff_diag, stiff_off, mass_blocks, coupling, interface_block, global_iface):
    start_flat = start_modes[0]
    stiff_self = stiff_diag[0]
    stiff_link = stiff_off[0]
    mass_self = mass_blocks[0]
    coupling_blocks = coupling[0]
    interface_ids = interface_block[0]
    global_ids = global_iface[0]
    row_count, mode_count = start_flat.shape
    blocks_dev = stiff_self.shape[0]
    block_size = stiff_self.shape[1]
    dof_count = row_count * lax.axis_size("blk")
    link_next = passed_along(stiff_link[:1], "blk", -1)

    blk_count = lax.axis_size("blk")
    forward = [(i, i + 1) for i in range(blk_count - 1)]
    backward = [(target, source) for source, target in forward]

    def stiff_apply(vectors, keep, scale):
        low = lax.ppermute(vectors[row_count - block_size :], "blk", forward)
        high = lax.ppermute(vectors[:block_size], "blk", backward)
        result = stiff_filter(
            vectors.reshape(blocks_dev, block_size, mode_count),
            low[None],
            high[None],
            stiff_self,
            stiff_link,
            link_next,
            keep,
            scale,
        )
        return result.reshape(row_count, mode_count)

    def mass_apply(vectors):
        return block_product(
            mass_self, vectors.reshape(blocks_dev, block_size, mode_count)
        ).reshape(row_count, mode_count)

    def gram_matrix(left, right):
        return jnp.dot(left.T, right, precision=fast)

    first = stiff_apply(start_flat, 1.0, -step_size)
    second = stiff_apply(first, 1.0, -step_size)
    iface_count = global_ids.shape[0]
    block_terms = jnp.einsum(
        "bkm,bkl->bml",
        second.reshape(blocks_dev, block_size, mode_count),
        coupling_blocks,
        precision=fast,
    )
    onehot = (interface_ids[:, None] == jnp.arange(iface_count, dtype=jnp.int32)[None, :]).astype(
        jnp.float32
    )
    coupling_term = jnp.einsum("bj,bml->mjl", onehot, block_terms, precision=highest)
    second, coupling_term = lax.optimization_barrier((second, coupling_term))
    rounds = lax.axis_size("blk").bit_length() - 1
    levels = list(range(rounds))
    swapped = levels[1:2] + levels[:1] + levels[2:]
    coupling_flat = halving_step(coupling_term.reshape(-1), "blk", swapped[0])
    second, coupling_flat = lax.optimization_barrier((second, coupling_flat))
    stiff_second = stiff_apply(second, 0.0, 1.0)
    early = min(2, rounds)
    if early > 1:
        coupling_flat = halving_step(coupling_flat, "blk", swapped[1])
    stiff_second, coupling_flat = lax.optimization_barrier((stiff_second, coupling_flat))
    coupling_sum = permute_sum(coupling_flat, "blk", swapped, early).reshape(coupling_term.shape)
    first_gram, mass_gram, stiff_gram = permute_sum(
        jnp.stack(
            [
                gram_matrix(first, mass_apply(first)),
                gram_matrix(second, mass_apply(second)),
                gram_matrix(second, stiff_second),
            ]
        ),
        "blk",
        levels,
    ).reshape(3, mode_count, mode_count)
    grams = jnp.stack([first_gram, mass_gram, stiff_gram]) / dof_count
    inverses, roots = inverse_factors(0.5 * (grams + jnp.swapaxes(grams, 1, 2)), 2)
    guard = 0.0 * jnp.sum(roots[0])
    factor_inv = inverses[0] + guard
    chain_inv = inverses[1] + guard
    basis = jnp.dot(second, factor_inv.T, precision=fast)
    reduced = (
        jnp.dot(
            jnp.dot(factor_inv, stiff_gram, precision=highest), factor_inv.T, precision=highest
        )
        / dof_count
    )
    scaled = jnp.einsum("nm,mjl->njl", chain_inv, coupling_sum, precision=highest) / dof_count**0.5
    condensed = jnp.einsum("njk,njl->jkl", scaled, scaled, precision=highest)
    global_count = GIFC * lax.axis_size("comp")
    placed = (global_ids[:, None] == jnp.arange(global_count, dtype=jnp.int32)[None, :]).astype(
        jnp.float32
    )
    dense_sum = jnp.einsum("jg,jkl->gkl", placed, condensed, precision=highest)
    comp_count = lax.axis_size("comp")
    comp_me = lax.axis_index("comp")
    owned = lax.dynamic_slice_in_dim(dense_sum, comp_me * GIFC, GIFC)
    for shift in range(1, comp_count):
        target = lax.rem(comp_me + shift, comp_count)
        outgoing = lax.dynamic_slice_in_dim(dense_sum, target * GIFC, GIFC)
        pairs = [(i, (i + shift) % comp_count) for i in range(comp_count)]
        owned = owned + lax.ppermute(outgoing, "comp", pairs)
    return (basis[None], reduced[None], owned)


def solution(mesh):
    in_specs = (
        P("comp", "blk", None),
        P("comp", "blk", None, None),
        P("comp", "blk", None, None),
        P("comp", "blk", None, None),
        P("comp", "blk", None, None),
        P("comp", "blk"),
        P("comp", None),
    )
    out_specs = (P("comp", "blk", None), P("comp", None, None), P("comp", None, None))
    return jax.shard_map(local, mesh=mesh, in_specs=in_specs, out_specs=out_specs, check_vma=False)
```

```python
import functools
import jax
import jax.numpy as jnp
from jax import lax
from jax.experimental import pallas as pl
from jax.experimental.pallas import tpu as pltpu
from jax.sharding import PartitionSpec as P

ITERS = 2
GIFC = 4


highest = lax.Precision.HIGHEST
fast = lax.Precision.HIGH
step_size = 0.15


def passed_along(value, axis, steps):
    count = lax.axis_size(axis)
    initial, last = (max(0, -steps), min(count, count - steps))
    return lax.ppermute(value, axis, [(source, source + steps) for source in range(initial, last)])


def extended_2(block, sides, width):
    for axis, dim in sides:
        count = lax.axis_size(axis)
        forward = [(i, i + 1) for i in range(count - 1)]
        backward = [(target, source) for source, target in forward]
        low = lax.ppermute(
            lax.slice_in_dim(block, block.shape[dim] - width, None, axis=dim), axis, forward
        )
        high = lax.ppermute(lax.slice_in_dim(block, 0, width, axis=dim), axis, backward)
        block = jnp.concatenate([low, block, high], axis=dim)
    return block


def permute_sum(value, axis, order):
    count = lax.axis_size(axis)
    rounds = count.bit_length() - 1
    assert count == 1 << rounds and sorted(order) == list(range(rounds))
    me = lax.axis_index(axis)
    shape = value.shape
    flat = value.reshape(-1)
    piece = flat.shape[0] >> rounds
    assert piece << rounds == flat.shape[0]
    for level in order:
        half = flat.shape[0] // 2
        upper = (me >> level) & 1
        pairs = [(i, i ^ (1 << level)) for i in range(count)]
        sent = lax.dynamic_slice_in_dim(flat, (1 - upper) * half, half)
        kept = lax.dynamic_slice_in_dim(flat, upper * half, half)
        flat = kept + lax.ppermute(sent, axis, pairs)
    for level in reversed(order):
        upper = (me >> level) & 1
        pairs = [(i, i ^ (1 << level)) for i in range(count)]
        other = lax.ppermute(flat, axis, pairs)
        flat = jnp.where(
            upper == 1, jnp.concatenate([other, flat]), jnp.concatenate([flat, other])
        )
    return flat.reshape(shape)


def block_product(blocks, vectors):
    return jnp.einsum("bij,bjm->bim", blocks, vectors, precision=fast)


def _split(value):
    high = value.astype(jnp.bfloat16)
    return high, (value - high.astype(jnp.float32)).astype(jnp.bfloat16)


def _split_dot(left, right):
    left_hi, left_lo = left
    right_hi, right_lo = right
    total = jnp.dot(left_hi, right_hi, preferred_element_type=jnp.float32)
    total = total + jnp.dot(left_lo, right_hi, preferred_element_type=jnp.float32)
    return total + jnp.dot(left_hi, right_lo, preferred_element_type=jnp.float32)


def _stiff_kernel(keep, scale, group, x_ref, prev_ref, next_ref, low_ref, high_ref,
                  diag_ref, link_ref, link_on_ref, tail_ref, out_ref):
    step = pl.program_id(0)
    last = pl.num_programs(0) - 1
    before = jnp.where(step == 0, low_ref[0], prev_ref[0])
    beyond = jnp.where(step == last, high_ref[0], next_ref[0])
    link_beyond = jnp.where(step == last, tail_ref[0], link_on_ref[0])
    parts = [_split(before)] + [_split(x_ref[j]) for j in range(group)] + [_split(beyond)]
    for j in range(group):
        after = link_ref[j + 1] if j + 1 < group else link_beyond
        diag_hi, diag_lo = _split(diag_ref[j])
        link_hi, link_lo = _split(link_ref[j])
        stacked_left = (
            jnp.concatenate([diag_hi, link_hi], axis=1),
            jnp.concatenate([diag_lo, link_lo], axis=1),
        )
        stacked_right = (
            jnp.concatenate([parts[j + 1][0], parts[j][0]], axis=0),
            jnp.concatenate([parts[j + 1][1], parts[j][1]], axis=0),
        )
        acc = _split_dot(stacked_left, stacked_right)
        acc = acc + _split_dot(_split(after.T), parts[j + 2])
        out_ref[j] = scale * acc if keep == 0.0 else keep * x_ref[j] + scale * acc


def stiff_filter(vectors, low, high, diag, link, tail, keep, scale, group=4):
    blocks, size, modes = vectors.shape
    steps = blocks // group
    assert steps * group == blocks
    block_spec = pl.BlockSpec((group, size, modes), lambda g: (g, 0, 0))
    single = (1, size, modes)
    mat_spec = pl.BlockSpec((group, size, size), lambda g: (g, 0, 0))
    return pl.pallas_call(
        functools.partial(_stiff_kernel, keep, scale, group),
        grid=(steps,),
        out_shape=jax.ShapeDtypeStruct(vectors.shape, jnp.float32),
        in_specs=[
            block_spec,
            pl.BlockSpec(single, lambda g: (jnp.maximum(g * group - 1, 0), 0, 0)),
            pl.BlockSpec(single, lambda g: (jnp.minimum(g * group + group, blocks - 1), 0, 0)),
            pl.BlockSpec(single, lambda g: (0, 0, 0)),
            pl.BlockSpec(single, lambda g: (0, 0, 0)),
            mat_spec,
            mat_spec,
            pl.BlockSpec((1, size, size), lambda g: (jnp.minimum(g * group + group, blocks - 1), 0, 0)),
            pl.BlockSpec((1, size, size), lambda g: (0, 0, 0)),
        ],
        out_specs=block_spec,
    )(vectors, vectors, vectors, low, high, diag, link, link, tail)


def _inverse_factor_kernel(a_in, w_out, root_out, a_ref, x_ref):
    batch, size, _ = a_in.shape
    solved = x_ref.shape[0]
    a_ref[...] = a_in[...]
    rows = lax.broadcasted_iota(jnp.int32, (size, size), 0)
    cols = lax.broadcasted_iota(jnp.int32, (size, size), 1)
    eye = jnp.where(rows == cols, 1.0, 0.0).astype(jnp.float32)
    x_ref[...] = jnp.broadcast_to(eye, x_ref.shape)
    phase = 32
    lanes = 128
    sublanes = 8

    def pick_rows(tile, tile0, k):
        sub = lax.broadcasted_iota(jnp.int32, tile.shape, 1) + tile0
        first = jnp.sum(jnp.where(sub == k, tile, 0.0), axis=1, keepdims=True)
        second = jnp.sum(jnp.where(sub == k + 1, tile, 0.0), axis=1, keepdims=True)
        return first, second

    def lane_value(row, col0, k):
        lane = lax.broadcasted_iota(jnp.int32, row.shape, 2) + col0
        return jnp.sum(jnp.where(lane == k, row, 0.0), axis=2, keepdims=True)

    for start in range(0, size, phase):
        a_col0 = (start // lanes) * lanes
        x_col1 = min(size, -(-(start + phase) // lanes) * lanes)

        def step(pair, carry, start=start, a_col0=a_col0, x_col1=x_col1):
            k = start + 2 * pair
            tile0 = pl.multiple_of((k // sublanes) * sublanes, sublanes)
            row_a0, row_a1 = pick_rows(a_ref[:, pl.ds(tile0, sublanes), a_col0:], tile0, k)
            row_x0, row_x1 = pick_rows(x_ref[:, pl.ds(tile0, sublanes), :x_col1], tile0, k)
            block0 = pl.multiple_of((k // lanes) * lanes, lanes)
            col_block = a_ref[:, start:, pl.ds(block0, lanes)]
            lane = lax.broadcasted_iota(jnp.int32, col_block.shape, 2) + block0
            col0 = jnp.sum(jnp.where(lane == k, col_block, 0.0), axis=2, keepdims=True)
            col1 = jnp.sum(jnp.where(lane == k + 1, col_block, 0.0), axis=2, keepdims=True)
            pivot0 = lane_value(row_a0, a_col0, k)
            upper01 = lane_value(row_a0, a_col0, k + 1)
            lower10 = lane_value(row_a1, a_col0, k)
            diag11 = lane_value(row_a1, a_col0, k + 1)
            ratio = lower10 / pivot0
            pivot1 = diag11 - ratio * upper01
            row_ids = lax.broadcasted_iota(jnp.int32, col0.shape, 1) + start
            mult0 = jnp.where(row_ids > k, col0 / pivot0, 0.0)
            mult1 = jnp.where(row_ids > k + 1, (col1 - mult0 * upper01) / pivot1, 0.0)
            row_a1 = row_a1 - ratio * row_a0
            row_x1 = row_x1 - ratio[batch - solved :] * row_x0
            a_ref[:, start:, a_col0:] = a_ref[:, start:, a_col0:] - mult0 * row_a0 - mult1 * row_a1
            x_ref[:, start:, :x_col1] = (
                x_ref[:, start:, :x_col1]
                - mult0[batch - solved :] * row_x0
                - mult1[batch - solved :] * row_x1
            )
            return carry

        lax.fori_loop(0, phase // 2, step, 0)
    pivots = jnp.sum(jnp.where(rows == cols, a_ref[...], 0.0), axis=2, keepdims=True)
    roots = lax.rsqrt(pivots)
    w_out[...] = x_ref[...] * roots[batch - solved :]
    root_out[...] = jnp.broadcast_to(roots, root_out.shape)


def inverse_factors(matrices, solved):
    batch, size, _ = matrices.shape
    return pl.pallas_call(
        _inverse_factor_kernel,
        out_shape=(
            jax.ShapeDtypeStruct((solved, size, size), jnp.float32),
            jax.ShapeDtypeStruct((batch, size, 128), jnp.float32),
        ),
        in_specs=[pl.BlockSpec(memory_space=pltpu.VMEM)],
        out_specs=(pl.BlockSpec(memory_space=pltpu.VMEM), pl.BlockSpec(memory_space=pltpu.VMEM)),
        scratch_shapes=[
            pltpu.VMEM(matrices.shape, jnp.float32),
            pltpu.VMEM((solved, size, size), jnp.float32),
        ],
    )(matrices)


def local(start_modes, stiff_diag, stiff_off, mass_blocks, coupling, interface_block, global_iface):
    start_flat = start_modes[0]
    stiff_self = stiff_diag[0]
    stiff_link = stiff_off[0]
    mass_self = mass_blocks[0]
    coupling_blocks = coupling[0]
    interface_ids = interface_block[0]
    global_ids = global_iface[0]
    row_count, mode_count = start_flat.shape
    blocks_dev = stiff_self.shape[0]
    block_size = stiff_self.shape[1]
    dof_count = row_count * lax.axis_size("blk")
    link_next = passed_along(stiff_link[:1], "blk", -1)

    blk_count = lax.axis_size("blk")
    forward = [(i, i + 1) for i in range(blk_count - 1)]
    backward = [(target, source) for source, target in forward]

    def stiff_apply(vectors, keep, scale):
        low = lax.ppermute(vectors[row_count - block_size :], "blk", forward)
        high = lax.ppermute(vectors[:block_size], "blk", backward)
        result = stiff_filter(
            vectors.reshape(blocks_dev, block_size, mode_count),
            low[None],
            high[None],
            stiff_self,
            stiff_link,
            link_next,
            keep,
            scale,
        )
        return result.reshape(row_count, mode_count)

    def mass_apply(vectors):
        return block_product(
            mass_self, vectors.reshape(blocks_dev, block_size, mode_count)
        ).reshape(row_count, mode_count)

    def gram_matrix(left, right):
        return jnp.dot(left.T, right, precision=fast)

    first = stiff_apply(start_flat, 1.0, -step_size)
    second = stiff_apply(first, 1.0, -step_size)
    iface_count = global_ids.shape[0]
    block_terms = jnp.einsum(
        "bkm,bkl->bml",
        second.reshape(blocks_dev, block_size, mode_count),
        coupling_blocks,
        precision=fast,
    )
    onehot = (interface_ids[:, None] == jnp.arange(iface_count, dtype=jnp.int32)[None, :]).astype(
        jnp.float32
    )
    coupling_term = jnp.einsum("bj,bml->mjl", onehot, block_terms, precision=highest)
    second, coupling_term = lax.optimization_barrier((second, coupling_term))
    rounds = lax.axis_size("blk").bit_length() - 1
    levels = list(range(rounds))
    swapped = levels[1:2] + levels[:1] + levels[2:]
    stiff_second = stiff_apply(second, 0.0, 1.0)
    grams_flat = jnp.stack(
        [
            gram_matrix(first, mass_apply(first)),
            gram_matrix(second, mass_apply(second)),
            gram_matrix(second, stiff_second),
        ]
    ).reshape(-1)
    payload = jnp.concatenate([grams_flat, coupling_term.reshape(-1)])
    middle = payload.shape[0] // 2
    assert middle >= grams_flat.shape[0]
    summed = jnp.concatenate(
        [
            permute_sum(payload[:middle], "blk", levels),
            permute_sum(payload[middle:], "blk", swapped),
        ]
    )
    first_gram, mass_gram, stiff_gram = summed[: grams_flat.shape[0]].reshape(3, mode_count, mode_count)
    coupling_sum = summed[grams_flat.shape[0] :].reshape(coupling_term.shape)
    grams = jnp.stack([first_gram, mass_gram, stiff_gram]) / dof_count
    inverses, roots = inverse_factors(0.5 * (grams + jnp.swapaxes(grams, 1, 2)), 2)
    guard = 0.0 * jnp.sum(roots[0])
    factor_inv = inverses[0] + guard
    chain_inv = inverses[1] + guard
    basis = jnp.dot(second, factor_inv.T, precision=fast)
    reduced = (
        jnp.dot(
            jnp.dot(factor_inv, stiff_gram, precision=highest), factor_inv.T, precision=highest
        )
        / dof_count
    )
    scaled = jnp.einsum("nm,mjl->njl", chain_inv, coupling_sum, precision=highest) / dof_count**0.5
    condensed = jnp.einsum("njk,njl->jkl", scaled, scaled, precision=highest)
    global_count = GIFC * lax.axis_size("comp")
    placed = (global_ids[:, None] == jnp.arange(global_count, dtype=jnp.int32)[None, :]).astype(
        jnp.float32
    )
    dense_sum = jnp.einsum("jg,jkl->gkl", placed, condensed, precision=highest)
    comp_count = lax.axis_size("comp")
    comp_me = lax.axis_index("comp")
    owned = lax.dynamic_slice_in_dim(dense_sum, comp_me * GIFC, GIFC)
    for shift in range(1, comp_count):
        target = lax.rem(comp_me + shift, comp_count)
        outgoing = lax.dynamic_slice_in_dim(dense_sum, target * GIFC, GIFC)
        pairs = [(i, (i + shift) % comp_count) for i in range(comp_count)]
        owned = owned + lax.ppermute(outgoing, "comp", pairs)
    return (basis[None], reduced[None], owned)


def solution(mesh):
    in_specs = (
        P("comp", "blk", None),
        P("comp", "blk", None, None),
        P("comp", "blk", None, None),
        P("comp", "blk", None, None),
        P("comp", "blk", None, None),
        P("comp", "blk"),
        P("comp", None),
    )
    out_specs = (P("comp", "blk", None), P("comp", None, None), P("comp", None, None))
    return jax.shard_map(local, mesh=mesh, in_specs=in_specs, out_specs=out_specs, check_vma=False)
```

```python
import functools
import jax
import jax.numpy as jnp
from jax import lax
from jax.experimental import pallas as pl
from jax.experimental.pallas import tpu as pltpu
from jax.sharding import PartitionSpec as P

ITERS = 2
GIFC = 4


highest = lax.Precision.HIGHEST
fast = lax.Precision.HIGH
step_size = 0.15


def passed_along(value, axis, steps):
    count = lax.axis_size(axis)
    initial, last = (max(0, -steps), min(count, count - steps))
    return lax.ppermute(value, axis, [(source, source + steps) for source in range(initial, last)])


def extended_2(block, sides, width):
    for axis, dim in sides:
        count = lax.axis_size(axis)
        forward = [(i, i + 1) for i in range(count - 1)]
        backward = [(target, source) for source, target in forward]
        low = lax.ppermute(
            lax.slice_in_dim(block, block.shape[dim] - width, None, axis=dim), axis, forward
        )
        high = lax.ppermute(lax.slice_in_dim(block, 0, width, axis=dim), axis, backward)
        block = jnp.concatenate([low, block, high], axis=dim)
    return block


def permute_sum(value, axis, order):
    count = lax.axis_size(axis)
    rounds = count.bit_length() - 1
    assert count == 1 << rounds and sorted(order) == list(range(rounds))
    me = lax.axis_index(axis)
    shape = value.shape
    flat = value.reshape(-1)
    piece = flat.shape[0] >> rounds
    assert piece << rounds == flat.shape[0]
    for level in order:
        half = flat.shape[0] // 2
        upper = (me >> level) & 1
        pairs = [(i, i ^ (1 << level)) for i in range(count)]
        sent = lax.dynamic_slice_in_dim(flat, (1 - upper) * half, half)
        kept = lax.dynamic_slice_in_dim(flat, upper * half, half)
        flat = kept + lax.ppermute(sent, axis, pairs)
    for level in reversed(order):
        upper = (me >> level) & 1
        pairs = [(i, i ^ (1 << level)) for i in range(count)]
        other = lax.ppermute(flat, axis, pairs)
        flat = jnp.where(
            upper == 1, jnp.concatenate([other, flat]), jnp.concatenate([flat, other])
        )
    return flat.reshape(shape)


def block_product(blocks, vectors):
    return jnp.einsum("bij,bjm->bim", blocks, vectors, precision=fast)


def _split(value):
    high = value.astype(jnp.bfloat16)
    return high, (value - high.astype(jnp.float32)).astype(jnp.bfloat16)


def _split_dot(left, right):
    left_hi, left_lo = left
    right_hi, right_lo = right
    total = jnp.dot(left_hi, right_hi, preferred_element_type=jnp.float32)
    total = total + jnp.dot(left_lo, right_hi, preferred_element_type=jnp.float32)
    return total + jnp.dot(left_hi, right_lo, preferred_element_type=jnp.float32)


def _stiff_kernel(keep, scale, group, x_ref, prev_ref, next_ref, low_ref, high_ref,
                  diag_ref, link_ref, link_on_ref, tail_ref, out_ref):
    step = pl.program_id(0)
    last = pl.num_programs(0) - 1
    before = jnp.where(step == 0, low_ref[0], prev_ref[0])
    beyond = jnp.where(step == last, high_ref[0], next_ref[0])
    link_beyond = jnp.where(step == last, tail_ref[0], link_on_ref[0])
    parts = [_split(before)] + [_split(x_ref[j]) for j in range(group)] + [_split(beyond)]
    for j in range(group):
        after = link_ref[j + 1] if j + 1 < group else link_beyond
        diag_hi, diag_lo = _split(diag_ref[j])
        link_hi, link_lo = _split(link_ref[j])
        stacked_left = (
            jnp.concatenate([diag_hi, link_hi], axis=1),
            jnp.concatenate([diag_lo, link_lo], axis=1),
        )
        stacked_right = (
            jnp.concatenate([parts[j + 1][0], parts[j][0]], axis=0),
            jnp.concatenate([parts[j + 1][1], parts[j][1]], axis=0),
        )
        acc = _split_dot(stacked_left, stacked_right)
        acc = acc + _split_dot(_split(after.T), parts[j + 2])
        out_ref[j] = scale * acc if keep == 0.0 else keep * x_ref[j] + scale * acc


def stiff_filter(vectors, low, high, diag, link, tail, keep, scale, group=8):
    blocks, size, modes = vectors.shape
    steps = blocks // group
    assert steps * group == blocks
    block_spec = pl.BlockSpec((group, size, modes), lambda g: (g, 0, 0))
    single = (1, size, modes)
    mat_spec = pl.BlockSpec((group, size, size), lambda g: (g, 0, 0))
    return pl.pallas_call(
        functools.partial(_stiff_kernel, keep, scale, group),
        grid=(steps,),
        out_shape=jax.ShapeDtypeStruct(vectors.shape, jnp.float32),
        in_specs=[
            block_spec,
            pl.BlockSpec(single, lambda g: (jnp.maximum(g * group - 1, 0), 0, 0)),
            pl.BlockSpec(single, lambda g: (jnp.minimum(g * group + group, blocks - 1), 0, 0)),
            pl.BlockSpec(single, lambda g: (0, 0, 0)),
            pl.BlockSpec(single, lambda g: (0, 0, 0)),
            mat_spec,
            mat_spec,
            pl.BlockSpec((1, size, size), lambda g: (jnp.minimum(g * group + group, blocks - 1), 0, 0)),
            pl.BlockSpec((1, size, size), lambda g: (0, 0, 0)),
        ],
        out_specs=block_spec,
    )(vectors, vectors, vectors, low, high, diag, link, link, tail)


def _inverse_factor_kernel(a_in, w_out, root_out, a_ref, x_ref):
    batch, size, _ = a_in.shape
    solved = x_ref.shape[0]
    a_ref[...] = a_in[...]
    rows = lax.broadcasted_iota(jnp.int32, (size, size), 0)
    cols = lax.broadcasted_iota(jnp.int32, (size, size), 1)
    eye = jnp.where(rows == cols, 1.0, 0.0).astype(jnp.float32)
    x_ref[...] = jnp.broadcast_to(eye, x_ref.shape)
    phase = 32
    lanes = 128
    sublanes = 8

    def pick_rows(tile, tile0, k):
        sub = lax.broadcasted_iota(jnp.int32, tile.shape, 1) + tile0
        first = jnp.sum(jnp.where(sub == k, tile, 0.0), axis=1, keepdims=True)
        second = jnp.sum(jnp.where(sub == k + 1, tile, 0.0), axis=1, keepdims=True)
        return first, second

    def lane_value(row, col0, k):
        lane = lax.broadcasted_iota(jnp.int32, row.shape, 2) + col0
        return jnp.sum(jnp.where(lane == k, row, 0.0), axis=2, keepdims=True)

    for start in range(0, size, phase):
        a_col0 = (start // lanes) * lanes
        x_col1 = min(size, -(-(start + phase) // lanes) * lanes)

        def step(pair, carry, start=start, a_col0=a_col0, x_col1=x_col1):
            k = start + 2 * pair
            tile0 = pl.multiple_of((k // sublanes) * sublanes, sublanes)
            row_a0, row_a1 = pick_rows(a_ref[:, pl.ds(tile0, sublanes), a_col0:], tile0, k)
            row_x0, row_x1 = pick_rows(x_ref[:, pl.ds(tile0, sublanes), :x_col1], tile0, k)
            block0 = pl.multiple_of((k // lanes) * lanes, lanes)
            col_block = a_ref[:, start:, pl.ds(block0, lanes)]
            lane = lax.broadcasted_iota(jnp.int32, col_block.shape, 2) + block0
            col0 = jnp.sum(jnp.where(lane == k, col_block, 0.0), axis=2, keepdims=True)
            col1 = jnp.sum(jnp.where(lane == k + 1, col_block, 0.0), axis=2, keepdims=True)
            pivot0 = lane_value(row_a0, a_col0, k)
            upper01 = lane_value(row_a0, a_col0, k + 1)
            lower10 = lane_value(row_a1, a_col0, k)
            diag11 = lane_value(row_a1, a_col0, k + 1)
            ratio = lower10 / pivot0
            pivot1 = diag11 - ratio * upper01
            row_ids = lax.broadcasted_iota(jnp.int32, col0.shape, 1) + start
            mult0 = jnp.where(row_ids > k, col0 / pivot0, 0.0)
            mult1 = jnp.where(row_ids > k + 1, (col1 - mult0 * upper01) / pivot1, 0.0)
            row_a1 = row_a1 - ratio * row_a0
            row_x1 = row_x1 - ratio[batch - solved :] * row_x0
            a_ref[:, start:, a_col0:] = a_ref[:, start:, a_col0:] - mult0 * row_a0 - mult1 * row_a1
            x_ref[:, start:, :x_col1] = (
                x_ref[:, start:, :x_col1]
                - mult0[batch - solved :] * row_x0
                - mult1[batch - solved :] * row_x1
            )
            return carry

        lax.fori_loop(0, phase // 2, step, 0)
    pivots = jnp.sum(jnp.where(rows == cols, a_ref[...], 0.0), axis=2, keepdims=True)
    roots = lax.rsqrt(pivots)
    w_out[...] = x_ref[...] * roots[batch - solved :]
    root_out[...] = jnp.broadcast_to(roots, root_out.shape)


def inverse_factors(matrices, solved):
    batch, size, _ = matrices.shape
    return pl.pallas_call(
        _inverse_factor_kernel,
        out_shape=(
            jax.ShapeDtypeStruct((solved, size, size), jnp.float32),
            jax.ShapeDtypeStruct((batch, size, 128), jnp.float32),
        ),
        in_specs=[pl.BlockSpec(memory_space=pltpu.VMEM)],
        out_specs=(pl.BlockSpec(memory_space=pltpu.VMEM), pl.BlockSpec(memory_space=pltpu.VMEM)),
        scratch_shapes=[
            pltpu.VMEM(matrices.shape, jnp.float32),
            pltpu.VMEM((solved, size, size), jnp.float32),
        ],
    )(matrices)


def local(start_modes, stiff_diag, stiff_off, mass_blocks, coupling, interface_block, global_iface):
    start_flat = start_modes[0]
    stiff_self = stiff_diag[0]
    stiff_link = stiff_off[0]
    mass_self = mass_blocks[0]
    coupling_blocks = coupling[0]
    interface_ids = interface_block[0]
    global_ids = global_iface[0]
    row_count, mode_count = start_flat.shape
    blocks_dev = stiff_self.shape[0]
    block_size = stiff_self.shape[1]
    dof_count = row_count * lax.axis_size("blk")
    link_next = passed_along(stiff_link[:1], "blk", -1)

    blk_count = lax.axis_size("blk")
    forward = [(i, i + 1) for i in range(blk_count - 1)]
    backward = [(target, source) for source, target in forward]

    def stiff_apply(vectors, keep, scale):
        low = lax.ppermute(vectors[row_count - block_size :], "blk", forward)
        high = lax.ppermute(vectors[:block_size], "blk", backward)
        result = stiff_filter(
            vectors.reshape(blocks_dev, block_size, mode_count),
            low[None],
            high[None],
            stiff_self,
            stiff_link,
            link_next,
            keep,
            scale,
        )
        return result.reshape(row_count, mode_count)

    def mass_apply(vectors):
        return block_product(
            mass_self, vectors.reshape(blocks_dev, block_size, mode_count)
        ).reshape(row_count, mode_count)

    def gram_matrix(left, right):
        return jnp.dot(left.T, right, precision=fast)

    first = stiff_apply(start_flat, 1.0, -step_size)
    second = stiff_apply(first, 1.0, -step_size)
    iface_count = global_ids.shape[0]
    block_terms = jnp.einsum(
        "bkm,bkl->bml",
        second.reshape(blocks_dev, block_size, mode_count),
        coupling_blocks,
        precision=fast,
    )
    onehot = (interface_ids[:, None] == jnp.arange(iface_count, dtype=jnp.int32)[None, :]).astype(
        jnp.float32
    )
    coupling_term = jnp.einsum("bj,bml->mjl", onehot, block_terms, precision=highest)
    second, coupling_term = lax.optimization_barrier((second, coupling_term))
    rounds = lax.axis_size("blk").bit_length() - 1
    levels = list(range(rounds))
    swapped = levels[1:2] + levels[:1] + levels[2:]
    coupling_sum = permute_sum(coupling_term, "blk", swapped)
    stiff_second = stiff_apply(second, 0.0, 1.0)
    first_gram, mass_gram, stiff_gram = permute_sum(
        jnp.stack(
            [
                gram_matrix(first, mass_apply(first)),
                gram_matrix(second, mass_apply(second)),
                gram_matrix(second, stiff_second),
            ]
        ),
        "blk",
        levels,
    )
    grams = jnp.stack([first_gram, mass_gram, stiff_gram]) / dof_count
    inverses, roots = inverse_factors(0.5 * (grams + jnp.swapaxes(grams, 1, 2)), 2)
    guard = 0.0 * jnp.sum(roots[0])
    factor_inv = inverses[0] + guard
    chain_inv = inverses[1] + guard
    basis = jnp.dot(second, factor_inv.T, precision=fast)
    reduced = (
        jnp.dot(
            jnp.dot(factor_inv, stiff_gram, precision=highest), factor_inv.T, precision=highest
        )
        / dof_count
    )
    scaled = jnp.einsum("nm,mjl->njl", chain_inv, coupling_sum, precision=highest) / dof_count**0.5
    condensed = jnp.einsum("njk,njl->jkl", scaled, scaled, precision=highest)
    global_count = GIFC * lax.axis_size("comp")
    placed = (global_ids[:, None] == jnp.arange(global_count, dtype=jnp.int32)[None, :]).astype(
        jnp.float32
    )
    dense_sum = jnp.einsum("jg,jkl->gkl", placed, condensed, precision=highest)
    comp_count = lax.axis_size("comp")
    comp_me = lax.axis_index("comp")
    owned = lax.dynamic_slice_in_dim(dense_sum, comp_me * GIFC, GIFC)
    for shift in range(1, comp_count):
        target = lax.rem(comp_me + shift, comp_count)
        outgoing = lax.dynamic_slice_in_dim(dense_sum, target * GIFC, GIFC)
        pairs = [(i, (i + shift) % comp_count) for i in range(comp_count)]
        owned = owned + lax.ppermute(outgoing, "comp", pairs)
    return (basis[None], reduced[None], owned)


def solution(mesh):
    in_specs = (
        P("comp", "blk", None),
        P("comp", "blk", None, None),
        P("comp", "blk", None, None),
        P("comp", "blk", None, None),
        P("comp", "blk", None, None),
        P("comp", "blk"),
        P("comp", None),
    )
    out_specs = (P("comp", "blk", None), P("comp", None, None), P("comp", None, None))
    return jax.shard_map(local, mesh=mesh, in_specs=in_specs, out_specs=out_specs, check_vma=False)
```

```python
import functools
import jax
import jax.numpy as jnp
from jax import lax
from jax.experimental import pallas as pl
from jax.experimental.pallas import tpu as pltpu
from jax.sharding import PartitionSpec as P

ITERS = 2
GIFC = 4


highest = lax.Precision.HIGHEST
fast = lax.Precision.HIGH
step_size = 0.15


def passed_along(value, axis, steps):
    count = lax.axis_size(axis)
    initial, last = (max(0, -steps), min(count, count - steps))
    return lax.ppermute(value, axis, [(source, source + steps) for source in range(initial, last)])


def extended_2(block, sides, width):
    for axis, dim in sides:
        count = lax.axis_size(axis)
        forward = [(i, i + 1) for i in range(count - 1)]
        backward = [(target, source) for source, target in forward]
        low = lax.ppermute(
            lax.slice_in_dim(block, block.shape[dim] - width, None, axis=dim), axis, forward
        )
        high = lax.ppermute(lax.slice_in_dim(block, 0, width, axis=dim), axis, backward)
        block = jnp.concatenate([low, block, high], axis=dim)
    return block


def permute_sum(value, axis, order):
    count = lax.axis_size(axis)
    rounds = count.bit_length() - 1
    assert count == 1 << rounds and sorted(order) == list(range(rounds))
    me = lax.axis_index(axis)
    shape = value.shape
    flat = value.reshape(-1)
    piece = flat.shape[0] >> rounds
    assert piece << rounds == flat.shape[0]
    for level in order:
        half = flat.shape[0] // 2
        upper = (me >> level) & 1
        pairs = [(i, i ^ (1 << level)) for i in range(count)]
        sent = lax.dynamic_slice_in_dim(flat, (1 - upper) * half, half)
        kept = lax.dynamic_slice_in_dim(flat, upper * half, half)
        flat = kept + lax.ppermute(sent, axis, pairs)
    for level in reversed(order):
        upper = (me >> level) & 1
        pairs = [(i, i ^ (1 << level)) for i in range(count)]
        other = lax.ppermute(flat, axis, pairs)
        flat = jnp.where(
            upper == 1, jnp.concatenate([other, flat]), jnp.concatenate([flat, other])
        )
    return flat.reshape(shape)


def block_product(blocks, vectors):
    return jnp.einsum("bij,bjm->bim", blocks, vectors, precision=fast)


def _split(value):
    high = value.astype(jnp.bfloat16)
    return high, (value - high.astype(jnp.float32)).astype(jnp.bfloat16)


def _split_dot(left, right):
    left_hi, left_lo = left
    right_hi, right_lo = right
    total = jnp.dot(left_hi, right_hi, preferred_element_type=jnp.float32)
    total = total + jnp.dot(left_lo, right_hi, preferred_element_type=jnp.float32)
    return total + jnp.dot(left_hi, right_lo, preferred_element_type=jnp.float32)


def _stiff_kernel(keep, scale, group, x_ref, prev_ref, next_ref, low_ref, high_ref,
                  diag_ref, link_ref, link_on_ref, tail_ref, out_ref):
    step = pl.program_id(0)
    last = pl.num_programs(0) - 1
    before = jnp.where(step == 0, low_ref[0], prev_ref[0])
    beyond = jnp.where(step == last, high_ref[0], next_ref[0])
    link_beyond = jnp.where(step == last, tail_ref[0], link_on_ref[0])
    parts = [_split(before)] + [_split(x_ref[j]) for j in range(group)] + [_split(beyond)]
    for j in range(group):
        after = link_ref[j + 1] if j + 1 < group else link_beyond
        diag_hi, diag_lo = _split(diag_ref[j])
        link_hi, link_lo = _split(link_ref[j])
        stacked_left = (
            jnp.concatenate([diag_hi, link_hi], axis=1),
            jnp.concatenate([diag_lo, link_lo], axis=1),
        )
        stacked_right = (
            jnp.concatenate([parts[j + 1][0], parts[j][0]], axis=0),
            jnp.concatenate([parts[j + 1][1], parts[j][1]], axis=0),
        )
        acc = _split_dot(stacked_left, stacked_right)
        acc = acc + _split_dot(_split(after.T), parts[j + 2])
        out_ref[j] = scale * acc if keep == 0.0 else keep * x_ref[j] + scale * acc


def stiff_filter(vectors, low, high, diag, link, tail, keep, scale, group=8):
    blocks, size, modes = vectors.shape
    steps = blocks // group
    assert steps * group == blocks
    block_spec = pl.BlockSpec((group, size, modes), lambda g: (g, 0, 0))
    single = (1, size, modes)
    mat_spec = pl.BlockSpec((group, size, size), lambda g: (g, 0, 0))
    return pl.pallas_call(
        functools.partial(_stiff_kernel, keep, scale, group),
        grid=(steps,),
        out_shape=jax.ShapeDtypeStruct(vectors.shape, jnp.float32),
        in_specs=[
            block_spec,
            pl.BlockSpec(single, lambda g: (jnp.maximum(g * group - 1, 0), 0, 0)),
            pl.BlockSpec(single, lambda g: (jnp.minimum(g * group + group, blocks - 1), 0, 0)),
            pl.BlockSpec(single, lambda g: (0, 0, 0)),
            pl.BlockSpec(single, lambda g: (0, 0, 0)),
            mat_spec,
            mat_spec,
            pl.BlockSpec((1, size, size), lambda g: (jnp.minimum(g * group + group, blocks - 1), 0, 0)),
            pl.BlockSpec((1, size, size), lambda g: (0, 0, 0)),
        ],
        out_specs=block_spec,
    )(vectors, vectors, vectors, low, high, diag, link, link, tail)


def _inverse_factor_kernel(a_in, w_out, root_out, a_ref, x_ref):
    batch, size, _ = a_in.shape
    solved = x_ref.shape[0]
    a_ref[...] = a_in[...]
    rows = lax.broadcasted_iota(jnp.int32, (size, size), 0)
    cols = lax.broadcasted_iota(jnp.int32, (size, size), 1)
    eye = jnp.where(rows == cols, 1.0, 0.0).astype(jnp.float32)
    x_ref[...] = jnp.broadcast_to(eye, x_ref.shape)
    phase = 16
    lanes = 128
    sublanes = 8

    def pick_rows(tile, tile0, k):
        sub = lax.broadcasted_iota(jnp.int32, tile.shape, 1) + tile0
        first = jnp.sum(jnp.where(sub == k, tile, 0.0), axis=1, keepdims=True)
        second = jnp.sum(jnp.where(sub == k + 1, tile, 0.0), axis=1, keepdims=True)
        return first, second

    def lane_value(row, col0, k):
        lane = lax.broadcasted_iota(jnp.int32, row.shape, 2) + col0
        return jnp.sum(jnp.where(lane == k, row, 0.0), axis=2, keepdims=True)

    for start in range(0, size, phase):
        a_col0 = (start // lanes) * lanes
        x_col1 = min(size, -(-(start + phase) // lanes) * lanes)

        def step(pair, carry, start=start, a_col0=a_col0, x_col1=x_col1):
            k = start + 2 * pair
            tile0 = pl.multiple_of((k // sublanes) * sublanes, sublanes)
            row_a0, row_a1 = pick_rows(a_ref[:, pl.ds(tile0, sublanes), a_col0:], tile0, k)
            row_x0, row_x1 = pick_rows(x_ref[:, pl.ds(tile0, sublanes), :x_col1], tile0, k)
            block0 = pl.multiple_of((k // lanes) * lanes, lanes)
            col_block = a_ref[:, start:, pl.ds(block0, lanes)]
            lane = lax.broadcasted_iota(jnp.int32, col_block.shape, 2) + block0
            col0 = jnp.sum(jnp.where(lane == k, col_block, 0.0), axis=2, keepdims=True)
            col1 = jnp.sum(jnp.where(lane == k + 1, col_block, 0.0), axis=2, keepdims=True)
            pivot0 = lane_value(row_a0, a_col0, k)
            upper01 = lane_value(row_a0, a_col0, k + 1)
            lower10 = lane_value(row_a1, a_col0, k)
            diag11 = lane_value(row_a1, a_col0, k + 1)
            ratio = lower10 / pivot0
            pivot1 = diag11 - ratio * upper01
            row_ids = lax.broadcasted_iota(jnp.int32, col0.shape, 1) + start
            mult0 = jnp.where(row_ids > k, col0 / pivot0, 0.0)
            mult1 = jnp.where(row_ids > k + 1, (col1 - mult0 * upper01) / pivot1, 0.0)
            row_a1 = row_a1 - ratio * row_a0
            row_x1 = row_x1 - ratio[batch - solved :] * row_x0
            a_ref[:, start:, a_col0:] = a_ref[:, start:, a_col0:] - mult0 * row_a0 - mult1 * row_a1
            x_ref[:, start:, :x_col1] = (
                x_ref[:, start:, :x_col1]
                - mult0[batch - solved :] * row_x0
                - mult1[batch - solved :] * row_x1
            )
            return carry

        lax.fori_loop(0, phase // 2, step, 0)
    pivots = jnp.sum(jnp.where(rows == cols, a_ref[...], 0.0), axis=2, keepdims=True)
    roots = lax.rsqrt(pivots)
    w_out[...] = x_ref[...] * roots[batch - solved :]
    root_out[...] = jnp.broadcast_to(roots, root_out.shape)


def inverse_factors(matrices, solved):
    batch, size, _ = matrices.shape
    return pl.pallas_call(
        _inverse_factor_kernel,
        out_shape=(
            jax.ShapeDtypeStruct((solved, size, size), jnp.float32),
            jax.ShapeDtypeStruct((batch, size, 128), jnp.float32),
        ),
        in_specs=[pl.BlockSpec(memory_space=pltpu.VMEM)],
        out_specs=(pl.BlockSpec(memory_space=pltpu.VMEM), pl.BlockSpec(memory_space=pltpu.VMEM)),
        scratch_shapes=[
            pltpu.VMEM(matrices.shape, jnp.float32),
            pltpu.VMEM((solved, size, size), jnp.float32),
        ],
    )(matrices)


def local(start_modes, stiff_diag, stiff_off, mass_blocks, coupling, interface_block, global_iface):
    start_flat = start_modes[0]
    stiff_self = stiff_diag[0]
    stiff_link = stiff_off[0]
    mass_self = mass_blocks[0]
    coupling_blocks = coupling[0]
    interface_ids = interface_block[0]
    global_ids = global_iface[0]
    row_count, mode_count = start_flat.shape
    blocks_dev = stiff_self.shape[0]
    block_size = stiff_self.shape[1]
    dof_count = row_count * lax.axis_size("blk")
    link_next = passed_along(stiff_link[:1], "blk", -1)

    blk_count = lax.axis_size("blk")
    forward = [(i, i + 1) for i in range(blk_count - 1)]
    backward = [(target, source) for source, target in forward]

    def stiff_apply(vectors, keep, scale):
        low = lax.ppermute(vectors[row_count - block_size :], "blk", forward)
        high = lax.ppermute(vectors[:block_size], "blk", backward)
        result = stiff_filter(
            vectors.reshape(blocks_dev, block_size, mode_count),
            low[None],
            high[None],
            stiff_self,
            stiff_link,
            link_next,
            keep,
            scale,
        )
        return result.reshape(row_count, mode_count)

    def mass_apply(vectors):
        return block_product(
            mass_self, vectors.reshape(blocks_dev, block_size, mode_count)
        ).reshape(row_count, mode_count)

    def gram_matrix(left, right):
        return jnp.dot(left.T, right, precision=fast)

    first = stiff_apply(start_flat, 1.0, -step_size)
    second = stiff_apply(first, 1.0, -step_size)
    iface_count = global_ids.shape[0]
    block_terms = jnp.einsum(
        "bkm,bkl->bml",
        second.reshape(blocks_dev, block_size, mode_count),
        coupling_blocks,
        precision=fast,
    )
    onehot = (interface_ids[:, None] == jnp.arange(iface_count, dtype=jnp.int32)[None, :]).astype(
        jnp.float32
    )
    coupling_term = jnp.einsum("bj,bml->mjl", onehot, block_terms, precision=highest)
    second, coupling_term = lax.optimization_barrier((second, coupling_term))
    rounds = lax.axis_size("blk").bit_length() - 1
    levels = list(range(rounds))
    swapped = levels[1:2] + levels[:1] + levels[2:]
    coupling_sum = permute_sum(coupling_term, "blk", swapped)
    stiff_second = stiff_apply(second, 0.0, 1.0)
    first_gram, mass_gram, stiff_gram = permute_sum(
        jnp.stack(
            [
                gram_matrix(first, mass_apply(first)),
                gram_matrix(second, mass_apply(second)),
                gram_matrix(second, stiff_second),
            ]
        ),
        "blk",
        levels,
    )
    grams = jnp.stack([first_gram, mass_gram, stiff_gram]) / dof_count
    inverses, roots = inverse_factors(0.5 * (grams + jnp.swapaxes(grams, 1, 2)), 2)
    guard = 0.0 * jnp.sum(roots[0])
    factor_inv = inverses[0] + guard
    chain_inv = inverses[1] + guard
    basis = jnp.dot(second, factor_inv.T, precision=fast)
    reduced = (
        jnp.dot(
            jnp.dot(factor_inv, stiff_gram, precision=highest), factor_inv.T, precision=highest
        )
        / dof_count
    )
    scaled = jnp.einsum("nm,mjl->njl", chain_inv, coupling_sum, precision=highest) / dof_count**0.5
    condensed = jnp.einsum("njk,njl->jkl", scaled, scaled, precision=highest)
    global_count = GIFC * lax.axis_size("comp")
    placed = (global_ids[:, None] == jnp.arange(global_count, dtype=jnp.int32)[None, :]).astype(
        jnp.float32
    )
    dense_sum = jnp.einsum("jg,jkl->gkl", placed, condensed, precision=highest)
    comp_count = lax.axis_size("comp")
    comp_me = lax.axis_index("comp")
    owned = lax.dynamic_slice_in_dim(dense_sum, comp_me * GIFC, GIFC)
    for shift in range(1, comp_count):
        target = lax.rem(comp_me + shift, comp_count)
        outgoing = lax.dynamic_slice_in_dim(dense_sum, target * GIFC, GIFC)
        pairs = [(i, (i + shift) % comp_count) for i in range(comp_count)]
        owned = owned + lax.ppermute(outgoing, "comp", pairs)
    return (basis[None], reduced[None], owned)


def solution(mesh):
    in_specs = (
        P("comp", "blk", None),
        P("comp", "blk", None, None),
        P("comp", "blk", None, None),
        P("comp", "blk", None, None),
        P("comp", "blk", None, None),
        P("comp", "blk"),
        P("comp", None),
    )
    out_specs = (P("comp", "blk", None), P("comp", None, None), P("comp", None, None))
    return jax.shard_map(local, mesh=mesh, in_specs=in_specs, out_specs=out_specs, check_vma=False)
```

```python
import functools
import jax
import jax.numpy as jnp
from jax import lax
from jax.experimental import pallas as pl
from jax.experimental.pallas import tpu as pltpu
from jax.sharding import PartitionSpec as P

ITERS = 2
GIFC = 4


highest = lax.Precision.HIGHEST
fast = lax.Precision.HIGH
step_size = 0.15


def passed_along(value, axis, steps):
    count = lax.axis_size(axis)
    initial, last = (max(0, -steps), min(count, count - steps))
    return lax.ppermute(value, axis, [(source, source + steps) for source in range(initial, last)])


def extended_2(block, sides, width):
    for axis, dim in sides:
        count = lax.axis_size(axis)
        forward = [(i, i + 1) for i in range(count - 1)]
        backward = [(target, source) for source, target in forward]
        low = lax.ppermute(
            lax.slice_in_dim(block, block.shape[dim] - width, None, axis=dim), axis, forward
        )
        high = lax.ppermute(lax.slice_in_dim(block, 0, width, axis=dim), axis, backward)
        block = jnp.concatenate([low, block, high], axis=dim)
    return block


def permute_sum(value, axis, order):
    count = lax.axis_size(axis)
    rounds = count.bit_length() - 1
    assert count == 1 << rounds and sorted(order) == list(range(rounds))
    me = lax.axis_index(axis)
    shape = value.shape
    flat = value.reshape(-1)
    piece = flat.shape[0] >> rounds
    assert piece << rounds == flat.shape[0]
    for level in order:
        half = flat.shape[0] // 2
        upper = (me >> level) & 1
        pairs = [(i, i ^ (1 << level)) for i in range(count)]
        sent = lax.dynamic_slice_in_dim(flat, (1 - upper) * half, half)
        kept = lax.dynamic_slice_in_dim(flat, upper * half, half)
        flat = kept + lax.ppermute(sent, axis, pairs)
    for level in reversed(order):
        upper = (me >> level) & 1
        pairs = [(i, i ^ (1 << level)) for i in range(count)]
        other = lax.ppermute(flat, axis, pairs)
        flat = jnp.where(
            upper == 1, jnp.concatenate([other, flat]), jnp.concatenate([flat, other])
        )
    return flat.reshape(shape)


def block_product(blocks, vectors):
    return jnp.einsum("bij,bjm->bim", blocks, vectors, precision=fast)


def _split(value):
    high = value.astype(jnp.bfloat16)
    return high, (value - high.astype(jnp.float32)).astype(jnp.bfloat16)


def _split_dot(left, right):
    left_hi, left_lo = left
    right_hi, right_lo = right
    total = jnp.dot(left_hi, right_hi, preferred_element_type=jnp.float32)
    total = total + jnp.dot(left_lo, right_hi, preferred_element_type=jnp.float32)
    return total + jnp.dot(left_hi, right_lo, preferred_element_type=jnp.float32)


def _stiff_kernel(keep, scale, group, x_ref, prev_ref, next_ref, low_ref, high_ref,
                  diag_ref, link_ref, link_on_ref, tail_ref, out_ref):
    step = pl.program_id(0)
    last = pl.num_programs(0) - 1
    before = jnp.where(step == 0, low_ref[0], prev_ref[0])
    beyond = jnp.where(step == last, high_ref[0], next_ref[0])
    link_beyond = jnp.where(step == last, tail_ref[0], link_on_ref[0])
    parts = [_split(before)] + [_split(x_ref[j]) for j in range(group)] + [_split(beyond)]
    for j in range(group):
        after = link_ref[j + 1] if j + 1 < group else link_beyond
        diag_hi, diag_lo = _split(diag_ref[j])
        link_hi, link_lo = _split(link_ref[j])
        stacked_left = (
            jnp.concatenate([diag_hi, link_hi], axis=1),
            jnp.concatenate([diag_lo, link_lo], axis=1),
        )
        stacked_right = (
            jnp.concatenate([parts[j + 1][0], parts[j][0]], axis=0),
            jnp.concatenate([parts[j + 1][1], parts[j][1]], axis=0),
        )
        acc = _split_dot(stacked_left, stacked_right)
        acc = acc + _split_dot(_split(after.T), parts[j + 2])
        out_ref[j] = scale * acc if keep == 0.0 else keep * x_ref[j] + scale * acc


def stiff_filter(vectors, low, high, diag, link, tail, keep, scale, group=16):
    blocks, size, modes = vectors.shape
    steps = blocks // group
    assert steps * group == blocks
    block_spec = pl.BlockSpec((group, size, modes), lambda g: (g, 0, 0))
    single = (1, size, modes)
    mat_spec = pl.BlockSpec((group, size, size), lambda g: (g, 0, 0))
    return pl.pallas_call(
        functools.partial(_stiff_kernel, keep, scale, group),
        grid=(steps,),
        out_shape=jax.ShapeDtypeStruct(vectors.shape, jnp.float32),
        in_specs=[
            block_spec,
            pl.BlockSpec(single, lambda g: (jnp.maximum(g * group - 1, 0), 0, 0)),
            pl.BlockSpec(single, lambda g: (jnp.minimum(g * group + group, blocks - 1), 0, 0)),
            pl.BlockSpec(single, lambda g: (0, 0, 0)),
            pl.BlockSpec(single, lambda g: (0, 0, 0)),
            mat_spec,
            mat_spec,
            pl.BlockSpec((1, size, size), lambda g: (jnp.minimum(g * group + group, blocks - 1), 0, 0)),
            pl.BlockSpec((1, size, size), lambda g: (0, 0, 0)),
        ],
        out_specs=block_spec,
    )(vectors, vectors, vectors, low, high, diag, link, link, tail)


def _inverse_factor_kernel(a_in, w_out, root_out, a_ref, x_ref):
    batch, size, _ = a_in.shape
    solved = x_ref.shape[0]
    a_ref[...] = a_in[...]
    rows = lax.broadcasted_iota(jnp.int32, (size, size), 0)
    cols = lax.broadcasted_iota(jnp.int32, (size, size), 1)
    eye = jnp.where(rows == cols, 1.0, 0.0).astype(jnp.float32)
    x_ref[...] = jnp.broadcast_to(eye, x_ref.shape)
    phase = 16
    lanes = 128
    sublanes = 8

    def pick_rows(tile, tile0, k):
        sub = lax.broadcasted_iota(jnp.int32, tile.shape, 1) + tile0
        first = jnp.sum(jnp.where(sub == k, tile, 0.0), axis=1, keepdims=True)
        second = jnp.sum(jnp.where(sub == k + 1, tile, 0.0), axis=1, keepdims=True)
        return first, second

    def lane_value(row, col0, k):
        lane = lax.broadcasted_iota(jnp.int32, row.shape, 2) + col0
        return jnp.sum(jnp.where(lane == k, row, 0.0), axis=2, keepdims=True)

    for start in range(0, size, phase):
        a_col0 = (start // lanes) * lanes
        x_col1 = min(size, -(-(start + phase) // lanes) * lanes)

        def step(pair, carry, start=start, a_col0=a_col0, x_col1=x_col1):
            k = start + 2 * pair
            tile0 = pl.multiple_of((k // sublanes) * sublanes, sublanes)
            row_a0, row_a1 = pick_rows(a_ref[:, pl.ds(tile0, sublanes), a_col0:], tile0, k)
            row_x0, row_x1 = pick_rows(x_ref[:, pl.ds(tile0, sublanes), :x_col1], tile0, k)
            block0 = pl.multiple_of((k // lanes) * lanes, lanes)
            col_block = a_ref[:, start:, pl.ds(block0, lanes)]
            lane = lax.broadcasted_iota(jnp.int32, col_block.shape, 2) + block0
            col0 = jnp.sum(jnp.where(lane == k, col_block, 0.0), axis=2, keepdims=True)
            col1 = jnp.sum(jnp.where(lane == k + 1, col_block, 0.0), axis=2, keepdims=True)
            pivot0 = lane_value(row_a0, a_col0, k)
            upper01 = lane_value(row_a0, a_col0, k + 1)
            lower10 = lane_value(row_a1, a_col0, k)
            diag11 = lane_value(row_a1, a_col0, k + 1)
            ratio = lower10 / pivot0
            pivot1 = diag11 - ratio * upper01
            row_ids = lax.broadcasted_iota(jnp.int32, col0.shape, 1) + start
            mult0 = jnp.where(row_ids > k, col0 / pivot0, 0.0)
            mult1 = jnp.where(row_ids > k + 1, (col1 - mult0 * upper01) / pivot1, 0.0)
            row_a1 = row_a1 - ratio * row_a0
            row_x1 = row_x1 - ratio[batch - solved :] * row_x0
            a_ref[:, start:, a_col0:] = a_ref[:, start:, a_col0:] - mult0 * row_a0 - mult1 * row_a1
            x_ref[:, start:, :x_col1] = (
                x_ref[:, start:, :x_col1]
                - mult0[batch - solved :] * row_x0
                - mult1[batch - solved :] * row_x1
            )
            return carry

        lax.fori_loop(0, phase // 2, step, 0)
    pivots = jnp.sum(jnp.where(rows == cols, a_ref[...], 0.0), axis=2, keepdims=True)
    roots = lax.rsqrt(pivots)
    w_out[...] = x_ref[...] * roots[batch - solved :]
    root_out[...] = jnp.broadcast_to(roots, root_out.shape)


def inverse_factors(matrices, solved):
    batch, size, _ = matrices.shape
    return pl.pallas_call(
        _inverse_factor_kernel,
        out_shape=(
            jax.ShapeDtypeStruct((solved, size, size), jnp.float32),
            jax.ShapeDtypeStruct((batch, size, 128), jnp.float32),
        ),
        in_specs=[pl.BlockSpec(memory_space=pltpu.VMEM)],
        out_specs=(pl.BlockSpec(memory_space=pltpu.VMEM), pl.BlockSpec(memory_space=pltpu.VMEM)),
        scratch_shapes=[
            pltpu.VMEM(matrices.shape, jnp.float32),
            pltpu.VMEM((solved, size, size), jnp.float32),
        ],
    )(matrices)


def local(start_modes, stiff_diag, stiff_off, mass_blocks, coupling, interface_block, global_iface):
    start_flat = start_modes[0]
    stiff_self = stiff_diag[0]
    stiff_link = stiff_off[0]
    mass_self = mass_blocks[0]
    coupling_blocks = coupling[0]
    interface_ids = interface_block[0]
    global_ids = global_iface[0]
    row_count, mode_count = start_flat.shape
    blocks_dev = stiff_self.shape[0]
    block_size = stiff_self.shape[1]
    dof_count = row_count * lax.axis_size("blk")
    link_next = passed_along(stiff_link[:1], "blk", -1)

    blk_count = lax.axis_size("blk")
    forward = [(i, i + 1) for i in range(blk_count - 1)]
    backward = [(target, source) for source, target in forward]

    def stiff_apply(vectors, keep, scale):
        low = lax.ppermute(vectors[row_count - block_size :], "blk", forward)
        high = lax.ppermute(vectors[:block_size], "blk", backward)
        result = stiff_filter(
            vectors.reshape(blocks_dev, block_size, mode_count),
            low[None],
            high[None],
            stiff_self,
            stiff_link,
            link_next,
            keep,
            scale,
        )
        return result.reshape(row_count, mode_count)

    def mass_apply(vectors):
        return block_product(
            mass_self, vectors.reshape(blocks_dev, block_size, mode_count)
        ).reshape(row_count, mode_count)

    def gram_matrix(left, right):
        return jnp.dot(left.T, right, precision=fast)

    first = stiff_apply(start_flat, 1.0, -step_size)
    second = stiff_apply(first, 1.0, -step_size)
    iface_count = global_ids.shape[0]
    block_terms = jnp.einsum(
        "bkm,bkl->bml",
        second.reshape(blocks_dev, block_size, mode_count),
        coupling_blocks,
        precision=fast,
    )
    onehot = (interface_ids[:, None] == jnp.arange(iface_count, dtype=jnp.int32)[None, :]).astype(
        jnp.float32
    )
    coupling_term = jnp.einsum("bj,bml->mjl", onehot, block_terms, precision=highest)
    second, coupling_term = lax.optimization_barrier((second, coupling_term))
    rounds = lax.axis_size("blk").bit_length() - 1
    levels = list(range(rounds))
    swapped = levels[1:2] + levels[:1] + levels[2:]
    coupling_sum = permute_sum(coupling_term, "blk", swapped)
    stiff_second = stiff_apply(second, 0.0, 1.0)
    first_gram, mass_gram, stiff_gram = permute_sum(
        jnp.stack(
            [
                gram_matrix(first, mass_apply(first)),
                gram_matrix(second, mass_apply(second)),
                gram_matrix(second, stiff_second),
            ]
        ),
        "blk",
        levels,
    )
    grams = jnp.stack([first_gram, mass_gram, stiff_gram]) / dof_count
    inverses, roots = inverse_factors(0.5 * (grams + jnp.swapaxes(grams, 1, 2)), 2)
    guard = 0.0 * jnp.sum(roots[0])
    factor_inv = inverses[0] + guard
    chain_inv = inverses[1] + guard
    basis = jnp.dot(second, factor_inv.T, precision=fast)
    reduced = (
        jnp.dot(
            jnp.dot(factor_inv, stiff_gram, precision=highest), factor_inv.T, precision=highest
        )
        / dof_count
    )
    scaled = jnp.einsum("nm,mjl->njl", chain_inv, coupling_sum, precision=highest) / dof_count**0.5
    condensed = jnp.einsum("njk,njl->jkl", scaled, scaled, precision=highest)
    global_count = GIFC * lax.axis_size("comp")
    placed = (global_ids[:, None] == jnp.arange(global_count, dtype=jnp.int32)[None, :]).astype(
        jnp.float32
    )
    dense_sum = jnp.einsum("jg,jkl->gkl", placed, condensed, precision=highest)
    comp_count = lax.axis_size("comp")
    comp_me = lax.axis_index("comp")
    owned = lax.dynamic_slice_in_dim(dense_sum, comp_me * GIFC, GIFC)
    for shift in range(1, comp_count):
        target = lax.rem(comp_me + shift, comp_count)
        outgoing = lax.dynamic_slice_in_dim(dense_sum, target * GIFC, GIFC)
        pairs = [(i, (i + shift) % comp_count) for i in range(comp_count)]
        owned = owned + lax.ppermute(outgoing, "comp", pairs)
    return (basis[None], reduced[None], owned)


def solution(mesh):
    in_specs = (
        P("comp", "blk", None),
        P("comp", "blk", None, None),
        P("comp", "blk", None, None),
        P("comp", "blk", None, None),
        P("comp", "blk", None, None),
        P("comp", "blk"),
        P("comp", None),
    )
    out_specs = (P("comp", "blk", None), P("comp", None, None), P("comp", None, None))
    return jax.shard_map(local, mesh=mesh, in_specs=in_specs, out_specs=out_specs, check_vma=False)
```

```python
import functools
import jax
import jax.numpy as jnp
from jax import lax
from jax.experimental import pallas as pl
from jax.experimental.pallas import tpu as pltpu
from jax.sharding import PartitionSpec as P

ITERS = 2
GIFC = 4


highest = lax.Precision.HIGHEST
fast = lax.Precision.HIGH
step_size = 0.15


def passed_along(value, axis, steps):
    count = lax.axis_size(axis)
    initial, last = (max(0, -steps), min(count, count - steps))
    return lax.ppermute(value, axis, [(source, source + steps) for source in range(initial, last)])


def extended_2(block, sides, width):
    for axis, dim in sides:
        count = lax.axis_size(axis)
        forward = [(i, i + 1) for i in range(count - 1)]
        backward = [(target, source) for source, target in forward]
        low = lax.ppermute(
            lax.slice_in_dim(block, block.shape[dim] - width, None, axis=dim), axis, forward
        )
        high = lax.ppermute(lax.slice_in_dim(block, 0, width, axis=dim), axis, backward)
        block = jnp.concatenate([low, block, high], axis=dim)
    return block


def permute_sum(value, axis, order):
    count = lax.axis_size(axis)
    rounds = count.bit_length() - 1
    assert count == 1 << rounds and sorted(order) == list(range(rounds))
    me = lax.axis_index(axis)
    shape = value.shape
    flat = value.reshape(-1)
    piece = flat.shape[0] >> rounds
    assert piece << rounds == flat.shape[0]
    for level in order:
        half = flat.shape[0] // 2
        upper = (me >> level) & 1
        pairs = [(i, i ^ (1 << level)) for i in range(count)]
        sent = lax.dynamic_slice_in_dim(flat, (1 - upper) * half, half)
        kept = lax.dynamic_slice_in_dim(flat, upper * half, half)
        flat = kept + lax.ppermute(sent, axis, pairs)
    for level in reversed(order):
        upper = (me >> level) & 1
        pairs = [(i, i ^ (1 << level)) for i in range(count)]
        other = lax.ppermute(flat, axis, pairs)
        flat = jnp.where(
            upper == 1, jnp.concatenate([other, flat]), jnp.concatenate([flat, other])
        )
    return flat.reshape(shape)


def block_product(blocks, vectors):
    return jnp.einsum("bij,bjm->bim", blocks, vectors, precision=fast)


def _split(value):
    high = value.astype(jnp.bfloat16)
    return high, (value - high.astype(jnp.float32)).astype(jnp.bfloat16)


def _split_dot(left, right):
    left_hi, left_lo = left
    right_hi, right_lo = right
    total = jnp.dot(left_hi, right_hi, preferred_element_type=jnp.float32)
    total = total + jnp.dot(left_lo, right_hi, preferred_element_type=jnp.float32)
    return total + jnp.dot(left_hi, right_lo, preferred_element_type=jnp.float32)


def _stiff_kernel(keep, scale, group, x_ref, prev_ref, next_ref, low_ref, high_ref,
                  diag_ref, link_ref, link_on_ref, tail_ref, out_ref):
    step = pl.program_id(0)
    last = pl.num_programs(0) - 1
    before = jnp.where(step == 0, low_ref[0], prev_ref[0])
    beyond = jnp.where(step == last, high_ref[0], next_ref[0])
    link_beyond = jnp.where(step == last, tail_ref[0], link_on_ref[0])
    parts = [_split(before)] + [_split(x_ref[j]) for j in range(group)] + [_split(beyond)]
    for j in range(group):
        after = link_ref[j + 1] if j + 1 < group else link_beyond
        diag_hi, diag_lo = _split(diag_ref[j])
        link_hi, link_lo = _split(link_ref[j])
        stacked_left = (
            jnp.concatenate([diag_hi, link_hi], axis=1),
            jnp.concatenate([diag_lo, link_lo], axis=1),
        )
        stacked_right = (
            jnp.concatenate([parts[j + 1][0], parts[j][0]], axis=0),
            jnp.concatenate([parts[j + 1][1], parts[j][1]], axis=0),
        )
        acc = _split_dot(stacked_left, stacked_right)
        acc = acc + _split_dot(_split(after.T), parts[j + 2])
        out_ref[j] = scale * acc if keep == 0.0 else keep * x_ref[j] + scale * acc


def stiff_filter(vectors, low, high, diag, link, tail, keep, scale, group=16):
    blocks, size, modes = vectors.shape
    steps = blocks // group
    assert steps * group == blocks
    block_spec = pl.BlockSpec((group, size, modes), lambda g: (g, 0, 0))
    single = (1, size, modes)
    mat_spec = pl.BlockSpec((group, size, size), lambda g: (g, 0, 0))
    return pl.pallas_call(
        functools.partial(_stiff_kernel, keep, scale, group),
        grid=(steps,),
        out_shape=jax.ShapeDtypeStruct(vectors.shape, jnp.float32),
        in_specs=[
            block_spec,
            pl.BlockSpec(single, lambda g: (jnp.maximum(g * group - 1, 0), 0, 0)),
            pl.BlockSpec(single, lambda g: (jnp.minimum(g * group + group, blocks - 1), 0, 0)),
            pl.BlockSpec(single, lambda g: (0, 0, 0)),
            pl.BlockSpec(single, lambda g: (0, 0, 0)),
            mat_spec,
            mat_spec,
            pl.BlockSpec((1, size, size), lambda g: (jnp.minimum(g * group + group, blocks - 1), 0, 0)),
            pl.BlockSpec((1, size, size), lambda g: (0, 0, 0)),
        ],
        out_specs=block_spec,
    )(vectors, vectors, vectors, low, high, diag, link, link, tail)


def _inverse_factor_kernel(a_in, w_out, root_out, a_ref, x_ref):
    batch, size, _ = a_in.shape
    solved = x_ref.shape[0]
    a_ref[...] = a_in[...]
    rows = lax.broadcasted_iota(jnp.int32, (size, size), 0)
    cols = lax.broadcasted_iota(jnp.int32, (size, size), 1)
    eye = jnp.where(rows == cols, 1.0, 0.0).astype(jnp.float32)
    x_ref[...] = jnp.broadcast_to(eye, x_ref.shape)
    phase = 16
    lanes = 128
    sublanes = 8

    def pick_rows(tile, tile0, k):
        sub = lax.broadcasted_iota(jnp.int32, tile.shape, 1) + tile0
        first = jnp.sum(jnp.where(sub == k, tile, 0.0), axis=1, keepdims=True)
        second = jnp.sum(jnp.where(sub == k + 1, tile, 0.0), axis=1, keepdims=True)
        return first, second

    def lane_value(row, col0, k):
        lane = lax.broadcasted_iota(jnp.int32, row.shape, 2) + col0
        return jnp.sum(jnp.where(lane == k, row, 0.0), axis=2, keepdims=True)

    for start in range(0, size, phase):
        a_col0 = (start // lanes) * lanes
        x_col1 = min(size, -(-(start + phase) // lanes) * lanes)

        def step(pair, carry, start=start, a_col0=a_col0, x_col1=x_col1):
            k = start + 2 * pair
            tile0 = pl.multiple_of((k // sublanes) * sublanes, sublanes)
            row_a0, row_a1 = pick_rows(a_ref[:, pl.ds(tile0, sublanes), a_col0:], tile0, k)
            row_x0, row_x1 = pick_rows(x_ref[:, pl.ds(tile0, sublanes), :x_col1], tile0, k)
            block0 = pl.multiple_of((k // lanes) * lanes, lanes)
            col_block = a_ref[:, start:, pl.ds(block0, lanes)]
            lane = lax.broadcasted_iota(jnp.int32, col_block.shape, 2) + block0
            col0 = jnp.sum(jnp.where(lane == k, col_block, 0.0), axis=2, keepdims=True)
            col1 = jnp.sum(jnp.where(lane == k + 1, col_block, 0.0), axis=2, keepdims=True)
            pivot0 = lane_value(row_a0, a_col0, k)
            upper01 = lane_value(row_a0, a_col0, k + 1)
            lower10 = lane_value(row_a1, a_col0, k)
            diag11 = lane_value(row_a1, a_col0, k + 1)
            ratio = lower10 / pivot0
            pivot1 = diag11 - ratio * upper01
            row_ids = lax.broadcasted_iota(jnp.int32, col0.shape, 1) + start
            mult0 = jnp.where(row_ids > k, col0 / pivot0, 0.0)
            mult1 = jnp.where(row_ids > k + 1, (col1 - mult0 * upper01) / pivot1, 0.0)
            row_a1 = row_a1 - ratio * row_a0
            row_x1 = row_x1 - ratio[batch - solved :] * row_x0
            a_ref[:, start:, a_col0:] = a_ref[:, start:, a_col0:] - mult0 * row_a0 - mult1 * row_a1
            x_ref[:, start:, :x_col1] = (
                x_ref[:, start:, :x_col1]
                - mult0[batch - solved :] * row_x0
                - mult1[batch - solved :] * row_x1
            )
            return carry

        lax.fori_loop(0, phase // 2, step, 0)
    pivots = jnp.sum(jnp.where(rows == cols, a_ref[...], 0.0), axis=2, keepdims=True)
    roots = lax.rsqrt(pivots)
    w_out[...] = x_ref[...] * roots[batch - solved :]
    root_out[...] = jnp.broadcast_to(roots, root_out.shape)


def inverse_factors(matrices, solved):
    batch, size, _ = matrices.shape
    return pl.pallas_call(
        _inverse_factor_kernel,
        out_shape=(
            jax.ShapeDtypeStruct((solved, size, size), jnp.float32),
            jax.ShapeDtypeStruct((batch, size, 128), jnp.float32),
        ),
        in_specs=[pl.BlockSpec(memory_space=pltpu.VMEM)],
        out_specs=(pl.BlockSpec(memory_space=pltpu.VMEM), pl.BlockSpec(memory_space=pltpu.VMEM)),
        scratch_shapes=[
            pltpu.VMEM(matrices.shape, jnp.float32),
            pltpu.VMEM((solved, size, size), jnp.float32),
        ],
    )(matrices)


def local(start_modes, stiff_diag, stiff_off, mass_blocks, coupling, interface_block, global_iface):
    start_flat = start_modes[0]
    stiff_self = stiff_diag[0]
    stiff_link = stiff_off[0]
    mass_self = mass_blocks[0]
    coupling_blocks = coupling[0]
    interface_ids = interface_block[0]
    global_ids = global_iface[0]
    row_count, mode_count = start_flat.shape
    blocks_dev = stiff_self.shape[0]
    block_size = stiff_self.shape[1]
    dof_count = row_count * lax.axis_size("blk")
    link_next = passed_along(stiff_link[:1], "blk", -1)

    blk_count = lax.axis_size("blk")
    forward = [(i, i + 1) for i in range(blk_count - 1)]
    backward = [(target, source) for source, target in forward]

    def stiff_apply(vectors, keep, scale):
        low = lax.ppermute(vectors[row_count - block_size :], "blk", forward)
        high = lax.ppermute(vectors[:block_size], "blk", backward)
        result = stiff_filter(
            vectors.reshape(blocks_dev, block_size, mode_count),
            low[None],
            high[None],
            stiff_self,
            stiff_link,
            link_next,
            keep,
            scale,
        )
        return result.reshape(row_count, mode_count)

    def mass_apply(vectors):
        return block_product(
            mass_self, vectors.reshape(blocks_dev, block_size, mode_count)
        ).reshape(row_count, mode_count)

    def gram_matrix(left, right):
        return jnp.dot(left.T, right, precision=fast)

    first = stiff_apply(start_flat, 1.0, -step_size)
    second = stiff_apply(first, 1.0, -step_size)
    iface_count = global_ids.shape[0]
    block_terms = jnp.einsum(
        "bkm,bkl->bml",
        second.reshape(blocks_dev, block_size, mode_count),
        coupling_blocks,
        precision=fast,
    )
    onehot = (interface_ids[:, None] == jnp.arange(iface_count, dtype=jnp.int32)[None, :]).astype(
        jnp.float32
    )
    coupling_term = jnp.einsum("bj,bml->mjl", onehot, block_terms, precision=highest)
    second, coupling_term = lax.optimization_barrier((second, coupling_term))
    rounds = lax.axis_size("blk").bit_length() - 1
    levels = list(range(rounds))
    swapped = levels[1:2] + levels[:1] + levels[2:]
    coupling_sum = permute_sum(coupling_term, "blk", swapped)
    stiff_second = stiff_apply(second, 0.0, 1.0)
    first_gram, mass_gram, stiff_gram = permute_sum(
        jnp.stack(
            [
                gram_matrix(first, mass_apply(first)),
                gram_matrix(second, mass_apply(second)),
                gram_matrix(second, stiff_second),
            ]
        ),
        "blk",
        levels,
    )
    grams = jnp.stack([first_gram, mass_gram, stiff_gram]) / dof_count
    inverses, roots = inverse_factors(0.5 * (grams + jnp.swapaxes(grams, 1, 2)), 2)
    guard = 0.0 * jnp.sum(roots[0, :, :1])
    factor_inv = inverses[0] + guard
    chain_inv = inverses[1] + guard
    basis = jnp.dot(second, factor_inv.T, precision=fast)
    reduced = (
        jnp.dot(
            jnp.dot(factor_inv, stiff_gram, precision=highest), factor_inv.T, precision=highest
        )
        / dof_count
    )
    scaled = jnp.einsum("nm,mjl->njl", chain_inv, coupling_sum, precision=highest) / dof_count**0.5
    condensed = jnp.einsum("njk,njl->jkl", scaled, scaled, precision=highest)
    global_count = GIFC * lax.axis_size("comp")
    placed = (global_ids[:, None] == jnp.arange(global_count, dtype=jnp.int32)[None, :]).astype(
        jnp.float32
    )
    dense_sum = jnp.einsum("jg,jkl->gkl", placed, condensed, precision=highest)
    comp_count = lax.axis_size("comp")
    comp_me = lax.axis_index("comp")
    owned = lax.dynamic_slice_in_dim(dense_sum, comp_me * GIFC, GIFC)
    for shift in range(1, comp_count):
        target = lax.rem(comp_me + shift, comp_count)
        outgoing = lax.dynamic_slice_in_dim(dense_sum, target * GIFC, GIFC)
        pairs = [(i, (i + shift) % comp_count) for i in range(comp_count)]
        owned = owned + lax.ppermute(outgoing, "comp", pairs)
    return (basis[None], reduced[None], owned)


def solution(mesh):
    in_specs = (
        P("comp", "blk", None),
        P("comp", "blk", None, None),
        P("comp", "blk", None, None),
        P("comp", "blk", None, None),
        P("comp", "blk", None, None),
        P("comp", "blk"),
        P("comp", None),
    )
    out_specs = (P("comp", "blk", None), P("comp", None, None), P("comp", None, None))
    return jax.shard_map(local, mesh=mesh, in_specs=in_specs, out_specs=out_specs, check_vma=False)
```

```python
import functools
import jax
import jax.numpy as jnp
from jax import lax
from jax.experimental import pallas as pl
from jax.experimental.pallas import tpu as pltpu
from jax.sharding import PartitionSpec as P

ITERS = 2
GIFC = 4


highest = lax.Precision.HIGHEST
fast = lax.Precision.HIGH
step_size = 0.15


def passed_along(value, axis, steps):
    count = lax.axis_size(axis)
    initial, last = (max(0, -steps), min(count, count - steps))
    return lax.ppermute(value, axis, [(source, source + steps) for source in range(initial, last)])


def extended_2(block, sides, width):
    for axis, dim in sides:
        count = lax.axis_size(axis)
        forward = [(i, i + 1) for i in range(count - 1)]
        backward = [(target, source) for source, target in forward]
        low = lax.ppermute(
            lax.slice_in_dim(block, block.shape[dim] - width, None, axis=dim), axis, forward
        )
        high = lax.ppermute(lax.slice_in_dim(block, 0, width, axis=dim), axis, backward)
        block = jnp.concatenate([low, block, high], axis=dim)
    return block


def permute_sum(value, axis, order):
    count = lax.axis_size(axis)
    rounds = count.bit_length() - 1
    assert count == 1 << rounds and sorted(order) == list(range(rounds))
    me = lax.axis_index(axis)
    shape = value.shape
    flat = value.reshape(-1)
    piece = flat.shape[0] >> rounds
    assert piece << rounds == flat.shape[0]
    for level in order:
        half = flat.shape[0] // 2
        upper = (me >> level) & 1
        pairs = [(i, i ^ (1 << level)) for i in range(count)]
        sent = lax.dynamic_slice_in_dim(flat, (1 - upper) * half, half)
        kept = lax.dynamic_slice_in_dim(flat, upper * half, half)
        flat = kept + lax.ppermute(sent, axis, pairs)
    for level in reversed(order):
        upper = (me >> level) & 1
        pairs = [(i, i ^ (1 << level)) for i in range(count)]
        other = lax.ppermute(flat, axis, pairs)
        flat = jnp.where(
            upper == 1, jnp.concatenate([other, flat]), jnp.concatenate([flat, other])
        )
    return flat.reshape(shape)


def block_product(blocks, vectors):
    return jnp.einsum("bij,bjm->bim", blocks, vectors, precision=fast)


def _split(value):
    high = value.astype(jnp.bfloat16)
    return high, (value - high.astype(jnp.float32)).astype(jnp.bfloat16)


def _split_dot(left, right):
    left_hi, left_lo = left
    right_hi, right_lo = right
    total = jnp.dot(left_hi, right_hi, preferred_element_type=jnp.float32)
    total = total + jnp.dot(left_lo, right_hi, preferred_element_type=jnp.float32)
    return total + jnp.dot(left_hi, right_lo, preferred_element_type=jnp.float32)


def _stiff_kernel(keep, scale, group, x_ref, prev_ref, next_ref, low_ref, high_ref,
                  diag_ref, link_ref, link_on_ref, tail_ref, out_ref):
    step = pl.program_id(0)
    last = pl.num_programs(0) - 1
    before = jnp.where(step == 0, low_ref[0], prev_ref[0])
    beyond = jnp.where(step == last, high_ref[0], next_ref[0])
    link_beyond = jnp.where(step == last, tail_ref[0], link_on_ref[0])
    parts = [_split(before)] + [_split(x_ref[j]) for j in range(group)] + [_split(beyond)]
    for j in range(group):
        after = link_ref[j + 1] if j + 1 < group else link_beyond
        diag_hi, diag_lo = _split(diag_ref[j])
        link_hi, link_lo = _split(link_ref[j])
        stacked_left = (
            jnp.concatenate([diag_hi, link_hi], axis=1),
            jnp.concatenate([diag_lo, link_lo], axis=1),
        )
        stacked_right = (
            jnp.concatenate([parts[j + 1][0], parts[j][0]], axis=0),
            jnp.concatenate([parts[j + 1][1], parts[j][1]], axis=0),
        )
        acc = _split_dot(stacked_left, stacked_right)
        acc = acc + _split_dot(_split(after.T), parts[j + 2])
        out_ref[j] = scale * acc if keep == 0.0 else keep * x_ref[j] + scale * acc


def stiff_filter(vectors, low, high, diag, link, tail, keep, scale, group=16):
    blocks, size, modes = vectors.shape
    steps = blocks // group
    assert steps * group == blocks
    block_spec = pl.BlockSpec((group, size, modes), lambda g: (g, 0, 0))
    single = (1, size, modes)
    mat_spec = pl.BlockSpec((group, size, size), lambda g: (g, 0, 0))
    return pl.pallas_call(
        functools.partial(_stiff_kernel, keep, scale, group),
        grid=(steps,),
        out_shape=jax.ShapeDtypeStruct(vectors.shape, jnp.float32),
        in_specs=[
            block_spec,
            pl.BlockSpec(single, lambda g: (jnp.maximum(g * group - 1, 0), 0, 0)),
            pl.BlockSpec(single, lambda g: (jnp.minimum(g * group + group, blocks - 1), 0, 0)),
            pl.BlockSpec(single, lambda g: (0, 0, 0)),
            pl.BlockSpec(single, lambda g: (0, 0, 0)),
            mat_spec,
            mat_spec,
            pl.BlockSpec((1, size, size), lambda g: (jnp.minimum(g * group + group, blocks - 1), 0, 0)),
            pl.BlockSpec((1, size, size), lambda g: (0, 0, 0)),
        ],
        out_specs=block_spec,
    )(vectors, vectors, vectors, low, high, diag, link, link, tail)


def _inverse_factor_kernel(a_in, w_out, root_out, a_ref, x_ref):
    batch, size, _ = a_in.shape
    solved = x_ref.shape[0]
    a_ref[...] = a_in[...]
    rows = lax.broadcasted_iota(jnp.int32, (size, size), 0)
    cols = lax.broadcasted_iota(jnp.int32, (size, size), 1)
    eye = jnp.where(rows == cols, 1.0, 0.0).astype(jnp.float32)
    x_ref[...] = jnp.broadcast_to(eye, x_ref.shape)
    phase = 8
    lanes = 128
    sublanes = 8

    def pick_rows(tile, tile0, k):
        sub = lax.broadcasted_iota(jnp.int32, tile.shape, 1) + tile0
        first = jnp.sum(jnp.where(sub == k, tile, 0.0), axis=1, keepdims=True)
        second = jnp.sum(jnp.where(sub == k + 1, tile, 0.0), axis=1, keepdims=True)
        return first, second

    def lane_value(row, col0, k):
        lane = lax.broadcasted_iota(jnp.int32, row.shape, 2) + col0
        return jnp.sum(jnp.where(lane == k, row, 0.0), axis=2, keepdims=True)

    for start in range(0, size, phase):
        a_col0 = (start // lanes) * lanes
        x_col1 = min(size, -(-(start + phase) // lanes) * lanes)

        def step(pair, carry, start=start, a_col0=a_col0, x_col1=x_col1):
            k = start + 2 * pair
            tile0 = pl.multiple_of((k // sublanes) * sublanes, sublanes)
            row_a0, row_a1 = pick_rows(a_ref[:, pl.ds(tile0, sublanes), a_col0:], tile0, k)
            row_x0, row_x1 = pick_rows(x_ref[:, pl.ds(tile0, sublanes), :x_col1], tile0, k)
            block0 = pl.multiple_of((k // lanes) * lanes, lanes)
            col_block = a_ref[:, start:, pl.ds(block0, lanes)]
            lane = lax.broadcasted_iota(jnp.int32, col_block.shape, 2) + block0
            col0 = jnp.sum(jnp.where(lane == k, col_block, 0.0), axis=2, keepdims=True)
            col1 = jnp.sum(jnp.where(lane == k + 1, col_block, 0.0), axis=2, keepdims=True)
            pivot0 = lane_value(row_a0, a_col0, k)
            upper01 = lane_value(row_a0, a_col0, k + 1)
            lower10 = lane_value(row_a1, a_col0, k)
            diag11 = lane_value(row_a1, a_col0, k + 1)
            ratio = lower10 / pivot0
            pivot1 = diag11 - ratio * upper01
            row_ids = lax.broadcasted_iota(jnp.int32, col0.shape, 1) + start
            mult0 = jnp.where(row_ids > k, col0 / pivot0, 0.0)
            mult1 = jnp.where(row_ids > k + 1, (col1 - mult0 * upper01) / pivot1, 0.0)
            row_a1 = row_a1 - ratio * row_a0
            row_x1 = row_x1 - ratio[batch - solved :] * row_x0
            a_ref[:, start:, a_col0:] = a_ref[:, start:, a_col0:] - mult0 * row_a0 - mult1 * row_a1
            x_ref[:, start:, :x_col1] = (
                x_ref[:, start:, :x_col1]
                - mult0[batch - solved :] * row_x0
                - mult1[batch - solved :] * row_x1
            )
            return carry

        lax.fori_loop(0, phase // 2, step, 0)
    pivots = jnp.sum(jnp.where(rows == cols, a_ref[...], 0.0), axis=2, keepdims=True)
    roots = lax.rsqrt(pivots)
    w_out[...] = x_ref[...] * roots[batch - solved :]
    root_out[...] = jnp.broadcast_to(roots, root_out.shape)


def inverse_factors(matrices, solved):
    batch, size, _ = matrices.shape
    return pl.pallas_call(
        _inverse_factor_kernel,
        out_shape=(
            jax.ShapeDtypeStruct((solved, size, size), jnp.float32),
            jax.ShapeDtypeStruct((batch, size, 128), jnp.float32),
        ),
        in_specs=[pl.BlockSpec(memory_space=pltpu.VMEM)],
        out_specs=(pl.BlockSpec(memory_space=pltpu.VMEM), pl.BlockSpec(memory_space=pltpu.VMEM)),
        scratch_shapes=[
            pltpu.VMEM(matrices.shape, jnp.float32),
            pltpu.VMEM((solved, size, size), jnp.float32),
        ],
    )(matrices)


def local(start_modes, stiff_diag, stiff_off, mass_blocks, coupling, interface_block, global_iface):
    start_flat = start_modes[0]
    stiff_self = stiff_diag[0]
    stiff_link = stiff_off[0]
    mass_self = mass_blocks[0]
    coupling_blocks = coupling[0]
    interface_ids = interface_block[0]
    global_ids = global_iface[0]
    row_count, mode_count = start_flat.shape
    blocks_dev = stiff_self.shape[0]
    block_size = stiff_self.shape[1]
    dof_count = row_count * lax.axis_size("blk")
    link_next = passed_along(stiff_link[:1], "blk", -1)

    blk_count = lax.axis_size("blk")
    forward = [(i, i + 1) for i in range(blk_count - 1)]
    backward = [(target, source) for source, target in forward]

    def stiff_apply(vectors, keep, scale):
        low = lax.ppermute(vectors[row_count - block_size :], "blk", forward)
        high = lax.ppermute(vectors[:block_size], "blk", backward)
        result = stiff_filter(
            vectors.reshape(blocks_dev, block_size, mode_count),
            low[None],
            high[None],
            stiff_self,
            stiff_link,
            link_next,
            keep,
            scale,
        )
        return result.reshape(row_count, mode_count)

    def mass_apply(vectors):
        return block_product(
            mass_self, vectors.reshape(blocks_dev, block_size, mode_count)
        ).reshape(row_count, mode_count)

    def gram_matrix(left, right):
        return jnp.dot(left.T, right, precision=fast)

    first = stiff_apply(start_flat, 1.0, -step_size)
    second = stiff_apply(first, 1.0, -step_size)
    iface_count = global_ids.shape[0]
    block_terms = jnp.einsum(
        "bkm,bkl->bml",
        second.reshape(blocks_dev, block_size, mode_count),
        coupling_blocks,
        precision=fast,
    )
    onehot = (interface_ids[:, None] == jnp.arange(iface_count, dtype=jnp.int32)[None, :]).astype(
        jnp.float32
    )
    coupling_term = jnp.einsum("bj,bml->mjl", onehot, block_terms, precision=highest)
    second, coupling_term = lax.optimization_barrier((second, coupling_term))
    rounds = lax.axis_size("blk").bit_length() - 1
    levels = list(range(rounds))
    swapped = levels[1:2] + levels[:1] + levels[2:]
    coupling_sum = permute_sum(coupling_term, "blk", swapped)
    stiff_second = stiff_apply(second, 0.0, 1.0)
    first_gram, mass_gram, stiff_gram = permute_sum(
        jnp.stack(
            [
                gram_matrix(first, mass_apply(first)),
                gram_matrix(second, mass_apply(second)),
                gram_matrix(second, stiff_second),
            ]
        ),
        "blk",
        levels,
    )
    grams = jnp.stack([first_gram, mass_gram, stiff_gram]) / dof_count
    inverses, roots = inverse_factors(0.5 * (grams + jnp.swapaxes(grams, 1, 2)), 2)
    guard = 0.0 * jnp.sum(roots[0])
    factor_inv = inverses[0] + guard
    chain_inv = inverses[1] + guard
    basis = jnp.dot(second, factor_inv.T, precision=fast)
    reduced = (
        jnp.dot(
            jnp.dot(factor_inv, stiff_gram, precision=highest), factor_inv.T, precision=highest
        )
        / dof_count
    )
    scaled = jnp.einsum("nm,mjl->njl", chain_inv, coupling_sum, precision=highest) / dof_count**0.5
    condensed = jnp.einsum("njk,njl->jkl", scaled, scaled, precision=highest)
    global_count = GIFC * lax.axis_size("comp")
    placed = (global_ids[:, None] == jnp.arange(global_count, dtype=jnp.int32)[None, :]).astype(
        jnp.float32
    )
    dense_sum = jnp.einsum("jg,jkl->gkl", placed, condensed, precision=highest)
    comp_count = lax.axis_size("comp")
    comp_me = lax.axis_index("comp")
    owned = lax.dynamic_slice_in_dim(dense_sum, comp_me * GIFC, GIFC)
    for shift in range(1, comp_count):
        target = lax.rem(comp_me + shift, comp_count)
        outgoing = lax.dynamic_slice_in_dim(dense_sum, target * GIFC, GIFC)
        pairs = [(i, (i + shift) % comp_count) for i in range(comp_count)]
        owned = owned + lax.ppermute(outgoing, "comp", pairs)
    return (basis[None], reduced[None], owned)


def solution(mesh):
    in_specs = (
        P("comp", "blk", None),
        P("comp", "blk", None, None),
        P("comp", "blk", None, None),
        P("comp", "blk", None, None),
        P("comp", "blk", None, None),
        P("comp", "blk"),
        P("comp", None),
    )
    out_specs = (P("comp", "blk", None), P("comp", None, None), P("comp", None, None))
    return jax.shard_map(local, mesh=mesh, in_specs=in_specs, out_specs=out_specs, check_vma=False)
```
